32 devices in a mesh: mix: 2 (over x), seq: 16 (over z, y, core).
Axes of the slice: x: 2, y: 2, z: 4, core: 2. Of those that a mesh axis runs over, the one named last changes fastest.
Arguments:
- frames: bfloat16 [4096, 1024], P(('mix', 'seq')), parts along dimension 0, may hold values from -18 to 18
- segment_ids: int32 [4096], P(('mix', 'seq')), parts along dimension 0, may hold values from 0 to 2, never falling along the last dimension, each value on 1 to 1500 neighbouring positions
- out_grad: bfloat16 [4096, 1024], P(('mix', 'seq')), parts along dimension 0, may hold values from -6 to 6
- ln_gain: float32 [2048], P(('mix', 'seq')), parts along dimension 0, may hold values from 0.5 to 2
- w_in: bfloat16 [2048, 2048], P(('mix', 'seq')), parts along dimension 0, may hold values from -0.1875 to 0.1875
- dw_kernel: float32 [62, 1024], P('mix', 'seq'), parts along dimension 0, may hold values from -1 to 1
- bn_gain: float32 [2048], P(('mix', 'seq')), parts along dimension 0, may hold values from 0.5 to 2
- bn_bias: float32 [2048], P(('mix', 'seq')), parts along dimension 0, may hold values from -3 to 3
- w_out: bfloat16 [2048, 1024], P(('mix', 'seq')), parts along dimension 0, may hold values from -0.1875 to 0.1875
Outputs:
- outputs: bfloat16 [4096, 1024], P(('mix', 'seq')), parts along dimension 0
- grad_frames: bfloat16 [4096, 1024], P(('mix', 'seq')), parts along dimension 0
- grad_w_in: float32 [2048, 2048], P(('mix', 'seq')), parts along dimension 0
- grad_w_out: float32 [2048, 1024], P(('mix', 'seq')), parts along dimension 0
- grad_kernel: float32 [62, 1024], P('mix', 'seq'), parts along dimension 0
- grad_ln_gain: float32 [2048], P(('mix', 'seq')), parts along dimension 0
- grad_bn_gain: float32 [2048], P(('mix', 'seq')), parts along dimension 0
- grad_bn_bias: float32 [2048], P(('mix', 'seq')), parts along dimension 0
The draws below stay inside these ranges and needn't reach their ends.
There are 2 independent parts, one for each index of `mix`. The reference program is written for one: setup_inputs(seed, part) draws one part's arguments, and reference() takes and returns one part's arrays. A program takes and returns all parts, laid end to end along the dimension named above; each array names one. Nothing has to cross between parts.
Inputs may be any that keep to these rules, and one draw needn't show every extreme that they name: `segment_ids`: ids never fall along the stream; every utterance number is used, by 1 to 1500 consecutive frames, one utterance exactly 1500.
All inputs are finite; a program needn't handle non-finite values.
Results may differ from the reference program's by a relative error of at most 0.012.
The reference program's roundings to bfloat16 on the way (of `ln_x`, `glu`, `activation` and `grad_hidden`) count: a program that leaves them out, or rounds other values in their place, can miss the bound.
Values may be sent and summed in bfloat16 or wider, within the bound.
No kernel may reach another device: no remote copies, remote signals or barrier semaphores. Data moves between devices by JAX's collectives and lax.ppermute only.
A program may use at most 128 MiB of HBM per device.

```python
import math
import jax
import jax.numpy as jnp
import numpy as np
from jax import lax

D = 1024
KERNEL = 31
FRAMES = 2048
MAXLEN = 1500
UTTS = 3


def draw_frames(key, part):
    noise_key, pattern_key = jax.random.split(key)
    position = jnp.arange(FRAMES, dtype=jnp.float32)[:, None] / FRAMES
    noise = jax.random.truncated_normal(noise_key, -6.0, 6.0, (FRAMES, D), jnp.float32)
    pattern = jax.random.truncated_normal(pattern_key, -4.0, 4.0, (D,), jnp.float32)
    rising = 3.0 * position
    return (noise + rising * pattern).astype(jnp.bfloat16)


def shard_levels(key, extent, cuts, least, largest):
    factor_of, own = 1.0, jax.random.fold_in(key, 6)
    for axis_at, parts in cuts:
        steps = jnp.exp(jax.random.uniform(jax.random.fold_in(own, axis_at), (parts,), jnp.float32, least / len(cuts), largest / len(cuts)))
        factor_of = factor_of * jnp.repeat(steps, extent[axis_at] // parts).reshape([-1 if axis == axis_at else 1 for axis in range(len(extent))])
    return factor_of


def profile(amount, total, bound, lean):
    weights = [(1 << 20) // math.isqrt(rank ** lean) + 1 for rank in range(2, amount + 1)]
    surplus, counts = total - bound - (amount - 1), [1] * (amount - 1)
    while surplus > 0:
        candidates = [i for i in range(amount - 1) if counts[i] < bound]
        whole, remaining = sum([weights[i] for i in candidates]), surplus
        for i in candidates:
            addition = min(bound - counts[i], max(1, remaining * weights[i] // whole), surplus)
            counts[i] = counts[i] + addition
            surplus = surplus - addition
    return np.array([bound] + counts)


def ragged(own_key, amount, total, limit, skew):
    if amount == 2:
        one = jax.random.randint(own_key, (), max(1, total - limit), min(limit, total - 1) + 1)
        return jnp.stack([one, total - one])
    sizes = jnp.asarray(profile(amount, total, limit, skew), jnp.int32)
    pairs = (amount - 1) // 2
    giver, taker = sizes[1:1 + 2 * pairs:2], sizes[2:2 + 2 * pairs:2]
    slack = jnp.minimum(giver - 1, limit - taker)
    passed = jax.random.randint(jax.random.fold_in(own_key, 1), (pairs,), 0, 1 << 20) % (slack + 1)
    sizes = sizes.at[1:1 + 2 * pairs:2].set(giver - passed).at[2:2 + 2 * pairs:2].set(taker + passed)
    return sizes[jax.random.permutation(jax.random.fold_in(own_key, 2), amount)]


def normal_values(key, dims, deviation, limit, pieces=(), kind=jnp.bfloat16):
    result = deviation * jax.random.normal(key, dims, jnp.float32)
    if pieces:
        result = result * shard_levels(key, dims, pieces, -0.22, 0.18)
    return jnp.clip(result, -limit, limit).astype(kind)


def setup_inputs(seed: int = 0, part: int = 0) -> dict:
    arg_keys = jax.random.split(jax.random.key(seed), 10)
    part_keys = jax.random.split(jax.random.fold_in(arg_keys[9], part), 10)
    frames = draw_frames(jax.random.fold_in(jax.random.fold_in(arg_keys[9], part), 71), part)
    segment_ids = jnp.searchsorted(jnp.cumsum(ragged(part_keys[1], UTTS, FRAMES, MAXLEN, 2)), jnp.arange(FRAMES), side="right").astype(jnp.int32)
    out_grad = normal_values(part_keys[2], (FRAMES, D), 1.0, 6.0, ((0, 16),))
    ln_gain = jnp.clip(jnp.exp(math.log(2.0) - 1.3862944 * jax.random.uniform(part_keys[3], (D,), jnp.float32) ** shard_levels(part_keys[3], (D,), ((0, 16),), -0.2, 0.2)), 0.5, 2.0)
    w_in = normal_values(part_keys[4], (D, 2 * D), D ** -0.5, 0.1875, ((0, 16),))
    dw_kernel = normal_values(part_keys[5], (KERNEL, D), KERNEL ** -0.5, 1.0, ((1, 16),), jnp.float32)
    bn_gain = jnp.clip(jnp.exp(math.log(2.0) - 1.3862944 * jax.random.uniform(part_keys[6], (D,), jnp.float32) ** shard_levels(part_keys[6], (D,), ((0, 16),), -0.2, 0.2)), 0.5, 2.0)
    bn_bias = normal_values(part_keys[7], (D,), 0.5, 3.0, ((0, 16),), jnp.float32)
    w_out = normal_values(part_keys[8], (D, D), D ** -0.5, 0.1875, ((0, 16),))
    return {"frames": frames, "segment_ids": segment_ids, "out_grad": out_grad, "ln_gain": ln_gain, "w_in": w_in, "dw_kernel": dw_kernel, "bn_gain": bn_gain, "bn_bias": bn_bias, "w_out": w_out}


EPSILON = 1e-05

def reference(frames, segment_ids, out_grad, ln_gain, w_in, dw_kernel, bn_gain, bn_bias, w_out):
    margin = KERNEL // 2
    grad_scale = 1.0 / math.sqrt(FRAMES)
    frames_float = frames.astype(jnp.float32)
    mean_ln = lax.optimization_barrier(jnp.mean(frames_float, axis=1, keepdims=True))
    centred = frames_float - mean_ln
    rstd_ln = lax.rsqrt(lax.optimization_barrier(jnp.mean(centred * centred, axis=1, keepdims=True)) + EPSILON)
    ln_hat = centred * rstd_ln
    ln_x = (ln_hat * ln_gain).astype(jnp.bfloat16)
    hidden = jnp.dot(ln_x, w_in, preferred_element_type=jnp.float32)
    left_half = hidden[:, :D]
    right_gate = jax.nn.sigmoid(hidden[:, D:])
    glu = (left_half * right_gate).astype(jnp.bfloat16)
    own_ids = segment_ids + 1
    padded_ids = jnp.pad(own_ids, margin)
    masks = [(padded_ids[tap_index:tap_index + FRAMES] == own_ids).astype(jnp.float32)[:, None] for tap_index in range(KERNEL)]
    padded_glu = jnp.pad(glu, ((margin, margin), (0, 0)))
    conv_out = jnp.zeros((FRAMES, D), jnp.float32)
    for tap_index in range(KERNEL):
        conv_out = conv_out + dw_kernel[tap_index] * padded_glu[tap_index:tap_index + FRAMES].astype(jnp.float32) * masks[tap_index]
    bn_mean = lax.optimization_barrier(jnp.sum(conv_out, axis=0)) / FRAMES
    bn_var = lax.optimization_barrier(jnp.sum((conv_out - bn_mean) ** 2, axis=0)) / FRAMES
    bn_rstd = lax.rsqrt(bn_var + EPSILON)
    bn_hat = (conv_out - bn_mean) * bn_rstd
    zed = bn_hat * bn_gain + bn_bias
    zed_gate = jax.nn.sigmoid(zed)
    activation = (zed * zed_gate).astype(jnp.bfloat16)
    projected = jnp.dot(activation, w_out, preferred_element_type=jnp.float32)
    outputs = (frames_float + projected).astype(jnp.bfloat16)
    grad_w_out = jnp.dot(activation.T, out_grad, preferred_element_type=jnp.float32) * grad_scale
    grad_act = jnp.dot(out_grad, w_out.T, preferred_element_type=jnp.float32)
    grad_zed = grad_act * zed_gate * (1.0 + zed * (1.0 - zed_gate))
    bias_total = lax.optimization_barrier(jnp.sum(grad_zed, axis=0))
    gain_total = lax.optimization_barrier(jnp.sum(grad_zed * bn_hat, axis=0))
    grad_conv = bn_gain * bn_rstd * (grad_zed - bias_total / FRAMES - bn_hat * gain_total / FRAMES)
    kernel_rows = [lax.optimization_barrier(jnp.sum(grad_conv * padded_glu[tap_index:tap_index + FRAMES].astype(jnp.float32) * masks[tap_index], axis=0)) for tap_index in range(KERNEL)]
    grad_kernel = jnp.stack(kernel_rows) * grad_scale
    padded_conv = jnp.pad(grad_conv, ((margin, margin), (0, 0)))
    grad_glu = jnp.zeros((FRAMES, D), jnp.float32)
    for tap_index in range(KERNEL):
        mirror = 2 * margin - tap_index
        grad_glu = grad_glu + dw_kernel[tap_index] * padded_conv[mirror:mirror + FRAMES] * masks[mirror]
    grad_hidden = jnp.concatenate([grad_glu * right_gate, grad_glu * left_half * right_gate * (1.0 - right_gate)], axis=1).astype(jnp.bfloat16)
    grad_w_in = jnp.dot(ln_x.T, grad_hidden, preferred_element_type=jnp.float32) * grad_scale
    grad_ln = jnp.dot(grad_hidden, w_in.T, preferred_element_type=jnp.float32)
    grad_ln_gain = lax.optimization_barrier(jnp.sum(grad_ln * ln_hat, axis=0)) * grad_scale
    grad_hat = grad_ln * ln_gain
    grad_input = rstd_ln * (grad_hat - lax.optimization_barrier(jnp.mean(grad_hat, axis=1, keepdims=True)) - ln_hat * lax.optimization_barrier(jnp.mean(grad_hat * ln_hat, axis=1, keepdims=True)))
    grad_frames = (out_grad.astype(jnp.float32) + grad_input).astype(jnp.bfloat16)
    return (outputs, grad_frames, grad_w_in, grad_w_out, grad_kernel, grad_ln_gain, gain_total * grad_scale, bias_total * grad_scale)
```

```python
import math

import jax
import jax.numpy as jnp
from jax import lax
from jax.sharding import PartitionSpec as P

EPSILON = 1e-05


def with_halo(cells, sides, width):
    for axis, dim in sides:
        count = lax.axis_size(axis)
        ends = count - 1
        head = lax.slice_in_dim(cells, 0, width, axis=dim)
        tail = lax.slice_in_dim(cells, cells.shape[dim] - width, cells.shape[dim], axis=dim)
        cells = jnp.concatenate(
            [
                lax.ppermute(tail, axis, [(i, (i + 1) % count) for i in range(ends)]),
                cells,
                lax.ppermute(head, axis, [((i + 1) % count, i) for i in range(ends)]),
            ],
            axis=dim,
        )
    return cells


def local(frames, segment_ids, out_grad, ln_gain, w_in, dw_kernel, bn_gain, bn_bias, w_out):
    frame_count = frames.shape[0]
    width = frames.shape[1]
    taps = dw_kernel.shape[0]
    margin = taps // 2
    devices = lax.axis_size("seq")
    stream = frame_count * devices
    grad_scale = 1.0 / math.sqrt(stream)
    share = width // devices
    gains, kernel, bn_scale, bn_shift = (
        lax.all_gather(ln_gain, "seq", axis=0, tiled=True),
        lax.all_gather(dw_kernel, "seq", axis=1, tiled=True),
        lax.all_gather(bn_gain, "seq", axis=0, tiled=True),
        lax.all_gather(bn_bias, "seq", axis=0, tiled=True),
    )
    own_ids = segment_ids + 1
    padded_ids = with_halo(own_ids, (("seq", 0),), margin)
    masks = [
        (padded_ids[tap_index : tap_index + frame_count] == own_ids).astype(jnp.float32)[:, None]
        for tap_index in range(taps)
    ]
    frames_float = frames.astype(jnp.float32)
    mean_ln = jnp.mean(frames_float, axis=1, keepdims=True)
    centred = frames_float - mean_ln
    rstd_ln = lax.rsqrt(jnp.mean(centred * centred, axis=1, keepdims=True) + EPSILON)
    ln_hat = centred * rstd_ln
    ln_x = (ln_hat * gains).astype(jnp.bfloat16)
    columns = ln_x
    hidden = jnp.dot(
        columns, lax.all_gather(w_in, "seq", axis=0, tiled=True), preferred_element_type=jnp.float32
    )
    left_half = hidden[:, :width]
    right_gate = jax.nn.sigmoid(hidden[:, width:])
    glu = (left_half * right_gate).astype(jnp.bfloat16)
    padded_glu = with_halo(glu, (("seq", 0),), margin)
    conv_out = jnp.zeros((frame_count, width), jnp.float32)
    for tap_index in range(taps):
        conv_out = (
            conv_out
            + kernel[tap_index]
            * padded_glu[tap_index : tap_index + frame_count].astype(jnp.float32)
            * masks[tap_index]
        )
    plain_sums, square_sums = lax.psum(
        (jnp.sum(conv_out, axis=0), jnp.sum(conv_out * conv_out, axis=0)), "seq"
    )
    bn_mean = plain_sums / stream
    bn_var = square_sums / stream - bn_mean * bn_mean
    bn_rstd = lax.rsqrt(bn_var + EPSILON)
    bn_hat = (conv_out - bn_mean) * bn_rstd
    zed = bn_hat * bn_scale + bn_shift
    zed_gate = jax.nn.sigmoid(zed)
    activation = (zed * zed_gate).astype(jnp.bfloat16)
    columns = activation
    projected = jnp.dot(
        columns,
        lax.all_gather(w_out, "seq", axis=0, tiled=True),
        preferred_element_type=jnp.float32,
    )
    outputs = (frames_float + projected).astype(jnp.bfloat16)
    grad_w_out = lax.psum_scatter(
        jnp.einsum("fa,fb->ab", activation, out_grad, preferred_element_type=jnp.float32)
        * grad_scale,
        "seq",
        scatter_dimension=0,
        tiled=True,
    )
    grad_act = jnp.einsum(
        "fe,ne->fn",
        out_grad,
        lax.all_gather(w_out, "seq", axis=0, tiled=True),
        preferred_element_type=jnp.float32,
    )
    grad_zed = grad_act * zed_gate * (1.0 + zed * (1.0 - zed_gate))
    bias_total, gain_total = lax.psum(
        (jnp.sum(grad_zed, axis=0), jnp.sum(grad_zed * bn_hat, axis=0)), "seq"
    )
    grad_conv = bn_scale * bn_rstd * (grad_zed - bias_total / stream - bn_hat * gain_total / stream)
    first_channel = lax.axis_index("seq") * share
    grad_bn_bias = lax.dynamic_slice_in_dim(bias_total, first_channel, share, 0) * grad_scale
    grad_bn_gain = lax.dynamic_slice_in_dim(gain_total, first_channel, share, 0) * grad_scale
    kernel_rows = [
        jnp.sum(
            grad_conv
            * padded_glu[tap_index : tap_index + frame_count].astype(jnp.float32)
            * masks[tap_index],
            axis=0,
        )
        for tap_index in range(taps)
    ]
    kernel_term = jnp.stack(kernel_rows) * grad_scale
    padded_conv = with_halo(grad_conv, (("seq", 0),), margin)
    grad_glu = jnp.zeros((frame_count, width), jnp.float32)
    for tap_index in range(taps):
        mirror = 2 * margin - tap_index
        grad_glu = (
            grad_glu
            + kernel[tap_index] * padded_conv[mirror : mirror + frame_count] * masks[mirror]
        )
    grad_hidden = jnp.concatenate(
        [grad_glu * right_gate, grad_glu * left_half * right_gate * (1.0 - right_gate)], axis=1
    ).astype(jnp.bfloat16)
    grad_ln = jnp.einsum(
        "fe,ne->fn",
        grad_hidden,
        lax.all_gather(w_in, "seq", axis=0, tiled=True),
        preferred_element_type=jnp.float32,
    )
    in_term = (
        jnp.einsum("fa,fb->ab", ln_x, grad_hidden, preferred_element_type=jnp.float32) * grad_scale
    )
    gain_term = jnp.sum(grad_ln * ln_hat, axis=0) * grad_scale
    grad_w_in, grad_kernel, grad_ln_gain = (
        lax.psum_scatter(in_term, "seq", scatter_dimension=0, tiled=True),
        lax.psum_scatter(kernel_term, "seq", scatter_dimension=1, tiled=True),
        lax.psum_scatter(gain_term, "seq", scatter_dimension=0, tiled=True),
    )
    grad_hat = grad_ln * gains
    grad_input = rstd_ln * (
        grad_hat
        - jnp.mean(grad_hat, axis=1, keepdims=True)
        - ln_hat * jnp.mean(grad_hat * ln_hat, axis=1, keepdims=True)
    )
    grad_frames = (out_grad.astype(jnp.float32) + grad_input).astype(jnp.bfloat16)
    return (
        outputs,
        grad_frames,
        grad_w_in,
        grad_w_out,
        grad_kernel,
        grad_ln_gain,
        grad_bn_gain,
        grad_bn_bias,
    )


def channel_local(frames, segment_ids, out_grad, ln_gain, w_in, dw_kernel, bn_gain, bn_bias, w_out):
    rows = frames.shape[0]
    width = frames.shape[1]
    taps = dw_kernel.shape[0]
    margin = taps // 2
    devices = lax.axis_size("seq")
    stream = rows * devices
    grad_scale = 1.0 / math.sqrt(stream)
    share = width // devices

    small = lax.all_gather(
        jnp.concatenate([ln_gain, segment_ids.astype(jnp.float32)]), "seq", axis=0
    )
    gains = small[:, :share].reshape(width)
    all_ids = small[:, share:].reshape(stream).astype(jnp.int32)

    frames_all = lax.all_gather(frames, "seq", axis=0, tiled=True)
    w_out_all = lax.all_gather(w_out, "seq", axis=0, tiled=True)
    grad_all = lax.all_gather(out_grad, "seq", axis=0, tiled=True)
    w_in_all = lax.all_gather(w_in, "seq", axis=0, tiled=True)

    w_in_cols = lax.all_to_all(
        w_in.reshape(share, 2, devices, share).transpose(2, 0, 1, 3),
        "seq", 0, 0, tiled=True,
    ).reshape(width, 2 * share)

    def norm(block):
        block_float = block.astype(jnp.float32)
        mean = jnp.mean(block_float, axis=1, keepdims=True)
        centred = block_float - mean
        rstd = lax.rsqrt(jnp.mean(centred * centred, axis=1, keepdims=True) + EPSILON)
        return centred * rstd, rstd

    ln_all, _ = norm(frames_all)
    ln_x_all = (ln_all * gains).astype(jnp.bfloat16)

    hidden = jnp.dot(ln_x_all, w_in_cols, preferred_element_type=jnp.float32)
    left_half = hidden[:, :share]
    right_gate = jax.nn.sigmoid(hidden[:, share:])
    glu = (left_half * right_gate).astype(jnp.bfloat16)

    own_ids = all_ids + 1
    padded_ids = jnp.pad(own_ids, margin)
    masks = [
        (padded_ids[tap_index : tap_index + stream] == own_ids).astype(jnp.float32)[:, None]
        for tap_index in range(taps)
    ]
    padded_glu = jnp.pad(glu, ((margin, margin), (0, 0)))
    conv_out = jnp.zeros((stream, share), jnp.float32)
    for tap_index in range(taps):
        conv_out = (
            conv_out
            + dw_kernel[tap_index]
            * padded_glu[tap_index : tap_index + stream].astype(jnp.float32)
            * masks[tap_index]
        )
    bn_mean = jnp.sum(conv_out, axis=0) / stream
    bn_var = jnp.sum((conv_out - bn_mean) ** 2, axis=0) / stream
    bn_rstd = lax.rsqrt(bn_var + EPSILON)
    bn_hat = (conv_out - bn_mean) * bn_rstd
    zed = bn_hat * bn_gain + bn_bias
    zed_gate = jax.nn.sigmoid(zed)
    activation = (zed * zed_gate).astype(jnp.bfloat16)

    act_rows = (
        lax.all_to_all(activation.reshape(devices, rows, share), "seq", 0, 0, tiled=True)
        .transpose(1, 0, 2)
        .reshape(rows, width)
    )
    projected = jnp.dot(act_rows, w_out_all, preferred_element_type=jnp.float32)
    outputs = (frames.astype(jnp.float32) + projected).astype(jnp.bfloat16)

    grad_w_out = (
        jnp.einsum("fa,fb->ab", activation, grad_all, preferred_element_type=jnp.float32)
        * grad_scale
    )
    grad_act = jnp.einsum("fe,ne->fn", grad_all, w_out, preferred_element_type=jnp.float32)
    grad_zed = grad_act * zed_gate * (1.0 + zed * (1.0 - zed_gate))
    bias_total = jnp.sum(grad_zed, axis=0)
    gain_total = jnp.sum(grad_zed * bn_hat, axis=0)
    grad_conv = bn_gain * bn_rstd * (grad_zed - bias_total / stream - bn_hat * gain_total / stream)
    grad_kernel = (
        jnp.stack(
            [
                jnp.sum(
                    grad_conv
                    * padded_glu[tap_index : tap_index + stream].astype(jnp.float32)
                    * masks[tap_index],
                    axis=0,
                )
                for tap_index in range(taps)
            ]
        )
        * grad_scale
    )
    padded_conv = jnp.pad(grad_conv, ((margin, margin), (0, 0)))
    grad_glu = jnp.zeros((stream, share), jnp.float32)
    for tap_index in range(taps):
        mirror = 2 * margin - tap_index
        grad_glu = (
            grad_glu
            + dw_kernel[tap_index] * padded_conv[mirror : mirror + stream] * masks[mirror]
        )
    grad_hidden = jnp.concatenate(
        [grad_glu * right_gate, grad_glu * left_half * right_gate * (1.0 - right_gate)], axis=1
    ).astype(jnp.bfloat16)

    in_cols = (
        jnp.einsum("fa,fb->ab", ln_x_all, grad_hidden, preferred_element_type=jnp.float32)
        * grad_scale
    )
    grad_w_in = (
        lax.all_to_all(in_cols.reshape(devices, share, 2, share), "seq", 0, 0, tiled=True)
        .transpose(1, 2, 0, 3)
        .reshape(share, 2 * width)
    )
    hidden_rows = (
        lax.all_to_all(grad_hidden.reshape(devices, rows, 2, share), "seq", 0, 0, tiled=True)
        .transpose(1, 2, 0, 3)
        .reshape(rows, 2 * width)
    )
    grad_ln = jnp.einsum(
        "fe,ne->fn", hidden_rows, w_in_all, preferred_element_type=jnp.float32
    )
    ln_hat, rstd_ln = norm(frames)
    grad_ln_gain = lax.psum_scatter(
        jnp.sum(grad_ln * ln_hat, axis=0) * grad_scale, "seq", scatter_dimension=0, tiled=True
    )
    grad_hat = grad_ln * gains
    grad_input = rstd_ln * (
        grad_hat
        - jnp.mean(grad_hat, axis=1, keepdims=True)
        - ln_hat * jnp.mean(grad_hat * ln_hat, axis=1, keepdims=True)
    )
    grad_frames = (out_grad.astype(jnp.float32) + grad_input).astype(jnp.bfloat16)
    return (
        outputs,
        grad_frames,
        grad_w_in,
        grad_w_out,
        grad_kernel,
        grad_ln_gain,
        gain_total * grad_scale,
        bias_total * grad_scale,
    )


def solution(mesh):
    devices = mesh.shape["seq"]
    body = channel_local if devices <= 16 else local
    return jax.shard_map(
        body,
        mesh=mesh,
        in_specs=(
            P(("mix", "seq"), None),
            P(("mix", "seq")),
            P(("mix", "seq"), None),
            P(("mix", "seq")),
            P(("mix", "seq"), None),
            P("mix", "seq"),
            P(("mix", "seq")),
            P(("mix", "seq")),
            P(("mix", "seq"), None),
        ),
        out_specs=(
            P(("mix", "seq"), None),
            P(("mix", "seq"), None),
            P(("mix", "seq"), None),
            P(("mix", "seq"), None),
            P("mix", "seq"),
            P(("mix", "seq")),
            P(("mix", "seq")),
            P(("mix", "seq")),
        ),
        check_vma=False,
    )
```

```python
import math

import jax
import jax.numpy as jnp
from jax import lax
from jax.sharding import PartitionSpec as P

EPSILON = 1e-05


def with_halo(cells, sides, width):
    for axis, dim in sides:
        count = lax.axis_size(axis)
        ends = count - 1
        head = lax.slice_in_dim(cells, 0, width, axis=dim)
        tail = lax.slice_in_dim(cells, cells.shape[dim] - width, cells.shape[dim], axis=dim)
        cells = jnp.concatenate(
            [
                lax.ppermute(tail, axis, [(i, (i + 1) % count) for i in range(ends)]),
                cells,
                lax.ppermute(head, axis, [((i + 1) % count, i) for i in range(ends)]),
            ],
            axis=dim,
        )
    return cells


def local(frames, segment_ids, out_grad, ln_gain, w_in, dw_kernel, bn_gain, bn_bias, w_out):
    frame_count = frames.shape[0]
    width = frames.shape[1]
    taps = dw_kernel.shape[0]
    margin = taps // 2
    devices = lax.axis_size("seq")
    stream = frame_count * devices
    grad_scale = 1.0 / math.sqrt(stream)
    share = width // devices
    gains, kernel, bn_scale, bn_shift = (
        lax.all_gather(ln_gain, "seq", axis=0, tiled=True),
        lax.all_gather(dw_kernel, "seq", axis=1, tiled=True),
        lax.all_gather(bn_gain, "seq", axis=0, tiled=True),
        lax.all_gather(bn_bias, "seq", axis=0, tiled=True),
    )
    own_ids = segment_ids + 1
    padded_ids = with_halo(own_ids, (("seq", 0),), margin)
    masks = [
        (padded_ids[tap_index : tap_index + frame_count] == own_ids).astype(jnp.float32)[:, None]
        for tap_index in range(taps)
    ]
    frames_float = frames.astype(jnp.float32)
    mean_ln = jnp.mean(frames_float, axis=1, keepdims=True)
    centred = frames_float - mean_ln
    rstd_ln = lax.rsqrt(jnp.mean(centred * centred, axis=1, keepdims=True) + EPSILON)
    ln_hat = centred * rstd_ln
    ln_x = (ln_hat * gains).astype(jnp.bfloat16)
    columns = ln_x
    hidden = jnp.dot(
        columns, lax.all_gather(w_in, "seq", axis=0, tiled=True), preferred_element_type=jnp.float32
    )
    left_half = hidden[:, :width]
    right_gate = jax.nn.sigmoid(hidden[:, width:])
    glu = (left_half * right_gate).astype(jnp.bfloat16)
    padded_glu = with_halo(glu, (("seq", 0),), margin)
    conv_out = jnp.zeros((frame_count, width), jnp.float32)
    for tap_index in range(taps):
        conv_out = (
            conv_out
            + kernel[tap_index]
            * padded_glu[tap_index : tap_index + frame_count].astype(jnp.float32)
            * masks[tap_index]
        )
    plain_sums, square_sums = lax.psum(
        (jnp.sum(conv_out, axis=0), jnp.sum(conv_out * conv_out, axis=0)), "seq"
    )
    bn_mean = plain_sums / stream
    bn_var = square_sums / stream - bn_mean * bn_mean
    bn_rstd = lax.rsqrt(bn_var + EPSILON)
    bn_hat = (conv_out - bn_mean) * bn_rstd
    zed = bn_hat * bn_scale + bn_shift
    zed_gate = jax.nn.sigmoid(zed)
    activation = (zed * zed_gate).astype(jnp.bfloat16)
    columns = activation
    projected = jnp.dot(
        columns,
        lax.all_gather(w_out, "seq", axis=0, tiled=True),
        preferred_element_type=jnp.float32,
    )
    outputs = (frames_float + projected).astype(jnp.bfloat16)
    grad_w_out = lax.psum_scatter(
        jnp.einsum("fa,fb->ab", activation, out_grad, preferred_element_type=jnp.float32)
        * grad_scale,
        "seq",
        scatter_dimension=0,
        tiled=True,
    )
    grad_act = jnp.einsum(
        "fe,ne->fn",
        out_grad,
        lax.all_gather(w_out, "seq", axis=0, tiled=True),
        preferred_element_type=jnp.float32,
    )
    grad_zed = grad_act * zed_gate * (1.0 + zed * (1.0 - zed_gate))
    bias_total, gain_total = lax.psum(
        (jnp.sum(grad_zed, axis=0), jnp.sum(grad_zed * bn_hat, axis=0)), "seq"
    )
    grad_conv = bn_scale * bn_rstd * (grad_zed - bias_total / stream - bn_hat * gain_total / stream)
    first_channel = lax.axis_index("seq") * share
    grad_bn_bias = lax.dynamic_slice_in_dim(bias_total, first_channel, share, 0) * grad_scale
    grad_bn_gain = lax.dynamic_slice_in_dim(gain_total, first_channel, share, 0) * grad_scale
    kernel_rows = [
        jnp.sum(
            grad_conv
            * padded_glu[tap_index : tap_index + frame_count].astype(jnp.float32)
            * masks[tap_index],
            axis=0,
        )
        for tap_index in range(taps)
    ]
    kernel_term = jnp.stack(kernel_rows) * grad_scale
    padded_conv = with_halo(grad_conv, (("seq", 0),), margin)
    grad_glu = jnp.zeros((frame_count, width), jnp.float32)
    for tap_index in range(taps):
        mirror = 2 * margin - tap_index
        grad_glu = (
            grad_glu
            + kernel[tap_index] * padded_conv[mirror : mirror + frame_count] * masks[mirror]
        )
    grad_hidden = jnp.concatenate(
        [grad_glu * right_gate, grad_glu * left_half * right_gate * (1.0 - right_gate)], axis=1
    ).astype(jnp.bfloat16)
    grad_ln = jnp.einsum(
        "fe,ne->fn",
        grad_hidden,
        lax.all_gather(w_in, "seq", axis=0, tiled=True),
        preferred_element_type=jnp.float32,
    )
    in_term = (
        jnp.einsum("fa,fb->ab", ln_x, grad_hidden, preferred_element_type=jnp.float32) * grad_scale
    )
    gain_term = jnp.sum(grad_ln * ln_hat, axis=0) * grad_scale
    grad_w_in, grad_kernel, grad_ln_gain = (
        lax.psum_scatter(in_term, "seq", scatter_dimension=0, tiled=True),
        lax.psum_scatter(kernel_term, "seq", scatter_dimension=1, tiled=True),
        lax.psum_scatter(gain_term, "seq", scatter_dimension=0, tiled=True),
    )
    grad_hat = grad_ln * gains
    grad_input = rstd_ln * (
        grad_hat
        - jnp.mean(grad_hat, axis=1, keepdims=True)
        - ln_hat * jnp.mean(grad_hat * ln_hat, axis=1, keepdims=True)
    )
    grad_frames = (out_grad.astype(jnp.float32) + grad_input).astype(jnp.bfloat16)
    return (
        outputs,
        grad_frames,
        grad_w_in,
        grad_w_out,
        grad_kernel,
        grad_ln_gain,
        grad_bn_gain,
        grad_bn_bias,
    )


def channel_local(frames, segment_ids, out_grad, ln_gain, w_in, dw_kernel, bn_gain, bn_bias, w_out):
    rows = frames.shape[0]
    width = frames.shape[1]
    taps = dw_kernel.shape[0]
    margin = taps // 2
    devices = lax.axis_size("seq")
    stream = rows * devices
    grad_scale = 1.0 / math.sqrt(stream)
    share = width // devices

    def spread(block):
        copies = jnp.broadcast_to(block[None], (devices,) + block.shape)
        return lax.all_to_all(copies, "seq", 0, 0, tiled=True)

    small = spread(jnp.concatenate([ln_gain, segment_ids.astype(jnp.float32)]))
    gains = small[:, :share].reshape(width)
    all_ids = small[:, share:].reshape(stream).astype(jnp.int32)

    frames_all = lax.all_gather(frames, "seq", axis=0, tiled=True)
    w_out_all = lax.all_gather(w_out, "seq", axis=0, tiled=True)
    grad_all = lax.all_gather(out_grad, "seq", axis=0, tiled=True)
    w_in_all = spread(w_in).reshape(width, 2 * width)

    first_channel = lax.axis_index("seq") * share
    w_in_cols = jnp.concatenate(
        [
            lax.dynamic_slice_in_dim(w_in_all, first_channel, share, 1),
            lax.dynamic_slice_in_dim(w_in_all, width + first_channel, share, 1),
        ],
        axis=1,
    )

    def norm(block):
        block_float = block.astype(jnp.float32)
        mean = jnp.mean(block_float, axis=1, keepdims=True)
        centred = block_float - mean
        rstd = lax.rsqrt(jnp.mean(centred * centred, axis=1, keepdims=True) + EPSILON)
        return centred * rstd, rstd

    ln_all, _ = norm(frames_all)
    ln_x_all = (ln_all * gains).astype(jnp.bfloat16)

    hidden = jnp.dot(ln_x_all, w_in_cols, preferred_element_type=jnp.float32)
    left_half = hidden[:, :share]
    right_gate = jax.nn.sigmoid(hidden[:, share:])
    glu = (left_half * right_gate).astype(jnp.bfloat16)

    own_ids = all_ids + 1
    padded_ids = jnp.pad(own_ids, margin)
    masks = [
        (padded_ids[tap_index : tap_index + stream] == own_ids).astype(jnp.float32)[:, None]
        for tap_index in range(taps)
    ]
    padded_glu = jnp.pad(glu, ((margin, margin), (0, 0)))
    conv_out = jnp.zeros((stream, share), jnp.float32)
    for tap_index in range(taps):
        conv_out = (
            conv_out
            + dw_kernel[tap_index]
            * padded_glu[tap_index : tap_index + stream].astype(jnp.float32)
            * masks[tap_index]
        )
    bn_mean = jnp.sum(conv_out, axis=0) / stream
    bn_var = jnp.sum((conv_out - bn_mean) ** 2, axis=0) / stream
    bn_rstd = lax.rsqrt(bn_var + EPSILON)
    bn_hat = (conv_out - bn_mean) * bn_rstd
    zed = bn_hat * bn_gain + bn_bias
    zed_gate = jax.nn.sigmoid(zed)
    activation = (zed * zed_gate).astype(jnp.bfloat16)

    act_rows = (
        lax.all_to_all(activation.reshape(devices, rows, share), "seq", 0, 0, tiled=True)
        .transpose(1, 0, 2)
        .reshape(rows, width)
    )
    projected = jnp.dot(act_rows, w_out_all, preferred_element_type=jnp.float32)
    outputs = (frames.astype(jnp.float32) + projected).astype(jnp.bfloat16)

    grad_w_out = (
        jnp.einsum("fa,fb->ab", activation, grad_all, preferred_element_type=jnp.float32)
        * grad_scale
    )
    grad_act = jnp.einsum("fe,ne->fn", grad_all, w_out, preferred_element_type=jnp.float32)
    grad_zed = grad_act * zed_gate * (1.0 + zed * (1.0 - zed_gate))
    bias_total = jnp.sum(grad_zed, axis=0)
    gain_total = jnp.sum(grad_zed * bn_hat, axis=0)
    grad_conv = bn_gain * bn_rstd * (grad_zed - bias_total / stream - bn_hat * gain_total / stream)
    grad_kernel = (
        jnp.stack(
            [
                jnp.sum(
                    grad_conv
                    * padded_glu[tap_index : tap_index + stream].astype(jnp.float32)
                    * masks[tap_index],
                    axis=0,
                )
                for tap_index in range(taps)
            ]
        )
        * grad_scale
    )
    padded_conv = jnp.pad(grad_conv, ((margin, margin), (0, 0)))
    grad_glu = jnp.zeros((stream, share), jnp.float32)
    for tap_index in range(taps):
        mirror = 2 * margin - tap_index
        grad_glu = (
            grad_glu
            + dw_kernel[tap_index] * padded_conv[mirror : mirror + stream] * masks[mirror]
        )
    grad_hidden = jnp.concatenate(
        [grad_glu * right_gate, grad_glu * left_half * right_gate * (1.0 - right_gate)], axis=1
    ).astype(jnp.bfloat16)

    in_cols = (
        jnp.einsum("fa,fb->ab", ln_x_all, grad_hidden, preferred_element_type=jnp.float32)
        * grad_scale
    )
    hidden_rows = (
        lax.all_to_all(grad_hidden.reshape(devices, rows, 2, share), "seq", 0, 0, tiled=True)
        .transpose(1, 2, 0, 3)
        .reshape(rows, 2 * width)
    )
    grad_ln = jnp.einsum(
        "fe,ne->fn", hidden_rows, w_in_all, preferred_element_type=jnp.float32
    )
    ln_hat, rstd_ln = norm(frames)
    gain_part = jnp.sum(grad_ln * ln_hat, axis=0) * grad_scale
    packed = lax.all_to_all(
        jnp.concatenate(
            [in_cols.reshape(devices, share * 2 * share), gain_part.reshape(devices, share)],
            axis=1,
        ),
        "seq", 0, 0, tiled=True,
    )
    grad_w_in = (
        packed[:, : share * 2 * share]
        .reshape(devices, share, 2, share)
        .transpose(1, 2, 0, 3)
        .reshape(share, 2 * width)
    )
    grad_ln_gain = jnp.sum(packed[:, share * 2 * share :], axis=0)
    grad_hat = grad_ln * gains
    grad_input = rstd_ln * (
        grad_hat
        - jnp.mean(grad_hat, axis=1, keepdims=True)
        - ln_hat * jnp.mean(grad_hat * ln_hat, axis=1, keepdims=True)
    )
    grad_frames = (out_grad.astype(jnp.float32) + grad_input).astype(jnp.bfloat16)
    return (
        outputs,
        grad_frames,
        grad_w_in,
        grad_w_out,
        grad_kernel,
        grad_ln_gain,
        gain_total * grad_scale,
        bias_total * grad_scale,
    )


def solution(mesh):
    devices = mesh.shape["seq"]
    body = channel_local if devices <= 16 else local
    return jax.shard_map(
        body,
        mesh=mesh,
        in_specs=(
            P(("mix", "seq"), None),
            P(("mix", "seq")),
            P(("mix", "seq"), None),
            P(("mix", "seq")),
            P(("mix", "seq"), None),
            P("mix", "seq"),
            P(("mix", "seq")),
            P(("mix", "seq")),
            P(("mix", "seq"), None),
        ),
        out_specs=(
            P(("mix", "seq"), None),
            P(("mix", "seq"), None),
            P(("mix", "seq"), None),
            P(("mix", "seq"), None),
            P("mix", "seq"),
            P(("mix", "seq")),
            P(("mix", "seq")),
            P(("mix", "seq")),
        ),
        check_vma=False,
    )
```

```python
import math

import jax
import jax.numpy as jnp
from jax import lax
from jax.sharding import PartitionSpec as P

EPSILON = 1e-05


def with_halo(cells, sides, width):
    for axis, dim in sides:
        count = lax.axis_size(axis)
        ends = count - 1
        head = lax.slice_in_dim(cells, 0, width, axis=dim)
        tail = lax.slice_in_dim(cells, cells.shape[dim] - width, cells.shape[dim], axis=dim)
        cells = jnp.concatenate(
            [
                lax.ppermute(tail, axis, [(i, (i + 1) % count) for i in range(ends)]),
                cells,
                lax.ppermute(head, axis, [((i + 1) % count, i) for i in range(ends)]),
            ],
            axis=dim,
        )
    return cells


def local(frames, segment_ids, out_grad, ln_gain, w_in, dw_kernel, bn_gain, bn_bias, w_out):
    frame_count = frames.shape[0]
    width = frames.shape[1]
    taps = dw_kernel.shape[0]
    margin = taps // 2
    devices = lax.axis_size("seq")
    stream = frame_count * devices
    grad_scale = 1.0 / math.sqrt(stream)
    share = width // devices
    gains, kernel, bn_scale, bn_shift = (
        lax.all_gather(ln_gain, "seq", axis=0, tiled=True),
        lax.all_gather(dw_kernel, "seq", axis=1, tiled=True),
        lax.all_gather(bn_gain, "seq", axis=0, tiled=True),
        lax.all_gather(bn_bias, "seq", axis=0, tiled=True),
    )
    own_ids = segment_ids + 1
    padded_ids = with_halo(own_ids, (("seq", 0),), margin)
    masks = [
        (padded_ids[tap_index : tap_index + frame_count] == own_ids).astype(jnp.float32)[:, None]
        for tap_index in range(taps)
    ]
    frames_float = frames.astype(jnp.float32)
    mean_ln = jnp.mean(frames_float, axis=1, keepdims=True)
    centred = frames_float - mean_ln
    rstd_ln = lax.rsqrt(jnp.mean(centred * centred, axis=1, keepdims=True) + EPSILON)
    ln_hat = centred * rstd_ln
    ln_x = (ln_hat * gains).astype(jnp.bfloat16)
    columns = ln_x
    hidden = jnp.dot(
        columns, lax.all_gather(w_in, "seq", axis=0, tiled=True), preferred_element_type=jnp.float32
    )
    left_half = hidden[:, :width]
    right_gate = jax.nn.sigmoid(hidden[:, width:])
    glu = (left_half * right_gate).astype(jnp.bfloat16)
    padded_glu = with_halo(glu, (("seq", 0),), margin)
    conv_out = jnp.zeros((frame_count, width), jnp.float32)
    for tap_index in range(taps):
        conv_out = (
            conv_out
            + kernel[tap_index]
            * padded_glu[tap_index : tap_index + frame_count].astype(jnp.float32)
            * masks[tap_index]
        )
    plain_sums, square_sums = lax.psum(
        (jnp.sum(conv_out, axis=0), jnp.sum(conv_out * conv_out, axis=0)), "seq"
    )
    bn_mean = plain_sums / stream
    bn_var = square_sums / stream - bn_mean * bn_mean
    bn_rstd = lax.rsqrt(bn_var + EPSILON)
    bn_hat = (conv_out - bn_mean) * bn_rstd
    zed = bn_hat * bn_scale + bn_shift
    zed_gate = jax.nn.sigmoid(zed)
    activation = (zed * zed_gate).astype(jnp.bfloat16)
    columns = activation
    projected = jnp.dot(
        columns,
        lax.all_gather(w_out, "seq", axis=0, tiled=True),
        preferred_element_type=jnp.float32,
    )
    outputs = (frames_float + projected).astype(jnp.bfloat16)
    grad_w_out = lax.psum_scatter(
        jnp.einsum("fa,fb->ab", activation, out_grad, preferred_element_type=jnp.float32)
        * grad_scale,
        "seq",
        scatter_dimension=0,
        tiled=True,
    )
    grad_act = jnp.einsum(
        "fe,ne->fn",
        out_grad,
        lax.all_gather(w_out, "seq", axis=0, tiled=True),
        preferred_element_type=jnp.float32,
    )
    grad_zed = grad_act * zed_gate * (1.0 + zed * (1.0 - zed_gate))
    bias_total, gain_total = lax.psum(
        (jnp.sum(grad_zed, axis=0), jnp.sum(grad_zed * bn_hat, axis=0)), "seq"
    )
    grad_conv = bn_scale * bn_rstd * (grad_zed - bias_total / stream - bn_hat * gain_total / stream)
    first_channel = lax.axis_index("seq") * share
    grad_bn_bias = lax.dynamic_slice_in_dim(bias_total, first_channel, share, 0) * grad_scale
    grad_bn_gain = lax.dynamic_slice_in_dim(gain_total, first_channel, share, 0) * grad_scale
    kernel_rows = [
        jnp.sum(
            grad_conv
            * padded_glu[tap_index : tap_index + frame_count].astype(jnp.float32)
            * masks[tap_index],
            axis=0,
        )
        for tap_index in range(taps)
    ]
    kernel_term = jnp.stack(kernel_rows) * grad_scale
    padded_conv = with_halo(grad_conv, (("seq", 0),), margin)
    grad_glu = jnp.zeros((frame_count, width), jnp.float32)
    for tap_index in range(taps):
        mirror = 2 * margin - tap_index
        grad_glu = (
            grad_glu
            + kernel[tap_index] * padded_conv[mirror : mirror + frame_count] * masks[mirror]
        )
    grad_hidden = jnp.concatenate(
        [grad_glu * right_gate, grad_glu * left_half * right_gate * (1.0 - right_gate)], axis=1
    ).astype(jnp.bfloat16)
    grad_ln = jnp.einsum(
        "fe,ne->fn",
        grad_hidden,
        lax.all_gather(w_in, "seq", axis=0, tiled=True),
        preferred_element_type=jnp.float32,
    )
    in_term = (
        jnp.einsum("fa,fb->ab", ln_x, grad_hidden, preferred_element_type=jnp.float32) * grad_scale
    )
    gain_term = jnp.sum(grad_ln * ln_hat, axis=0) * grad_scale
    grad_w_in, grad_kernel, grad_ln_gain = (
        lax.psum_scatter(in_term, "seq", scatter_dimension=0, tiled=True),
        lax.psum_scatter(kernel_term, "seq", scatter_dimension=1, tiled=True),
        lax.psum_scatter(gain_term, "seq", scatter_dimension=0, tiled=True),
    )
    grad_hat = grad_ln * gains
    grad_input = rstd_ln * (
        grad_hat
        - jnp.mean(grad_hat, axis=1, keepdims=True)
        - ln_hat * jnp.mean(grad_hat * ln_hat, axis=1, keepdims=True)
    )
    grad_frames = (out_grad.astype(jnp.float32) + grad_input).astype(jnp.bfloat16)
    return (
        outputs,
        grad_frames,
        grad_w_in,
        grad_w_out,
        grad_kernel,
        grad_ln_gain,
        grad_bn_gain,
        grad_bn_bias,
    )


SEQ = ("chip", "core")


def gather_rows(block):
    chips = lax.all_gather(block, "chip", axis=0)
    both = lax.all_gather(chips, "core", axis=0)
    return both.transpose(1, 0, *range(2, both.ndim)).reshape(-1, *block.shape[1:])


def channel_local(frames, segment_ids, out_grad, ln_gain, w_in, dw_kernel, bn_gain, bn_bias, w_out):
    rows = frames.shape[0]
    width = frames.shape[1]
    taps = dw_kernel.shape[0]
    margin = taps // 2
    devices = lax.axis_size("chip") * lax.axis_size("core")
    stream = rows * devices
    grad_scale = 1.0 / math.sqrt(stream)
    share = width // devices

    def spread(block):
        copies = jnp.broadcast_to(block[None], (devices,) + block.shape)
        return lax.all_to_all(copies, SEQ, 0, 0, tiled=True)

    small = spread(jnp.concatenate([ln_gain, segment_ids.astype(jnp.float32)]))
    gains = small[:, :share].reshape(width)
    all_ids = small[:, share:].reshape(stream).astype(jnp.int32)

    frames_all = gather_rows(frames)
    w_out_all = gather_rows(w_out)
    grad_all = gather_rows(out_grad)
    w_in_all = gather_rows(w_in)

    first_channel = (lax.axis_index("chip") * lax.axis_size("core") + lax.axis_index("core")) * share
    w_in_cols = jnp.concatenate(
        [
            lax.dynamic_slice_in_dim(w_in_all, first_channel, share, 1),
            lax.dynamic_slice_in_dim(w_in_all, width + first_channel, share, 1),
        ],
        axis=1,
    )

    def norm(block):
        block_float = block.astype(jnp.float32)
        mean = jnp.mean(block_float, axis=1, keepdims=True)
        centred = block_float - mean
        rstd = lax.rsqrt(jnp.mean(centred * centred, axis=1, keepdims=True) + EPSILON)
        return centred * rstd, rstd

    ln_all, _ = norm(frames_all)
    ln_x_all = (ln_all * gains).astype(jnp.bfloat16)

    hidden = jnp.dot(ln_x_all, w_in_cols, preferred_element_type=jnp.float32)
    left_half = hidden[:, :share]
    right_gate = jax.nn.sigmoid(hidden[:, share:])
    glu = (left_half * right_gate).astype(jnp.bfloat16)

    own_ids = all_ids + 1
    padded_ids = jnp.pad(own_ids, margin)
    masks = [
        (padded_ids[tap_index : tap_index + stream] == own_ids).astype(jnp.float32)[:, None]
        for tap_index in range(taps)
    ]
    padded_glu = jnp.pad(glu, ((margin, margin), (0, 0)))
    conv_out = jnp.zeros((stream, share), jnp.float32)
    for tap_index in range(taps):
        conv_out = (
            conv_out
            + dw_kernel[tap_index]
            * padded_glu[tap_index : tap_index + stream].astype(jnp.float32)
            * masks[tap_index]
        )
    bn_mean = jnp.sum(conv_out, axis=0) / stream
    bn_var = jnp.sum((conv_out - bn_mean) ** 2, axis=0) / stream
    bn_rstd = lax.rsqrt(bn_var + EPSILON)
    bn_hat = (conv_out - bn_mean) * bn_rstd
    zed = bn_hat * bn_gain + bn_bias
    zed_gate = jax.nn.sigmoid(zed)
    activation = (zed * zed_gate).astype(jnp.bfloat16)

    act_rows = (
        lax.all_to_all(activation.reshape(devices, rows, share), SEQ, 0, 0, tiled=True)
        .transpose(1, 0, 2)
        .reshape(rows, width)
    )
    projected = jnp.dot(act_rows, w_out_all, preferred_element_type=jnp.float32)
    outputs = (frames.astype(jnp.float32) + projected).astype(jnp.bfloat16)

    grad_w_out = (
        jnp.einsum("fa,fb->ab", activation, grad_all, preferred_element_type=jnp.float32)
        * grad_scale
    )
    grad_act = jnp.einsum("fe,ne->fn", grad_all, w_out, preferred_element_type=jnp.float32)
    grad_zed = grad_act * zed_gate * (1.0 + zed * (1.0 - zed_gate))
    bias_total = jnp.sum(grad_zed, axis=0)
    gain_total = jnp.sum(grad_zed * bn_hat, axis=0)
    grad_conv = bn_gain * bn_rstd * (grad_zed - bias_total / stream - bn_hat * gain_total / stream)
    grad_kernel = (
        jnp.stack(
            [
                jnp.sum(
                    grad_conv
                    * padded_glu[tap_index : tap_index + stream].astype(jnp.float32)
                    * masks[tap_index],
                    axis=0,
                )
                for tap_index in range(taps)
            ]
        )
        * grad_scale
    )
    padded_conv = jnp.pad(grad_conv, ((margin, margin), (0, 0)))
    grad_glu = jnp.zeros((stream, share), jnp.float32)
    for tap_index in range(taps):
        mirror = 2 * margin - tap_index
        grad_glu = (
            grad_glu
            + dw_kernel[tap_index] * padded_conv[mirror : mirror + stream] * masks[mirror]
        )
    grad_hidden = jnp.concatenate(
        [grad_glu * right_gate, grad_glu * left_half * right_gate * (1.0 - right_gate)], axis=1
    ).astype(jnp.bfloat16)

    in_cols = (
        jnp.einsum("fa,fb->ab", ln_x_all, grad_hidden, preferred_element_type=jnp.float32)
        * grad_scale
    )
    hidden_rows = (
        lax.all_to_all(grad_hidden.reshape(devices, rows, 2, share), SEQ, 0, 0, tiled=True)
        .transpose(1, 2, 0, 3)
        .reshape(rows, 2 * width)
    )
    grad_ln = jnp.einsum(
        "fe,ne->fn", hidden_rows, w_in_all, preferred_element_type=jnp.float32
    )
    ln_hat, rstd_ln = norm(frames)
    gain_part = jnp.sum(grad_ln * ln_hat, axis=0) * grad_scale
    packed = lax.all_to_all(
        jnp.concatenate(
            [in_cols.reshape(devices, share * 2 * share), gain_part.reshape(devices, share)],
            axis=1,
        ),
        SEQ, 0, 0, tiled=True,
    )
    grad_w_in = (
        packed[:, : share * 2 * share]
        .reshape(devices, share, 2, share)
        .transpose(1, 2, 0, 3)
        .reshape(share, 2 * width)
    )
    grad_ln_gain = jnp.sum(packed[:, share * 2 * share :], axis=0)
    grad_hat = grad_ln * gains
    grad_input = rstd_ln * (
        grad_hat
        - jnp.mean(grad_hat, axis=1, keepdims=True)
        - ln_hat * jnp.mean(grad_hat * ln_hat, axis=1, keepdims=True)
    )
    grad_frames = (out_grad.astype(jnp.float32) + grad_input).astype(jnp.bfloat16)
    return (
        outputs,
        grad_frames,
        grad_w_in,
        grad_w_out,
        grad_kernel,
        grad_ln_gain,
        gain_total * grad_scale,
        bias_total * grad_scale,
    )


def solution(mesh):
    devices = mesh.shape["seq"]
    if devices <= 16:
        cores = 2
        grid = mesh.devices.reshape(mesh.shape["mix"], devices // cores, cores)
        mesh = jax.sharding.Mesh(grid, ("mix", "chip", "core"))
        rows = ("mix", "chip", "core")
        chans = ("chip", "core")
        body = channel_local
    else:
        rows = ("mix", "seq")
        chans = "seq"
        body = local
    return jax.shard_map(
        body,
        mesh=mesh,
        in_specs=(
            P(rows, None),
            P(rows),
            P(rows, None),
            P(rows),
            P(rows, None),
            P("mix", chans),
            P(rows),
            P(rows),
            P(rows, None),
        ),
        out_specs=(
            P(rows, None),
            P(rows, None),
            P(rows, None),
            P(rows, None),
            P("mix", chans),
            P(rows),
            P(rows),
            P(rows),
        ),
        check_vma=False,
    )
```

```python
import math

import jax
import jax.numpy as jnp
from jax import lax
from jax.sharding import PartitionSpec as P

EPSILON = 1e-05


def with_halo(cells, sides, width):
    for axis, dim in sides:
        count = lax.axis_size(axis)
        ends = count - 1
        head = lax.slice_in_dim(cells, 0, width, axis=dim)
        tail = lax.slice_in_dim(cells, cells.shape[dim] - width, cells.shape[dim], axis=dim)
        cells = jnp.concatenate(
            [
                lax.ppermute(tail, axis, [(i, (i + 1) % count) for i in range(ends)]),
                cells,
                lax.ppermute(head, axis, [((i + 1) % count, i) for i in range(ends)]),
            ],
            axis=dim,
        )
    return cells


def local(frames, segment_ids, out_grad, ln_gain, w_in, dw_kernel, bn_gain, bn_bias, w_out):
    frame_count = frames.shape[0]
    width = frames.shape[1]
    taps = dw_kernel.shape[0]
    margin = taps // 2
    devices = lax.axis_size("seq")
    stream = frame_count * devices
    grad_scale = 1.0 / math.sqrt(stream)
    share = width // devices
    gains, kernel, bn_scale, bn_shift = (
        lax.all_gather(ln_gain, "seq", axis=0, tiled=True),
        lax.all_gather(dw_kernel, "seq", axis=1, tiled=True),
        lax.all_gather(bn_gain, "seq", axis=0, tiled=True),
        lax.all_gather(bn_bias, "seq", axis=0, tiled=True),
    )
    own_ids = segment_ids + 1
    padded_ids = with_halo(own_ids, (("seq", 0),), margin)
    masks = [
        (padded_ids[tap_index : tap_index + frame_count] == own_ids).astype(jnp.float32)[:, None]
        for tap_index in range(taps)
    ]
    frames_float = frames.astype(jnp.float32)
    mean_ln = jnp.mean(frames_float, axis=1, keepdims=True)
    centred = frames_float - mean_ln
    rstd_ln = lax.rsqrt(jnp.mean(centred * centred, axis=1, keepdims=True) + EPSILON)
    ln_hat = centred * rstd_ln
    ln_x = (ln_hat * gains).astype(jnp.bfloat16)
    columns = ln_x
    hidden = jnp.dot(
        columns, lax.all_gather(w_in, "seq", axis=0, tiled=True), preferred_element_type=jnp.float32
    )
    left_half = hidden[:, :width]
    right_gate = jax.nn.sigmoid(hidden[:, width:])
    glu = (left_half * right_gate).astype(jnp.bfloat16)
    padded_glu = with_halo(glu, (("seq", 0),), margin)
    conv_out = jnp.zeros((frame_count, width), jnp.float32)
    for tap_index in range(taps):
        conv_out = (
            conv_out
            + kernel[tap_index]
            * padded_glu[tap_index : tap_index + frame_count].astype(jnp.float32)
            * masks[tap_index]
        )
    plain_sums, square_sums = lax.psum(
        (jnp.sum(conv_out, axis=0), jnp.sum(conv_out * conv_out, axis=0)), "seq"
    )
    bn_mean = plain_sums / stream
    bn_var = square_sums / stream - bn_mean * bn_mean
    bn_rstd = lax.rsqrt(bn_var + EPSILON)
    bn_hat = (conv_out - bn_mean) * bn_rstd
    zed = bn_hat * bn_scale + bn_shift
    zed_gate = jax.nn.sigmoid(zed)
    activation = (zed * zed_gate).astype(jnp.bfloat16)
    columns = activation
    projected = jnp.dot(
        columns,
        lax.all_gather(w_out, "seq", axis=0, tiled=True),
        preferred_element_type=jnp.float32,
    )
    outputs = (frames_float + projected).astype(jnp.bfloat16)
    grad_w_out = lax.psum_scatter(
        jnp.einsum("fa,fb->ab", activation, out_grad, preferred_element_type=jnp.float32)
        * grad_scale,
        "seq",
        scatter_dimension=0,
        tiled=True,
    )
    grad_act = jnp.einsum(
        "fe,ne->fn",
        out_grad,
        lax.all_gather(w_out, "seq", axis=0, tiled=True),
        preferred_element_type=jnp.float32,
    )
    grad_zed = grad_act * zed_gate * (1.0 + zed * (1.0 - zed_gate))
    bias_total, gain_total = lax.psum(
        (jnp.sum(grad_zed, axis=0), jnp.sum(grad_zed * bn_hat, axis=0)), "seq"
    )
    grad_conv = bn_scale * bn_rstd * (grad_zed - bias_total / stream - bn_hat * gain_total / stream)
    first_channel = lax.axis_index("seq") * share
    grad_bn_bias = lax.dynamic_slice_in_dim(bias_total, first_channel, share, 0) * grad_scale
    grad_bn_gain = lax.dynamic_slice_in_dim(gain_total, first_channel, share, 0) * grad_scale
    kernel_rows = [
        jnp.sum(
            grad_conv
            * padded_glu[tap_index : tap_index + frame_count].astype(jnp.float32)
            * masks[tap_index],
            axis=0,
        )
        for tap_index in range(taps)
    ]
    kernel_term = jnp.stack(kernel_rows) * grad_scale
    padded_conv = with_halo(grad_conv, (("seq", 0),), margin)
    grad_glu = jnp.zeros((frame_count, width), jnp.float32)
    for tap_index in range(taps):
        mirror = 2 * margin - tap_index
        grad_glu = (
            grad_glu
            + kernel[tap_index] * padded_conv[mirror : mirror + frame_count] * masks[mirror]
        )
    grad_hidden = jnp.concatenate(
        [grad_glu * right_gate, grad_glu * left_half * right_gate * (1.0 - right_gate)], axis=1
    ).astype(jnp.bfloat16)
    grad_ln = jnp.einsum(
        "fe,ne->fn",
        grad_hidden,
        lax.all_gather(w_in, "seq", axis=0, tiled=True),
        preferred_element_type=jnp.float32,
    )
    in_term = (
        jnp.einsum("fa,fb->ab", ln_x, grad_hidden, preferred_element_type=jnp.float32) * grad_scale
    )
    gain_term = jnp.sum(grad_ln * ln_hat, axis=0) * grad_scale
    grad_w_in, grad_kernel, grad_ln_gain = (
        lax.psum_scatter(in_term, "seq", scatter_dimension=0, tiled=True),
        lax.psum_scatter(kernel_term, "seq", scatter_dimension=1, tiled=True),
        lax.psum_scatter(gain_term, "seq", scatter_dimension=0, tiled=True),
    )
    grad_hat = grad_ln * gains
    grad_input = rstd_ln * (
        grad_hat
        - jnp.mean(grad_hat, axis=1, keepdims=True)
        - ln_hat * jnp.mean(grad_hat * ln_hat, axis=1, keepdims=True)
    )
    grad_frames = (out_grad.astype(jnp.float32) + grad_input).astype(jnp.bfloat16)
    return (
        outputs,
        grad_frames,
        grad_w_in,
        grad_w_out,
        grad_kernel,
        grad_ln_gain,
        grad_bn_gain,
        grad_bn_bias,
    )


def channel_local(frames, segment_ids, out_grad, ln_gain, w_in, dw_kernel, bn_gain, bn_bias, w_out):
    rows = frames.shape[0]
    width = frames.shape[1]
    taps = dw_kernel.shape[0]
    margin = taps // 2
    devices = lax.axis_size("seq")
    stream = rows * devices
    grad_scale = 1.0 / math.sqrt(stream)
    share = width // devices

    def spread(block):
        copies = jnp.broadcast_to(block[None], (devices,) + block.shape)
        return lax.all_to_all(copies, "seq", 0, 0, tiled=True)

    small = spread(jnp.concatenate([ln_gain, segment_ids.astype(jnp.float32)]))
    gains = small[:, :share].reshape(width)
    all_ids = small[:, share:].reshape(stream).astype(jnp.int32)

    in_rows = w_in.shape[0] * w_in.shape[1] // width
    out_rows = w_out.shape[0]
    pieces = lax.all_gather(
        jnp.concatenate([frames, out_grad, w_out, w_in.reshape(in_rows, width)], axis=0),
        "seq",
        axis=0,
    )
    frames_all = pieces[:, :rows].reshape(stream, width)
    grad_all = pieces[:, rows : 2 * rows].reshape(stream, width)
    w_out_all = pieces[:, 2 * rows : 2 * rows + out_rows].reshape(width, width)
    w_in_all = pieces[:, 2 * rows + out_rows :].reshape(width, 2 * width)

    first_channel = lax.axis_index("seq") * share
    w_in_cols = jnp.concatenate(
        [
            lax.dynamic_slice_in_dim(w_in_all, first_channel, share, 1),
            lax.dynamic_slice_in_dim(w_in_all, width + first_channel, share, 1),
        ],
        axis=1,
    )

    def norm(block):
        block_float = block.astype(jnp.float32)
        mean = jnp.mean(block_float, axis=1, keepdims=True)
        centred = block_float - mean
        rstd = lax.rsqrt(jnp.mean(centred * centred, axis=1, keepdims=True) + EPSILON)
        return centred * rstd, rstd

    ln_all, _ = norm(frames_all)
    ln_x_all = (ln_all * gains).astype(jnp.bfloat16)

    hidden = jnp.dot(ln_x_all, w_in_cols, preferred_element_type=jnp.float32)
    left_half = hidden[:, :share]
    right_gate = jax.nn.sigmoid(hidden[:, share:])
    glu = (left_half * right_gate).astype(jnp.bfloat16)

    own_ids = all_ids + 1
    padded_ids = jnp.pad(own_ids, margin)
    masks = [
        (padded_ids[tap_index : tap_index + stream] == own_ids).astype(jnp.float32)[:, None]
        for tap_index in range(taps)
    ]
    padded_glu = jnp.pad(glu, ((margin, margin), (0, 0)))
    conv_out = jnp.zeros((stream, share), jnp.float32)
    for tap_index in range(taps):
        conv_out = (
            conv_out
            + dw_kernel[tap_index]
            * padded_glu[tap_index : tap_index + stream].astype(jnp.float32)
            * masks[tap_index]
        )
    bn_mean = jnp.sum(conv_out, axis=0) / stream
    bn_var = jnp.sum((conv_out - bn_mean) ** 2, axis=0) / stream
    bn_rstd = lax.rsqrt(bn_var + EPSILON)
    bn_hat = (conv_out - bn_mean) * bn_rstd
    zed = bn_hat * bn_gain + bn_bias
    zed_gate = jax.nn.sigmoid(zed)
    activation = (zed * zed_gate).astype(jnp.bfloat16)

    act_rows = (
        lax.all_to_all(activation.reshape(devices, rows, share), "seq", 0, 0, tiled=True)
        .transpose(1, 0, 2)
        .reshape(rows, width)
    )
    projected = jnp.dot(act_rows, w_out_all, preferred_element_type=jnp.float32)
    outputs = (frames.astype(jnp.float32) + projected).astype(jnp.bfloat16)

    grad_w_out = (
        jnp.einsum("fa,fb->ab", activation, grad_all, preferred_element_type=jnp.float32)
        * grad_scale
    )
    grad_act = jnp.einsum("fe,ne->fn", grad_all, w_out, preferred_element_type=jnp.float32)
    grad_zed = grad_act * zed_gate * (1.0 + zed * (1.0 - zed_gate))
    bias_total = jnp.sum(grad_zed, axis=0)
    gain_total = jnp.sum(grad_zed * bn_hat, axis=0)
    grad_conv = bn_gain * bn_rstd * (grad_zed - bias_total / stream - bn_hat * gain_total / stream)
    grad_kernel = (
        jnp.stack(
            [
                jnp.sum(
                    grad_conv
                    * padded_glu[tap_index : tap_index + stream].astype(jnp.float32)
                    * masks[tap_index],
                    axis=0,
                )
                for tap_index in range(taps)
            ]
        )
        * grad_scale
    )
    padded_conv = jnp.pad(grad_conv, ((margin, margin), (0, 0)))
    grad_glu = jnp.zeros((stream, share), jnp.float32)
    for tap_index in range(taps):
        mirror = 2 * margin - tap_index
        grad_glu = (
            grad_glu
            + dw_kernel[tap_index] * padded_conv[mirror : mirror + stream] * masks[mirror]
        )
    grad_hidden = jnp.concatenate(
        [grad_glu * right_gate, grad_glu * left_half * right_gate * (1.0 - right_gate)], axis=1
    ).astype(jnp.bfloat16)

    in_cols = (
        jnp.einsum("fa,fb->ab", ln_x_all, grad_hidden, preferred_element_type=jnp.float32)
        * grad_scale
    )
    hidden_rows = (
        lax.all_to_all(grad_hidden.reshape(devices, rows, 2, share), "seq", 0, 0, tiled=True)
        .transpose(1, 2, 0, 3)
        .reshape(rows, 2 * width)
    )
    grad_ln = jnp.einsum(
        "fe,ne->fn", hidden_rows, w_in_all, preferred_element_type=jnp.float32
    )
    ln_hat, rstd_ln = norm(frames)
    gain_part = jnp.sum(grad_ln * ln_hat, axis=0) * grad_scale
    packed = lax.all_to_all(
        jnp.concatenate(
            [in_cols.reshape(devices, share * 2 * share), gain_part.reshape(devices, share)],
            axis=1,
        ),
        "seq", 0, 0, tiled=True,
    )
    grad_w_in = (
        packed[:, : share * 2 * share]
        .reshape(devices, share, 2, share)
        .transpose(1, 2, 0, 3)
        .reshape(share, 2 * width)
    )
    grad_ln_gain = jnp.sum(packed[:, share * 2 * share :], axis=0)
    grad_hat = grad_ln * gains
    grad_input = rstd_ln * (
        grad_hat
        - jnp.mean(grad_hat, axis=1, keepdims=True)
        - ln_hat * jnp.mean(grad_hat * ln_hat, axis=1, keepdims=True)
    )
    grad_frames = (out_grad.astype(jnp.float32) + grad_input).astype(jnp.bfloat16)
    return (
        outputs,
        grad_frames,
        grad_w_in,
        grad_w_out,
        grad_kernel,
        grad_ln_gain,
        gain_total * grad_scale,
        bias_total * grad_scale,
    )


def solution(mesh):
    devices = mesh.shape["seq"]
    body = channel_local if devices <= 16 else local
    return jax.shard_map(
        body,
        mesh=mesh,
        in_specs=(
            P(("mix", "seq"), None),
            P(("mix", "seq")),
            P(("mix", "seq"), None),
            P(("mix", "seq")),
            P(("mix", "seq"), None),
            P("mix", "seq"),
            P(("mix", "seq")),
            P(("mix", "seq")),
            P(("mix", "seq"), None),
        ),
        out_specs=(
            P(("mix", "seq"), None),
            P(("mix", "seq"), None),
            P(("mix", "seq"), None),
            P(("mix", "seq"), None),
            P("mix", "seq"),
            P(("mix", "seq")),
            P(("mix", "seq")),
            P(("mix", "seq")),
        ),
        check_vma=False,
    )
```

```python
import math

import jax
import jax.numpy as jnp
from jax import lax
from jax.sharding import PartitionSpec as P

EPSILON = 1e-05


def with_halo(cells, sides, width):
    for axis, dim in sides:
        count = lax.axis_size(axis)
        ends = count - 1
        head = lax.slice_in_dim(cells, 0, width, axis=dim)
        tail = lax.slice_in_dim(cells, cells.shape[dim] - width, cells.shape[dim], axis=dim)
        cells = jnp.concatenate(
            [
                lax.ppermute(tail, axis, [(i, (i + 1) % count) for i in range(ends)]),
                cells,
                lax.ppermute(head, axis, [((i + 1) % count, i) for i in range(ends)]),
            ],
            axis=dim,
        )
    return cells


def local(frames, segment_ids, out_grad, ln_gain, w_in, dw_kernel, bn_gain, bn_bias, w_out):
    frame_count = frames.shape[0]
    width = frames.shape[1]
    taps = dw_kernel.shape[0]
    margin = taps // 2
    devices = lax.axis_size("seq")
    stream = frame_count * devices
    grad_scale = 1.0 / math.sqrt(stream)
    share = width // devices
    gains, kernel, bn_scale, bn_shift = (
        lax.all_gather(ln_gain, "seq", axis=0, tiled=True),
        lax.all_gather(dw_kernel, "seq", axis=1, tiled=True),
        lax.all_gather(bn_gain, "seq", axis=0, tiled=True),
        lax.all_gather(bn_bias, "seq", axis=0, tiled=True),
    )
    own_ids = segment_ids + 1
    padded_ids = with_halo(own_ids, (("seq", 0),), margin)
    masks = [
        (padded_ids[tap_index : tap_index + frame_count] == own_ids).astype(jnp.float32)[:, None]
        for tap_index in range(taps)
    ]
    frames_float = frames.astype(jnp.float32)
    mean_ln = jnp.mean(frames_float, axis=1, keepdims=True)
    centred = frames_float - mean_ln
    rstd_ln = lax.rsqrt(jnp.mean(centred * centred, axis=1, keepdims=True) + EPSILON)
    ln_hat = centred * rstd_ln
    ln_x = (ln_hat * gains).astype(jnp.bfloat16)
    columns = ln_x
    hidden = jnp.dot(
        columns, lax.all_gather(w_in, "seq", axis=0, tiled=True), preferred_element_type=jnp.float32
    )
    left_half = hidden[:, :width]
    right_gate = jax.nn.sigmoid(hidden[:, width:])
    glu = (left_half * right_gate).astype(jnp.bfloat16)
    padded_glu = with_halo(glu, (("seq", 0),), margin)
    conv_out = jnp.zeros((frame_count, width), jnp.float32)
    for tap_index in range(taps):
        conv_out = (
            conv_out
            + kernel[tap_index]
            * padded_glu[tap_index : tap_index + frame_count].astype(jnp.float32)
            * masks[tap_index]
        )
    plain_sums, square_sums = lax.psum(
        (jnp.sum(conv_out, axis=0), jnp.sum(conv_out * conv_out, axis=0)), "seq"
    )
    bn_mean = plain_sums / stream
    bn_var = square_sums / stream - bn_mean * bn_mean
    bn_rstd = lax.rsqrt(bn_var + EPSILON)
    bn_hat = (conv_out - bn_mean) * bn_rstd
    zed = bn_hat * bn_scale + bn_shift
    zed_gate = jax.nn.sigmoid(zed)
    activation = (zed * zed_gate).astype(jnp.bfloat16)
    columns = activation
    projected = jnp.dot(
        columns,
        lax.all_gather(w_out, "seq", axis=0, tiled=True),
        preferred_element_type=jnp.float32,
    )
    outputs = (frames_float + projected).astype(jnp.bfloat16)
    grad_w_out = lax.psum_scatter(
        jnp.einsum("fa,fb->ab", activation, out_grad, preferred_element_type=jnp.float32)
        * grad_scale,
        "seq",
        scatter_dimension=0,
        tiled=True,
    )
    grad_act = jnp.einsum(
        "fe,ne->fn",
        out_grad,
        lax.all_gather(w_out, "seq", axis=0, tiled=True),
        preferred_element_type=jnp.float32,
    )
    grad_zed = grad_act * zed_gate * (1.0 + zed * (1.0 - zed_gate))
    bias_total, gain_total = lax.psum(
        (jnp.sum(grad_zed, axis=0), jnp.sum(grad_zed * bn_hat, axis=0)), "seq"
    )
    grad_conv = bn_scale * bn_rstd * (grad_zed - bias_total / stream - bn_hat * gain_total / stream)
    first_channel = lax.axis_index("seq") * share
    grad_bn_bias = lax.dynamic_slice_in_dim(bias_total, first_channel, share, 0) * grad_scale
    grad_bn_gain = lax.dynamic_slice_in_dim(gain_total, first_channel, share, 0) * grad_scale
    kernel_rows = [
        jnp.sum(
            grad_conv
            * padded_glu[tap_index : tap_index + frame_count].astype(jnp.float32)
            * masks[tap_index],
            axis=0,
        )
        for tap_index in range(taps)
    ]
    kernel_term = jnp.stack(kernel_rows) * grad_scale
    padded_conv = with_halo(grad_conv, (("seq", 0),), margin)
    grad_glu = jnp.zeros((frame_count, width), jnp.float32)
    for tap_index in range(taps):
        mirror = 2 * margin - tap_index
        grad_glu = (
            grad_glu
            + kernel[tap_index] * padded_conv[mirror : mirror + frame_count] * masks[mirror]
        )
    grad_hidden = jnp.concatenate(
        [grad_glu * right_gate, grad_glu * left_half * right_gate * (1.0 - right_gate)], axis=1
    ).astype(jnp.bfloat16)
    grad_ln = jnp.einsum(
        "fe,ne->fn",
        grad_hidden,
        lax.all_gather(w_in, "seq", axis=0, tiled=True),
        preferred_element_type=jnp.float32,
    )
    in_term = (
        jnp.einsum("fa,fb->ab", ln_x, grad_hidden, preferred_element_type=jnp.float32) * grad_scale
    )
    gain_term = jnp.sum(grad_ln * ln_hat, axis=0) * grad_scale
    grad_w_in, grad_kernel, grad_ln_gain = (
        lax.psum_scatter(in_term, "seq", scatter_dimension=0, tiled=True),
        lax.psum_scatter(kernel_term, "seq", scatter_dimension=1, tiled=True),
        lax.psum_scatter(gain_term, "seq", scatter_dimension=0, tiled=True),
    )
    grad_hat = grad_ln * gains
    grad_input = rstd_ln * (
        grad_hat
        - jnp.mean(grad_hat, axis=1, keepdims=True)
        - ln_hat * jnp.mean(grad_hat * ln_hat, axis=1, keepdims=True)
    )
    grad_frames = (out_grad.astype(jnp.float32) + grad_input).astype(jnp.bfloat16)
    return (
        outputs,
        grad_frames,
        grad_w_in,
        grad_w_out,
        grad_kernel,
        grad_ln_gain,
        grad_bn_gain,
        grad_bn_bias,
    )


def channel_local(frames, segment_ids, out_grad, ln_gain, w_in, dw_kernel, bn_gain, bn_bias, w_out):
    rows = frames.shape[0]
    width = frames.shape[1]
    taps = dw_kernel.shape[0]
    margin = taps // 2
    devices = lax.axis_size("seq")
    stream = rows * devices
    grad_scale = 1.0 / math.sqrt(stream)
    share = width // devices

    def spread(block):
        copies = jnp.broadcast_to(block[None], (devices,) + block.shape)
        return lax.all_to_all(copies, "seq", 0, 0, tiled=True)

    small = spread(jnp.concatenate([ln_gain, segment_ids.astype(jnp.float32)]))
    gains = small[:, :share].reshape(width)
    all_ids = small[:, share:].reshape(stream).astype(jnp.int32)

    out_rows = w_out.shape[0]
    pieces = lax.all_gather(
        jnp.concatenate([frames, out_grad, w_out, w_in[:, :width], w_in[:, width:]], axis=0),
        "seq",
        axis=0,
    )
    frames_all = pieces[:, :rows].reshape(stream, width)
    grad_all = pieces[:, rows : 2 * rows].reshape(stream, width)
    w_out_all = pieces[:, 2 * rows : 2 * rows + out_rows].reshape(width, width)
    w_in_left = pieces[:, 2 * rows + out_rows : 2 * rows + 2 * out_rows].reshape(width, width)
    w_in_right = pieces[:, 2 * rows + 2 * out_rows :].reshape(width, width)

    first_channel = lax.axis_index("seq") * share
    w_in_cols = jnp.concatenate(
        [
            lax.dynamic_slice_in_dim(w_in_left, first_channel, share, 1),
            lax.dynamic_slice_in_dim(w_in_right, first_channel, share, 1),
        ],
        axis=1,
    )

    def norm(block):
        block_float = block.astype(jnp.float32)
        mean = jnp.mean(block_float, axis=1, keepdims=True)
        centred = block_float - mean
        rstd = lax.rsqrt(jnp.mean(centred * centred, axis=1, keepdims=True) + EPSILON)
        return centred * rstd, rstd

    ln_all, _ = norm(frames_all)
    ln_x_all = (ln_all * gains).astype(jnp.bfloat16)

    hidden = jnp.dot(ln_x_all, w_in_cols, preferred_element_type=jnp.float32)
    left_half = hidden[:, :share]
    right_gate = jax.nn.sigmoid(hidden[:, share:])
    glu = (left_half * right_gate).astype(jnp.bfloat16)

    own_ids = all_ids + 1
    padded_ids = jnp.pad(own_ids, margin)
    masks = [
        (padded_ids[tap_index : tap_index + stream] == own_ids).astype(jnp.float32)[:, None]
        for tap_index in range(taps)
    ]
    padded_glu = jnp.pad(glu, ((margin, margin), (0, 0)))
    conv_out = jnp.zeros((stream, share), jnp.float32)
    for tap_index in range(taps):
        conv_out = (
            conv_out
            + dw_kernel[tap_index]
            * padded_glu[tap_index : tap_index + stream].astype(jnp.float32)
            * masks[tap_index]
        )
    bn_mean = jnp.sum(conv_out, axis=0) / stream
    bn_var = jnp.sum((conv_out - bn_mean) ** 2, axis=0) / stream
    bn_rstd = lax.rsqrt(bn_var + EPSILON)
    bn_hat = (conv_out - bn_mean) * bn_rstd
    zed = bn_hat * bn_gain + bn_bias
    zed_gate = jax.nn.sigmoid(zed)
    activation = (zed * zed_gate).astype(jnp.bfloat16)


    grad_w_out = (
        jnp.einsum("fa,fb->ab", activation, grad_all, preferred_element_type=jnp.float32)
        * grad_scale
    )
    grad_act = jnp.einsum("fe,ne->fn", grad_all, w_out, preferred_element_type=jnp.float32)
    grad_zed = grad_act * zed_gate * (1.0 + zed * (1.0 - zed_gate))
    bias_total = jnp.sum(grad_zed, axis=0)
    gain_total = jnp.sum(grad_zed * bn_hat, axis=0)
    grad_conv = bn_gain * bn_rstd * (grad_zed - bias_total / stream - bn_hat * gain_total / stream)
    grad_kernel = (
        jnp.stack(
            [
                jnp.sum(
                    grad_conv
                    * padded_glu[tap_index : tap_index + stream].astype(jnp.float32)
                    * masks[tap_index],
                    axis=0,
                )
                for tap_index in range(taps)
            ]
        )
        * grad_scale
    )
    padded_conv = jnp.pad(grad_conv, ((margin, margin), (0, 0)))
    grad_glu = jnp.zeros((stream, share), jnp.float32)
    for tap_index in range(taps):
        mirror = 2 * margin - tap_index
        grad_glu = (
            grad_glu
            + dw_kernel[tap_index] * padded_conv[mirror : mirror + stream] * masks[mirror]
        )
    grad_hidden = jnp.concatenate(
        [grad_glu * right_gate, grad_glu * left_half * right_gate * (1.0 - right_gate)], axis=1
    ).astype(jnp.bfloat16)

    in_cols = (
        jnp.einsum("fa,fb->ab", ln_x_all, grad_hidden, preferred_element_type=jnp.float32)
        * grad_scale
    )
    back = lax.all_to_all(
        jnp.concatenate([activation, grad_hidden], axis=1).reshape(devices, rows, 3 * share),
        "seq", 0, 0, tiled=True,
    )
    act_rows = back[:, :, :share].transpose(1, 0, 2).reshape(rows, width)
    hidden_rows = (
        back[:, :, share:].reshape(devices, rows, 2, share).transpose(1, 2, 0, 3)
        .reshape(rows, 2, width)
    )
    projected = jnp.dot(act_rows, w_out_all, preferred_element_type=jnp.float32)
    outputs = (frames.astype(jnp.float32) + projected).astype(jnp.bfloat16)
    grad_ln = jnp.einsum(
        "fe,ne->fn", hidden_rows[:, 0], w_in_left, preferred_element_type=jnp.float32
    ) + jnp.einsum("fe,ne->fn", hidden_rows[:, 1], w_in_right, preferred_element_type=jnp.float32)
    ln_hat, rstd_ln = norm(frames)
    gain_part = jnp.sum(grad_ln * ln_hat, axis=0) * grad_scale
    packed = lax.all_to_all(
        jnp.concatenate(
            [in_cols.reshape(devices, share * 2 * share), gain_part.reshape(devices, share)],
            axis=1,
        ),
        "seq", 0, 0, tiled=True,
    )
    grad_w_in = (
        packed[:, : share * 2 * share]
        .reshape(devices, share, 2, share)
        .transpose(1, 2, 0, 3)
        .reshape(share, 2 * width)
    )
    grad_ln_gain = jnp.sum(packed[:, share * 2 * share :], axis=0)
    grad_hat = grad_ln * gains
    grad_input = rstd_ln * (
        grad_hat
        - jnp.mean(grad_hat, axis=1, keepdims=True)
        - ln_hat * jnp.mean(grad_hat * ln_hat, axis=1, keepdims=True)
    )
    grad_frames = (out_grad.astype(jnp.float32) + grad_input).astype(jnp.bfloat16)
    return (
        outputs,
        grad_frames,
        grad_w_in,
        grad_w_out,
        grad_kernel,
        grad_ln_gain,
        gain_total * grad_scale,
        bias_total * grad_scale,
    )


def solution(mesh):
    devices = mesh.shape["seq"]
    body = channel_local if devices <= 16 else local
    return jax.shard_map(
        body,
        mesh=mesh,
        in_specs=(
            P(("mix", "seq"), None),
            P(("mix", "seq")),
            P(("mix", "seq"), None),
            P(("mix", "seq")),
            P(("mix", "seq"), None),
            P("mix", "seq"),
            P(("mix", "seq")),
            P(("mix", "seq")),
            P(("mix", "seq"), None),
        ),
        out_specs=(
            P(("mix", "seq"), None),
            P(("mix", "seq"), None),
            P(("mix", "seq"), None),
            P(("mix", "seq"), None),
            P("mix", "seq"),
            P(("mix", "seq")),
            P(("mix", "seq")),
            P(("mix", "seq")),
        ),
        check_vma=False,
    )
```

```python
import math

import jax
import jax.numpy as jnp
from jax import lax
from jax.sharding import PartitionSpec as P

EPSILON = 1e-05


def with_halo(cells, sides, width):
    for axis, dim in sides:
        count = lax.axis_size(axis)
        ends = count - 1
        head = lax.slice_in_dim(cells, 0, width, axis=dim)
        tail = lax.slice_in_dim(cells, cells.shape[dim] - width, cells.shape[dim], axis=dim)
        cells = jnp.concatenate(
            [
                lax.ppermute(tail, axis, [(i, (i + 1) % count) for i in range(ends)]),
                cells,
                lax.ppermute(head, axis, [((i + 1) % count, i) for i in range(ends)]),
            ],
            axis=dim,
        )
    return cells


def local(frames, segment_ids, out_grad, ln_gain, w_in, dw_kernel, bn_gain, bn_bias, w_out):
    frame_count = frames.shape[0]
    width = frames.shape[1]
    taps = dw_kernel.shape[0]
    margin = taps // 2
    devices = lax.axis_size("seq")
    stream = frame_count * devices
    grad_scale = 1.0 / math.sqrt(stream)
    share = width // devices
    gains, kernel, bn_scale, bn_shift = (
        lax.all_gather(ln_gain, "seq", axis=0, tiled=True),
        lax.all_gather(dw_kernel, "seq", axis=1, tiled=True),
        lax.all_gather(bn_gain, "seq", axis=0, tiled=True),
        lax.all_gather(bn_bias, "seq", axis=0, tiled=True),
    )
    own_ids = segment_ids + 1
    padded_ids = with_halo(own_ids, (("seq", 0),), margin)
    masks = [
        (padded_ids[tap_index : tap_index + frame_count] == own_ids).astype(jnp.float32)[:, None]
        for tap_index in range(taps)
    ]
    frames_float = frames.astype(jnp.float32)
    mean_ln = jnp.mean(frames_float, axis=1, keepdims=True)
    centred = frames_float - mean_ln
    rstd_ln = lax.rsqrt(jnp.mean(centred * centred, axis=1, keepdims=True) + EPSILON)
    ln_hat = centred * rstd_ln
    ln_x = (ln_hat * gains).astype(jnp.bfloat16)
    columns = ln_x
    hidden = jnp.dot(
        columns, lax.all_gather(w_in, "seq", axis=0, tiled=True), preferred_element_type=jnp.float32
    )
    left_half = hidden[:, :width]
    right_gate = jax.nn.sigmoid(hidden[:, width:])
    glu = (left_half * right_gate).astype(jnp.bfloat16)
    padded_glu = with_halo(glu, (("seq", 0),), margin)
    conv_out = jnp.zeros((frame_count, width), jnp.float32)
    for tap_index in range(taps):
        conv_out = (
            conv_out
            + kernel[tap_index]
            * padded_glu[tap_index : tap_index + frame_count].astype(jnp.float32)
            * masks[tap_index]
        )
    plain_sums, square_sums = lax.psum(
        (jnp.sum(conv_out, axis=0), jnp.sum(conv_out * conv_out, axis=0)), "seq"
    )
    bn_mean = plain_sums / stream
    bn_var = square_sums / stream - bn_mean * bn_mean
    bn_rstd = lax.rsqrt(bn_var + EPSILON)
    bn_hat = (conv_out - bn_mean) * bn_rstd
    zed = bn_hat * bn_scale + bn_shift
    zed_gate = jax.nn.sigmoid(zed)
    activation = (zed * zed_gate).astype(jnp.bfloat16)
    columns = activation
    projected = jnp.dot(
        columns,
        lax.all_gather(w_out, "seq", axis=0, tiled=True),
        preferred_element_type=jnp.float32,
    )
    outputs = (frames_float + projected).astype(jnp.bfloat16)
    grad_w_out = lax.psum_scatter(
        jnp.einsum("fa,fb->ab", activation, out_grad, preferred_element_type=jnp.float32)
        * grad_scale,
        "seq",
        scatter_dimension=0,
        tiled=True,
    )
    grad_act = jnp.einsum(
        "fe,ne->fn",
        out_grad,
        lax.all_gather(w_out, "seq", axis=0, tiled=True),
        preferred_element_type=jnp.float32,
    )
    grad_zed = grad_act * zed_gate * (1.0 + zed * (1.0 - zed_gate))
    bias_total, gain_total = lax.psum(
        (jnp.sum(grad_zed, axis=0), jnp.sum(grad_zed * bn_hat, axis=0)), "seq"
    )
    grad_conv = bn_scale * bn_rstd * (grad_zed - bias_total / stream - bn_hat * gain_total / stream)
    first_channel = lax.axis_index("seq") * share
    grad_bn_bias = lax.dynamic_slice_in_dim(bias_total, first_channel, share, 0) * grad_scale
    grad_bn_gain = lax.dynamic_slice_in_dim(gain_total, first_channel, share, 0) * grad_scale
    kernel_rows = [
        jnp.sum(
            grad_conv
            * padded_glu[tap_index : tap_index + frame_count].astype(jnp.float32)
            * masks[tap_index],
            axis=0,
        )
        for tap_index in range(taps)
    ]
    kernel_term = jnp.stack(kernel_rows) * grad_scale
    padded_conv = with_halo(grad_conv, (("seq", 0),), margin)
    grad_glu = jnp.zeros((frame_count, width), jnp.float32)
    for tap_index in range(taps):
        mirror = 2 * margin - tap_index
        grad_glu = (
            grad_glu
            + kernel[tap_index] * padded_conv[mirror : mirror + frame_count] * masks[mirror]
        )
    grad_hidden = jnp.concatenate(
        [grad_glu * right_gate, grad_glu * left_half * right_gate * (1.0 - right_gate)], axis=1
    ).astype(jnp.bfloat16)
    grad_ln = jnp.einsum(
        "fe,ne->fn",
        grad_hidden,
        lax.all_gather(w_in, "seq", axis=0, tiled=True),
        preferred_element_type=jnp.float32,
    )
    in_term = (
        jnp.einsum("fa,fb->ab", ln_x, grad_hidden, preferred_element_type=jnp.float32) * grad_scale
    )
    gain_term = jnp.sum(grad_ln * ln_hat, axis=0) * grad_scale
    grad_w_in, grad_kernel, grad_ln_gain = (
        lax.psum_scatter(in_term, "seq", scatter_dimension=0, tiled=True),
        lax.psum_scatter(kernel_term, "seq", scatter_dimension=1, tiled=True),
        lax.psum_scatter(gain_term, "seq", scatter_dimension=0, tiled=True),
    )
    grad_hat = grad_ln * gains
    grad_input = rstd_ln * (
        grad_hat
        - jnp.mean(grad_hat, axis=1, keepdims=True)
        - ln_hat * jnp.mean(grad_hat * ln_hat, axis=1, keepdims=True)
    )
    grad_frames = (out_grad.astype(jnp.float32) + grad_input).astype(jnp.bfloat16)
    return (
        outputs,
        grad_frames,
        grad_w_in,
        grad_w_out,
        grad_kernel,
        grad_ln_gain,
        grad_bn_gain,
        grad_bn_bias,
    )


def channel_local(frames, segment_ids, out_grad, ln_gain, w_in, dw_kernel, bn_gain, bn_bias, w_out):
    rows = frames.shape[0]
    width = frames.shape[1]
    taps = dw_kernel.shape[0]
    margin = taps // 2
    devices = lax.axis_size("seq")
    stream = rows * devices
    grad_scale = 1.0 / math.sqrt(stream)
    share = width // devices

    def spread(block):
        copies = jnp.broadcast_to(block[None], (devices,) + block.shape)
        return lax.all_to_all(copies, "seq", 0, 0, tiled=True)

    small = spread(jnp.concatenate([ln_gain, segment_ids.astype(jnp.float32)]))
    gains = small[:, :share].reshape(width)
    all_ids = small[:, share:].reshape(stream).astype(jnp.int32)

    out_rows = w_out.shape[0]
    pieces = lax.all_gather(
        jnp.concatenate([frames, out_grad, w_out, w_in[:, :width], w_in[:, width:]], axis=0),
        "seq",
        axis=0,
    )
    frames_all = pieces[:, :rows].reshape(stream, width)
    grad_all = pieces[:, rows : 2 * rows].reshape(stream, width)
    w_out_all = pieces[:, 2 * rows : 2 * rows + out_rows].reshape(width, width)
    w_in_left = pieces[:, 2 * rows + out_rows : 2 * rows + 2 * out_rows].reshape(width, width)
    w_in_right = pieces[:, 2 * rows + 2 * out_rows :].reshape(width, width)

    first_channel = lax.axis_index("seq") * share
    w_in_cols = jnp.concatenate(
        [
            lax.dynamic_slice_in_dim(w_in_left, first_channel, share, 1),
            lax.dynamic_slice_in_dim(w_in_right, first_channel, share, 1),
        ],
        axis=1,
    )

    def norm(block):
        block_float = block.astype(jnp.float32)
        mean = jnp.mean(block_float, axis=1, keepdims=True)
        centred = block_float - mean
        rstd = lax.rsqrt(jnp.mean(centred * centred, axis=1, keepdims=True) + EPSILON)
        return centred * rstd, rstd

    ln_all, _ = norm(frames_all)
    ln_x_all = (ln_all * gains).astype(jnp.bfloat16)

    hidden = jnp.dot(ln_x_all, w_in_cols, preferred_element_type=jnp.float32)
    left_half = hidden[:, :share]
    right_gate = jax.nn.sigmoid(hidden[:, share:])
    glu = (left_half * right_gate).astype(jnp.bfloat16)

    own_ids = all_ids + 1
    padded_ids = jnp.pad(own_ids, margin)
    masks = [
        (padded_ids[tap_index : tap_index + stream] == own_ids).astype(jnp.float32)[:, None]
        for tap_index in range(taps)
    ]
    padded_glu = jnp.pad(glu, ((margin, margin), (0, 0)))
    conv_out = jnp.zeros((stream, share), jnp.float32)
    for tap_index in range(taps):
        conv_out = (
            conv_out
            + dw_kernel[tap_index]
            * padded_glu[tap_index : tap_index + stream].astype(jnp.float32)
            * masks[tap_index]
        )
    bn_mean = jnp.sum(conv_out, axis=0) / stream
    bn_var = jnp.sum((conv_out - bn_mean) ** 2, axis=0) / stream
    bn_rstd = lax.rsqrt(bn_var + EPSILON)
    bn_hat = (conv_out - bn_mean) * bn_rstd
    zed = bn_hat * bn_gain + bn_bias
    zed_gate = jax.nn.sigmoid(zed)
    activation = (zed * zed_gate).astype(jnp.bfloat16)


    grad_w_out = (
        jnp.einsum("fa,fb->ab", activation, grad_all, preferred_element_type=jnp.float32)
        * grad_scale
    )
    grad_act = jnp.einsum("fe,ne->fn", grad_all, w_out, preferred_element_type=jnp.float32)
    grad_zed = grad_act * zed_gate * (1.0 + zed * (1.0 - zed_gate))
    bias_total = jnp.sum(grad_zed, axis=0)
    gain_total = jnp.sum(grad_zed * bn_hat, axis=0)
    grad_conv = bn_gain * bn_rstd * (grad_zed - bias_total / stream - bn_hat * gain_total / stream)
    grad_kernel = (
        jnp.stack(
            [
                jnp.sum(
                    grad_conv
                    * padded_glu[tap_index : tap_index + stream].astype(jnp.float32)
                    * masks[tap_index],
                    axis=0,
                )
                for tap_index in range(taps)
            ]
        )
        * grad_scale
    )
    padded_conv = jnp.pad(grad_conv, ((margin, margin), (0, 0)))
    grad_glu = jnp.zeros((stream, share), jnp.float32)
    for tap_index in range(taps):
        mirror = 2 * margin - tap_index
        grad_glu = (
            grad_glu
            + dw_kernel[tap_index] * padded_conv[mirror : mirror + stream] * masks[mirror]
        )
    grad_hidden = jnp.concatenate(
        [grad_glu * right_gate, grad_glu * left_half * right_gate * (1.0 - right_gate)], axis=1
    ).astype(jnp.bfloat16)

    in_cols = (
        jnp.einsum("fa,fb->ab", ln_x_all, grad_hidden, preferred_element_type=jnp.float32)
        * grad_scale
    )
    moments = jnp.einsum(
        "fa,fb->ab",
        ln_all,
        grad_hidden.astype(jnp.float32),
        preferred_element_type=jnp.float32,
        precision=lax.Precision.HIGHEST,
    )
    gain_part = jnp.sum(w_in_cols.astype(jnp.float32) * moments, axis=1) * grad_scale
    packed = lax.all_to_all(
        jnp.concatenate(
            [in_cols.reshape(devices, share * 2 * share), gain_part.reshape(devices, share)],
            axis=1,
        ),
        "seq", 0, 0, tiled=True,
    )
    grad_w_in = (
        packed[:, : share * 2 * share]
        .reshape(devices, share, 2, share)
        .transpose(1, 2, 0, 3)
        .reshape(share, 2 * width)
    )
    grad_ln_gain = jnp.sum(packed[:, share * 2 * share :], axis=0)
    back = lax.all_to_all(
        jnp.concatenate([activation, grad_hidden], axis=1).reshape(devices, rows, 3 * share),
        "seq", 0, 0, tiled=True,
    )
    act_rows = back[:, :, :share].transpose(1, 0, 2).reshape(rows, width)
    hidden_rows = (
        back[:, :, share:].reshape(devices, rows, 2, share).transpose(1, 2, 0, 3)
        .reshape(rows, 2, width)
    )
    projected = jnp.dot(act_rows, w_out_all, preferred_element_type=jnp.float32)
    outputs = (frames.astype(jnp.float32) + projected).astype(jnp.bfloat16)
    grad_ln = jnp.einsum(
        "fe,ne->fn", hidden_rows[:, 0], w_in_left, preferred_element_type=jnp.float32
    ) + jnp.einsum("fe,ne->fn", hidden_rows[:, 1], w_in_right, preferred_element_type=jnp.float32)
    ln_hat, rstd_ln = norm(frames)
    grad_hat = grad_ln * gains
    grad_input = rstd_ln * (
        grad_hat
        - jnp.mean(grad_hat, axis=1, keepdims=True)
        - ln_hat * jnp.mean(grad_hat * ln_hat, axis=1, keepdims=True)
    )
    grad_frames = (out_grad.astype(jnp.float32) + grad_input).astype(jnp.bfloat16)
    return (
        outputs,
        grad_frames,
        grad_w_in,
        grad_w_out,
        grad_kernel,
        grad_ln_gain,
        gain_total * grad_scale,
        bias_total * grad_scale,
    )


def solution(mesh):
    devices = mesh.shape["seq"]
    body = channel_local if devices <= 16 else local
    return jax.shard_map(
        body,
        mesh=mesh,
        in_specs=(
            P(("mix", "seq"), None),
            P(("mix", "seq")),
            P(("mix", "seq"), None),
            P(("mix", "seq")),
            P(("mix", "seq"), None),
            P("mix", "seq"),
            P(("mix", "seq")),
            P(("mix", "seq")),
            P(("mix", "seq"), None),
        ),
        out_specs=(
            P(("mix", "seq"), None),
            P(("mix", "seq"), None),
            P(("mix", "seq"), None),
            P(("mix", "seq"), None),
            P("mix", "seq"),
            P(("mix", "seq")),
            P(("mix", "seq")),
            P(("mix", "seq")),
        ),
        check_vma=False,
    )
```

```python
import math

import jax
import jax.numpy as jnp
from jax import lax
from jax.sharding import PartitionSpec as P

EPSILON = 1e-05


def with_halo(cells, sides, width):
    for axis, dim in sides:
        count = lax.axis_size(axis)
        ends = count - 1
        head = lax.slice_in_dim(cells, 0, width, axis=dim)
        tail = lax.slice_in_dim(cells, cells.shape[dim] - width, cells.shape[dim], axis=dim)
        cells = jnp.concatenate(
            [
                lax.ppermute(tail, axis, [(i, (i + 1) % count) for i in range(ends)]),
                cells,
                lax.ppermute(head, axis, [((i + 1) % count, i) for i in range(ends)]),
            ],
            axis=dim,
        )
    return cells


def local(frames, segment_ids, out_grad, ln_gain, w_in, dw_kernel, bn_gain, bn_bias, w_out):
    frame_count = frames.shape[0]
    width = frames.shape[1]
    taps = dw_kernel.shape[0]
    margin = taps // 2
    devices = lax.axis_size("seq")
    stream = frame_count * devices
    grad_scale = 1.0 / math.sqrt(stream)
    share = width // devices
    gains, kernel, bn_scale, bn_shift = (
        lax.all_gather(ln_gain, "seq", axis=0, tiled=True),
        lax.all_gather(dw_kernel, "seq", axis=1, tiled=True),
        lax.all_gather(bn_gain, "seq", axis=0, tiled=True),
        lax.all_gather(bn_bias, "seq", axis=0, tiled=True),
    )
    own_ids = segment_ids + 1
    padded_ids = with_halo(own_ids, (("seq", 0),), margin)
    masks = [
        (padded_ids[tap_index : tap_index + frame_count] == own_ids).astype(jnp.float32)[:, None]
        for tap_index in range(taps)
    ]
    frames_float = frames.astype(jnp.float32)
    mean_ln = jnp.mean(frames_float, axis=1, keepdims=True)
    centred = frames_float - mean_ln
    rstd_ln = lax.rsqrt(jnp.mean(centred * centred, axis=1, keepdims=True) + EPSILON)
    ln_hat = centred * rstd_ln
    ln_x = (ln_hat * gains).astype(jnp.bfloat16)
    columns = ln_x
    hidden = jnp.dot(
        columns, lax.all_gather(w_in, "seq", axis=0, tiled=True), preferred_element_type=jnp.float32
    )
    left_half = hidden[:, :width]
    right_gate = jax.nn.sigmoid(hidden[:, width:])
    glu = (left_half * right_gate).astype(jnp.bfloat16)
    padded_glu = with_halo(glu, (("seq", 0),), margin)
    conv_out = jnp.zeros((frame_count, width), jnp.float32)
    for tap_index in range(taps):
        conv_out = (
            conv_out
            + kernel[tap_index]
            * padded_glu[tap_index : tap_index + frame_count].astype(jnp.float32)
            * masks[tap_index]
        )
    plain_sums, square_sums = lax.psum(
        (jnp.sum(conv_out, axis=0), jnp.sum(conv_out * conv_out, axis=0)), "seq"
    )
    bn_mean = plain_sums / stream
    bn_var = square_sums / stream - bn_mean * bn_mean
    bn_rstd = lax.rsqrt(bn_var + EPSILON)
    bn_hat = (conv_out - bn_mean) * bn_rstd
    zed = bn_hat * bn_scale + bn_shift
    zed_gate = jax.nn.sigmoid(zed)
    activation = (zed * zed_gate).astype(jnp.bfloat16)
    columns = activation
    projected = jnp.dot(
        columns,
        lax.all_gather(w_out, "seq", axis=0, tiled=True),
        preferred_element_type=jnp.float32,
    )
    outputs = (frames_float + projected).astype(jnp.bfloat16)
    grad_w_out = lax.psum_scatter(
        jnp.einsum("fa,fb->ab", activation, out_grad, preferred_element_type=jnp.float32)
        * grad_scale,
        "seq",
        scatter_dimension=0,
        tiled=True,
    )
    grad_act = jnp.einsum(
        "fe,ne->fn",
        out_grad,
        lax.all_gather(w_out, "seq", axis=0, tiled=True),
        preferred_element_type=jnp.float32,
    )
    grad_zed = grad_act * zed_gate * (1.0 + zed * (1.0 - zed_gate))
    bias_total, gain_total = lax.psum(
        (jnp.sum(grad_zed, axis=0), jnp.sum(grad_zed * bn_hat, axis=0)), "seq"
    )
    grad_conv = bn_scale * bn_rstd * (grad_zed - bias_total / stream - bn_hat * gain_total / stream)
    first_channel = lax.axis_index("seq") * share
    grad_bn_bias = lax.dynamic_slice_in_dim(bias_total, first_channel, share, 0) * grad_scale
    grad_bn_gain = lax.dynamic_slice_in_dim(gain_total, first_channel, share, 0) * grad_scale
    kernel_rows = [
        jnp.sum(
            grad_conv
            * padded_glu[tap_index : tap_index + frame_count].astype(jnp.float32)
            * masks[tap_index],
            axis=0,
        )
        for tap_index in range(taps)
    ]
    kernel_term = jnp.stack(kernel_rows) * grad_scale
    padded_conv = with_halo(grad_conv, (("seq", 0),), margin)
    grad_glu = jnp.zeros((frame_count, width), jnp.float32)
    for tap_index in range(taps):
        mirror = 2 * margin - tap_index
        grad_glu = (
            grad_glu
            + kernel[tap_index] * padded_conv[mirror : mirror + frame_count] * masks[mirror]
        )
    grad_hidden = jnp.concatenate(
        [grad_glu * right_gate, grad_glu * left_half * right_gate * (1.0 - right_gate)], axis=1
    ).astype(jnp.bfloat16)
    grad_ln = jnp.einsum(
        "fe,ne->fn",
        grad_hidden,
        lax.all_gather(w_in, "seq", axis=0, tiled=True),
        preferred_element_type=jnp.float32,
    )
    in_term = (
        jnp.einsum("fa,fb->ab", ln_x, grad_hidden, preferred_element_type=jnp.float32) * grad_scale
    )
    gain_term = jnp.sum(grad_ln * ln_hat, axis=0) * grad_scale
    grad_w_in, grad_kernel, grad_ln_gain = (
        lax.psum_scatter(in_term, "seq", scatter_dimension=0, tiled=True),
        lax.psum_scatter(kernel_term, "seq", scatter_dimension=1, tiled=True),
        lax.psum_scatter(gain_term, "seq", scatter_dimension=0, tiled=True),
    )
    grad_hat = grad_ln * gains
    grad_input = rstd_ln * (
        grad_hat
        - jnp.mean(grad_hat, axis=1, keepdims=True)
        - ln_hat * jnp.mean(grad_hat * ln_hat, axis=1, keepdims=True)
    )
    grad_frames = (out_grad.astype(jnp.float32) + grad_input).astype(jnp.bfloat16)
    return (
        outputs,
        grad_frames,
        grad_w_in,
        grad_w_out,
        grad_kernel,
        grad_ln_gain,
        grad_bn_gain,
        grad_bn_bias,
    )


def channel_local(frames, segment_ids, out_grad, ln_gain, w_in, dw_kernel, bn_gain, bn_bias, w_out):
    rows = frames.shape[0]
    width = frames.shape[1]
    taps = dw_kernel.shape[0]
    margin = taps // 2
    devices = lax.axis_size("seq")
    stream = rows * devices
    grad_scale = 1.0 / math.sqrt(stream)
    share = width // devices

    def spread(block):
        copies = jnp.broadcast_to(block[None], (devices,) + block.shape)
        return lax.all_to_all(copies, "seq", 0, 0, tiled=True)

    small = spread(jnp.concatenate([ln_gain, segment_ids.astype(jnp.float32)]))
    gains = small[:, :share].reshape(width)
    all_ids = small[:, share:].reshape(stream).astype(jnp.int32)

    out_rows = w_out.shape[0]
    pieces = lax.all_gather(
        jnp.concatenate([frames, out_grad, w_out, w_in[:, :width], w_in[:, width:]], axis=0),
        "seq",
        axis=0,
    )
    frames_all = pieces[:, :rows].reshape(stream, width)
    grad_all = pieces[:, rows : 2 * rows].reshape(stream, width)
    w_out_all = pieces[:, 2 * rows : 2 * rows + out_rows].reshape(width, width)
    w_in_left = pieces[:, 2 * rows + out_rows : 2 * rows + 2 * out_rows].reshape(width, width)
    w_in_right = pieces[:, 2 * rows + 2 * out_rows :].reshape(width, width)

    first_channel = lax.axis_index("seq") * share
    w_in_cols = jnp.concatenate(
        [
            lax.dynamic_slice_in_dim(w_in_left, first_channel, share, 1),
            lax.dynamic_slice_in_dim(w_in_right, first_channel, share, 1),
        ],
        axis=1,
    )

    def norm(block):
        block_float = block.astype(jnp.float32)
        mean = jnp.mean(block_float, axis=1, keepdims=True)
        centred = block_float - mean
        rstd = lax.rsqrt(jnp.mean(centred * centred, axis=1, keepdims=True) + EPSILON)
        return centred * rstd, rstd

    ln_all, _ = norm(frames_all)
    ln_x_all = (ln_all * gains).astype(jnp.bfloat16)

    hidden = jnp.dot(ln_x_all, w_in_cols, preferred_element_type=jnp.float32)
    left_half = hidden[:, :share]
    right_gate = jax.nn.sigmoid(hidden[:, share:])
    glu = (left_half * right_gate).astype(jnp.bfloat16)

    own_ids = all_ids + 1
    padded_ids = jnp.pad(own_ids, margin)
    masks = [
        (padded_ids[tap_index : tap_index + stream] == own_ids).astype(jnp.float32)[:, None]
        for tap_index in range(taps)
    ]
    padded_glu = jnp.pad(glu, ((margin, margin), (0, 0)))
    conv_out = jnp.zeros((stream, share), jnp.float32)
    for tap_index in range(taps):
        conv_out = (
            conv_out
            + dw_kernel[tap_index]
            * padded_glu[tap_index : tap_index + stream].astype(jnp.float32)
            * masks[tap_index]
        )
    bn_mean = jnp.sum(conv_out, axis=0) / stream
    bn_var = jnp.sum((conv_out - bn_mean) ** 2, axis=0) / stream
    bn_rstd = lax.rsqrt(bn_var + EPSILON)
    bn_hat = (conv_out - bn_mean) * bn_rstd
    zed = bn_hat * bn_gain + bn_bias
    zed_gate = jax.nn.sigmoid(zed)
    activation = (zed * zed_gate).astype(jnp.bfloat16)


    grad_w_out = (
        jnp.einsum("fa,fb->ab", activation, grad_all, preferred_element_type=jnp.float32)
        * grad_scale
    )
    grad_act = jnp.einsum("fe,ne->fn", grad_all, w_out, preferred_element_type=jnp.float32)
    grad_zed = grad_act * zed_gate * (1.0 + zed * (1.0 - zed_gate))
    bias_total = jnp.sum(grad_zed, axis=0)
    gain_total = jnp.sum(grad_zed * bn_hat, axis=0)
    grad_conv = bn_gain * bn_rstd * (grad_zed - bias_total / stream - bn_hat * gain_total / stream)
    grad_kernel = (
        jnp.stack(
            [
                jnp.sum(
                    grad_conv
                    * padded_glu[tap_index : tap_index + stream].astype(jnp.float32)
                    * masks[tap_index],
                    axis=0,
                )
                for tap_index in range(taps)
            ]
        )
        * grad_scale
    )
    padded_conv = jnp.pad(grad_conv, ((margin, margin), (0, 0)))
    grad_glu = jnp.zeros((stream, share), jnp.float32)
    for tap_index in range(taps):
        mirror = 2 * margin - tap_index
        grad_glu = (
            grad_glu
            + dw_kernel[tap_index] * padded_conv[mirror : mirror + stream] * masks[mirror]
        )
    grad_hidden = jnp.concatenate(
        [grad_glu * right_gate, grad_glu * left_half * right_gate * (1.0 - right_gate)], axis=1
    ).astype(jnp.bfloat16)

    in_cols = (
        jnp.einsum("fa,fb->ab", ln_x_all, grad_hidden, preferred_element_type=jnp.float32)
        * grad_scale
    )
    head = lax.reduce_precision(in_cols, exponent_bits=8, mantissa_bits=7)
    tail = in_cols - head
    w_rows = width // devices
    weight_part = jnp.concatenate(
        [
            head.astype(jnp.bfloat16).reshape(devices, w_rows, 2 * share),
            tail.astype(jnp.bfloat16).reshape(devices, w_rows, 2 * share),
        ],
        axis=1,
    )
    back = lax.all_to_all(
        jnp.concatenate(
            [
                jnp.concatenate([activation, grad_hidden], axis=1).reshape(devices, rows, 3 * share),
                weight_part,
            ],
            axis=2,
        ),
        "seq", 0, 0, tiled=True,
    )
    weight_back = back[:, : 2 * w_rows, 3 * share :].astype(jnp.float32)
    grad_w_in = (
        (weight_back[:, :w_rows] + weight_back[:, w_rows:])
        .reshape(devices, w_rows, 2, share)
        .transpose(1, 2, 0, 3)
        .reshape(w_rows, 2 * width)
    )
    back = back[:, :, : 3 * share]
    act_rows = back[:, :, :share].transpose(1, 0, 2).reshape(rows, width)
    hidden_rows = (
        back[:, :, share:].reshape(devices, rows, 2, share).transpose(1, 2, 0, 3)
        .reshape(rows, 2, width)
    )
    projected = jnp.dot(act_rows, w_out_all, preferred_element_type=jnp.float32)
    outputs = (frames.astype(jnp.float32) + projected).astype(jnp.bfloat16)
    grad_ln = jnp.einsum(
        "fe,ne->fn", hidden_rows[:, 0], w_in_left, preferred_element_type=jnp.float32
    ) + jnp.einsum("fe,ne->fn", hidden_rows[:, 1], w_in_right, preferred_element_type=jnp.float32)
    ln_hat, rstd_ln = norm(frames)
    gain_part = jnp.sum(grad_ln * ln_hat, axis=0) * grad_scale
    grad_ln_gain = jnp.sum(
        lax.all_to_all(gain_part.reshape(devices, share), "seq", 0, 0, tiled=True), axis=0
    )
    grad_hat = grad_ln * gains
    grad_input = rstd_ln * (
        grad_hat
        - jnp.mean(grad_hat, axis=1, keepdims=True)
        - ln_hat * jnp.mean(grad_hat * ln_hat, axis=1, keepdims=True)
    )
    grad_frames = (out_grad.astype(jnp.float32) + grad_input).astype(jnp.bfloat16)
    return (
        outputs,
        grad_frames,
        grad_w_in,
        grad_w_out,
        grad_kernel,
        grad_ln_gain,
        gain_total * grad_scale,
        bias_total * grad_scale,
    )


def solution(mesh):
    devices = mesh.shape["seq"]
    body = channel_local if devices <= 16 else local
    return jax.shard_map(
        body,
        mesh=mesh,
        in_specs=(
            P(("mix", "seq"), None),
            P(("mix", "seq")),
            P(("mix", "seq"), None),
            P(("mix", "seq")),
            P(("mix", "seq"), None),
            P("mix", "seq"),
            P(("mix", "seq")),
            P(("mix", "seq")),
            P(("mix", "seq"), None),
        ),
        out_specs=(
            P(("mix", "seq"), None),
            P(("mix", "seq"), None),
            P(("mix", "seq"), None),
            P(("mix", "seq"), None),
            P("mix", "seq"),
            P(("mix", "seq")),
            P(("mix", "seq")),
            P(("mix", "seq")),
        ),
        check_vma=False,
    )
```

```python
import math

import jax
import jax.numpy as jnp
from jax import lax
from jax.sharding import PartitionSpec as P

EPSILON = 1e-05


def with_halo(cells, sides, width):
    for axis, dim in sides:
        count = lax.axis_size(axis)
        ends = count - 1
        head = lax.slice_in_dim(cells, 0, width, axis=dim)
        tail = lax.slice_in_dim(cells, cells.shape[dim] - width, cells.shape[dim], axis=dim)
        cells = jnp.concatenate(
            [
                lax.ppermute(tail, axis, [(i, (i + 1) % count) for i in range(ends)]),
                cells,
                lax.ppermute(head, axis, [((i + 1) % count, i) for i in range(ends)]),
            ],
            axis=dim,
        )
    return cells


def local(frames, segment_ids, out_grad, ln_gain, w_in, dw_kernel, bn_gain, bn_bias, w_out):
    frame_count = frames.shape[0]
    width = frames.shape[1]
    taps = dw_kernel.shape[0]
    margin = taps // 2
    devices = lax.axis_size("seq")
    stream = frame_count * devices
    grad_scale = 1.0 / math.sqrt(stream)
    share = width // devices
    gains, kernel, bn_scale, bn_shift = (
        lax.all_gather(ln_gain, "seq", axis=0, tiled=True),
        lax.all_gather(dw_kernel, "seq", axis=1, tiled=True),
        lax.all_gather(bn_gain, "seq", axis=0, tiled=True),
        lax.all_gather(bn_bias, "seq", axis=0, tiled=True),
    )
    own_ids = segment_ids + 1
    padded_ids = with_halo(own_ids, (("seq", 0),), margin)
    masks = [
        (padded_ids[tap_index : tap_index + frame_count] == own_ids).astype(jnp.float32)[:, None]
        for tap_index in range(taps)
    ]
    frames_float = frames.astype(jnp.float32)
    mean_ln = jnp.mean(frames_float, axis=1, keepdims=True)
    centred = frames_float - mean_ln
    rstd_ln = lax.rsqrt(jnp.mean(centred * centred, axis=1, keepdims=True) + EPSILON)
    ln_hat = centred * rstd_ln
    ln_x = (ln_hat * gains).astype(jnp.bfloat16)
    columns = ln_x
    hidden = jnp.dot(
        columns, lax.all_gather(w_in, "seq", axis=0, tiled=True), preferred_element_type=jnp.float32
    )
    left_half = hidden[:, :width]
    right_gate = jax.nn.sigmoid(hidden[:, width:])
    glu = (left_half * right_gate).astype(jnp.bfloat16)
    padded_glu = with_halo(glu, (("seq", 0),), margin)
    conv_out = jnp.zeros((frame_count, width), jnp.float32)
    for tap_index in range(taps):
        conv_out = (
            conv_out
            + kernel[tap_index]
            * padded_glu[tap_index : tap_index + frame_count].astype(jnp.float32)
            * masks[tap_index]
        )
    plain_sums, square_sums = lax.psum(
        (jnp.sum(conv_out, axis=0), jnp.sum(conv_out * conv_out, axis=0)), "seq"
    )
    bn_mean = plain_sums / stream
    bn_var = square_sums / stream - bn_mean * bn_mean
    bn_rstd = lax.rsqrt(bn_var + EPSILON)
    bn_hat = (conv_out - bn_mean) * bn_rstd
    zed = bn_hat * bn_scale + bn_shift
    zed_gate = jax.nn.sigmoid(zed)
    activation = (zed * zed_gate).astype(jnp.bfloat16)
    columns = activation
    projected = jnp.dot(
        columns,
        lax.all_gather(w_out, "seq", axis=0, tiled=True),
        preferred_element_type=jnp.float32,
    )
    outputs = (frames_float + projected).astype(jnp.bfloat16)
    grad_w_out = lax.psum_scatter(
        jnp.einsum("fa,fb->ab", activation, out_grad, preferred_element_type=jnp.float32)
        * grad_scale,
        "seq",
        scatter_dimension=0,
        tiled=True,
    )
    grad_act = jnp.einsum(
        "fe,ne->fn",
        out_grad,
        lax.all_gather(w_out, "seq", axis=0, tiled=True),
        preferred_element_type=jnp.float32,
    )
    grad_zed = grad_act * zed_gate * (1.0 + zed * (1.0 - zed_gate))
    bias_total, gain_total = lax.psum(
        (jnp.sum(grad_zed, axis=0), jnp.sum(grad_zed * bn_hat, axis=0)), "seq"
    )
    grad_conv = bn_scale * bn_rstd * (grad_zed - bias_total / stream - bn_hat * gain_total / stream)
    first_channel = lax.axis_index("seq") * share
    grad_bn_bias = lax.dynamic_slice_in_dim(bias_total, first_channel, share, 0) * grad_scale
    grad_bn_gain = lax.dynamic_slice_in_dim(gain_total, first_channel, share, 0) * grad_scale
    kernel_rows = [
        jnp.sum(
            grad_conv
            * padded_glu[tap_index : tap_index + frame_count].astype(jnp.float32)
            * masks[tap_index],
            axis=0,
        )
        for tap_index in range(taps)
    ]
    kernel_term = jnp.stack(kernel_rows) * grad_scale
    padded_conv = with_halo(grad_conv, (("seq", 0),), margin)
    grad_glu = jnp.zeros((frame_count, width), jnp.float32)
    for tap_index in range(taps):
        mirror = 2 * margin - tap_index
        grad_glu = (
            grad_glu
            + kernel[tap_index] * padded_conv[mirror : mirror + frame_count] * masks[mirror]
        )
    grad_hidden = jnp.concatenate(
        [grad_glu * right_gate, grad_glu * left_half * right_gate * (1.0 - right_gate)], axis=1
    ).astype(jnp.bfloat16)
    grad_ln = jnp.einsum(
        "fe,ne->fn",
        grad_hidden,
        lax.all_gather(w_in, "seq", axis=0, tiled=True),
        preferred_element_type=jnp.float32,
    )
    in_term = (
        jnp.einsum("fa,fb->ab", ln_x, grad_hidden, preferred_element_type=jnp.float32) * grad_scale
    )
    gain_term = jnp.sum(grad_ln * ln_hat, axis=0) * grad_scale
    grad_w_in, grad_kernel, grad_ln_gain = (
        lax.psum_scatter(in_term, "seq", scatter_dimension=0, tiled=True),
        lax.psum_scatter(kernel_term, "seq", scatter_dimension=1, tiled=True),
        lax.psum_scatter(gain_term, "seq", scatter_dimension=0, tiled=True),
    )
    grad_hat = grad_ln * gains
    grad_input = rstd_ln * (
        grad_hat
        - jnp.mean(grad_hat, axis=1, keepdims=True)
        - ln_hat * jnp.mean(grad_hat * ln_hat, axis=1, keepdims=True)
    )
    grad_frames = (out_grad.astype(jnp.float32) + grad_input).astype(jnp.bfloat16)
    return (
        outputs,
        grad_frames,
        grad_w_in,
        grad_w_out,
        grad_kernel,
        grad_ln_gain,
        grad_bn_gain,
        grad_bn_bias,
    )


def channel_local(frames, segment_ids, out_grad, ln_gain, w_in, dw_kernel, bn_gain, bn_bias, w_out):
    rows = frames.shape[0]
    width = frames.shape[1]
    taps = dw_kernel.shape[0]
    margin = taps // 2
    devices = lax.axis_size("seq")
    stream = rows * devices
    grad_scale = 1.0 / math.sqrt(stream)
    share = width // devices

    def spread(block):
        copies = jnp.broadcast_to(block[None], (devices,) + block.shape)
        return lax.all_to_all(copies, "seq", 0, 0, tiled=True)

    small = spread(jnp.concatenate([ln_gain, segment_ids.astype(jnp.float32)]))
    gains = small[:, :share].reshape(width)
    all_ids = small[:, share:].reshape(stream).astype(jnp.int32)

    out_rows = w_out.shape[0]
    pieces = lax.all_gather(
        jnp.concatenate([frames, out_grad, w_out], axis=0), "seq", axis=0
    )
    frames_all = pieces[:, :rows].reshape(stream, width)
    grad_all = pieces[:, rows : 2 * rows].reshape(stream, width)
    w_out_all = pieces[:, 2 * rows :].reshape(width, width)
    w_in_late, _ = lax.optimization_barrier((w_in, pieces))
    w_in_halves = lax.all_gather(
        jnp.concatenate([w_in_late[:, :width], w_in_late[:, width:]], axis=0), "seq", axis=0
    )
    w_in_left = w_in_halves[:, :out_rows].reshape(width, width)
    w_in_right = w_in_halves[:, out_rows:].reshape(width, width)

    first_channel = lax.axis_index("seq") * share
    w_in_cols = lax.all_to_all(
        w_in.reshape(share, 2, devices, share).transpose(2, 0, 1, 3), "seq", 0, 0, tiled=True
    ).reshape(width, 2 * share)

    def norm(block):
        block_float = block.astype(jnp.float32)
        mean = jnp.mean(block_float, axis=1, keepdims=True)
        centred = block_float - mean
        rstd = lax.rsqrt(jnp.mean(centred * centred, axis=1, keepdims=True) + EPSILON)
        return centred * rstd, rstd

    ln_all, _ = norm(frames_all)
    ln_x_all = (ln_all * gains).astype(jnp.bfloat16)

    hidden = jnp.dot(ln_x_all, w_in_cols, preferred_element_type=jnp.float32)
    left_half = hidden[:, :share]
    right_gate = jax.nn.sigmoid(hidden[:, share:])
    glu = (left_half * right_gate).astype(jnp.bfloat16)

    own_ids = all_ids + 1
    padded_ids = jnp.pad(own_ids, margin)
    masks = [
        (padded_ids[tap_index : tap_index + stream] == own_ids).astype(jnp.float32)[:, None]
        for tap_index in range(taps)
    ]
    padded_glu = jnp.pad(glu, ((margin, margin), (0, 0)))
    conv_out = jnp.zeros((stream, share), jnp.float32)
    for tap_index in range(taps):
        conv_out = (
            conv_out
            + dw_kernel[tap_index]
            * padded_glu[tap_index : tap_index + stream].astype(jnp.float32)
            * masks[tap_index]
        )
    bn_mean = jnp.sum(conv_out, axis=0) / stream
    bn_var = jnp.sum((conv_out - bn_mean) ** 2, axis=0) / stream
    bn_rstd = lax.rsqrt(bn_var + EPSILON)
    bn_hat = (conv_out - bn_mean) * bn_rstd
    zed = bn_hat * bn_gain + bn_bias
    zed_gate = jax.nn.sigmoid(zed)
    activation = (zed * zed_gate).astype(jnp.bfloat16)


    grad_w_out = (
        jnp.einsum("fa,fb->ab", activation, grad_all, preferred_element_type=jnp.float32)
        * grad_scale
    )
    grad_act = jnp.einsum("fe,ne->fn", grad_all, w_out, preferred_element_type=jnp.float32)
    grad_zed = grad_act * zed_gate * (1.0 + zed * (1.0 - zed_gate))
    bias_total = jnp.sum(grad_zed, axis=0)
    gain_total = jnp.sum(grad_zed * bn_hat, axis=0)
    grad_conv = bn_gain * bn_rstd * (grad_zed - bias_total / stream - bn_hat * gain_total / stream)
    grad_kernel = (
        jnp.stack(
            [
                jnp.sum(
                    grad_conv
                    * padded_glu[tap_index : tap_index + stream].astype(jnp.float32)
                    * masks[tap_index],
                    axis=0,
                )
                for tap_index in range(taps)
            ]
        )
        * grad_scale
    )
    padded_conv = jnp.pad(grad_conv, ((margin, margin), (0, 0)))
    grad_glu = jnp.zeros((stream, share), jnp.float32)
    for tap_index in range(taps):
        mirror = 2 * margin - tap_index
        grad_glu = (
            grad_glu
            + dw_kernel[tap_index] * padded_conv[mirror : mirror + stream] * masks[mirror]
        )
    grad_hidden = jnp.concatenate(
        [grad_glu * right_gate, grad_glu * left_half * right_gate * (1.0 - right_gate)], axis=1
    ).astype(jnp.bfloat16)

    in_cols = (
        jnp.einsum("fa,fb->ab", ln_x_all, grad_hidden, preferred_element_type=jnp.float32)
        * grad_scale
    )
    back = lax.all_to_all(
        jnp.concatenate([activation, grad_hidden], axis=1).reshape(devices, rows, 3 * share),
        "seq", 0, 0, tiled=True,
    )
    act_rows = back[:, :, :share].transpose(1, 0, 2).reshape(rows, width)
    hidden_rows = (
        back[:, :, share:].reshape(devices, rows, 2, share).transpose(1, 2, 0, 3)
        .reshape(rows, 2, width)
    )
    projected = jnp.dot(act_rows, w_out_all, preferred_element_type=jnp.float32)
    outputs = (frames.astype(jnp.float32) + projected).astype(jnp.bfloat16)
    grad_ln = jnp.einsum(
        "fe,ne->fn", hidden_rows[:, 0], w_in_left, preferred_element_type=jnp.float32
    ) + jnp.einsum("fe,ne->fn", hidden_rows[:, 1], w_in_right, preferred_element_type=jnp.float32)
    ln_hat, rstd_ln = norm(frames)
    gain_part = jnp.sum(grad_ln * ln_hat, axis=0) * grad_scale
    packed = lax.all_to_all(
        jnp.concatenate(
            [in_cols.reshape(devices, share * 2 * share), gain_part.reshape(devices, share)],
            axis=1,
        ),
        "seq", 0, 0, tiled=True,
    )
    grad_w_in = (
        packed[:, : share * 2 * share]
        .reshape(devices, share, 2, share)
        .transpose(1, 2, 0, 3)
        .reshape(share, 2 * width)
    )
    grad_ln_gain = jnp.sum(packed[:, share * 2 * share :], axis=0)
    grad_hat = grad_ln * gains
    grad_input = rstd_ln * (
        grad_hat
        - jnp.mean(grad_hat, axis=1, keepdims=True)
        - ln_hat * jnp.mean(grad_hat * ln_hat, axis=1, keepdims=True)
    )
    grad_frames = (out_grad.astype(jnp.float32) + grad_input).astype(jnp.bfloat16)
    return (
        outputs,
        grad_frames,
        grad_w_in,
        grad_w_out,
        grad_kernel,
        grad_ln_gain,
        gain_total * grad_scale,
        bias_total * grad_scale,
    )


def solution(mesh):
    devices = mesh.shape["seq"]
    body = channel_local if devices <= 16 else local
    return jax.shard_map(
        body,
        mesh=mesh,
        in_specs=(
            P(("mix", "seq"), None),
            P(("mix", "seq")),
            P(("mix", "seq"), None),
            P(("mix", "seq")),
            P(("mix", "seq"), None),
            P("mix", "seq"),
            P(("mix", "seq")),
            P(("mix", "seq")),
            P(("mix", "seq"), None),
        ),
        out_specs=(
            P(("mix", "seq"), None),
            P(("mix", "seq"), None),
            P(("mix", "seq"), None),
            P(("mix", "seq"), None),
            P("mix", "seq"),
            P(("mix", "seq")),
            P(("mix", "seq")),
            P(("mix", "seq")),
        ),
        check_vma=False,
    )
```

```python
import math

import jax
import jax.numpy as jnp
from jax import lax
from jax.sharding import PartitionSpec as P

EPSILON = 1e-05


def with_halo(cells, sides, width):
    for axis, dim in sides:
        count = lax.axis_size(axis)
        ends = count - 1
        head = lax.slice_in_dim(cells, 0, width, axis=dim)
        tail = lax.slice_in_dim(cells, cells.shape[dim] - width, cells.shape[dim], axis=dim)
        cells = jnp.concatenate(
            [
                lax.ppermute(tail, axis, [(i, (i + 1) % count) for i in range(ends)]),
                cells,
                lax.ppermute(head, axis, [((i + 1) % count, i) for i in range(ends)]),
            ],
            axis=dim,
        )
    return cells


def local(frames, segment_ids, out_grad, ln_gain, w_in, dw_kernel, bn_gain, bn_bias, w_out):
    frame_count = frames.shape[0]
    width = frames.shape[1]
    taps = dw_kernel.shape[0]
    margin = taps // 2
    devices = lax.axis_size("seq")
    stream = frame_count * devices
    grad_scale = 1.0 / math.sqrt(stream)
    share = width // devices
    gains, kernel, bn_scale, bn_shift = (
        lax.all_gather(ln_gain, "seq", axis=0, tiled=True),
        lax.all_gather(dw_kernel, "seq", axis=1, tiled=True),
        lax.all_gather(bn_gain, "seq", axis=0, tiled=True),
        lax.all_gather(bn_bias, "seq", axis=0, tiled=True),
    )
    own_ids = segment_ids + 1
    padded_ids = with_halo(own_ids, (("seq", 0),), margin)
    masks = [
        (padded_ids[tap_index : tap_index + frame_count] == own_ids).astype(jnp.float32)[:, None]
        for tap_index in range(taps)
    ]
    frames_float = frames.astype(jnp.float32)
    mean_ln = jnp.mean(frames_float, axis=1, keepdims=True)
    centred = frames_float - mean_ln
    rstd_ln = lax.rsqrt(jnp.mean(centred * centred, axis=1, keepdims=True) + EPSILON)
    ln_hat = centred * rstd_ln
    ln_x = (ln_hat * gains).astype(jnp.bfloat16)
    columns = ln_x
    hidden = jnp.dot(
        columns, lax.all_gather(w_in, "seq", axis=0, tiled=True), preferred_element_type=jnp.float32
    )
    left_half = hidden[:, :width]
    right_gate = jax.nn.sigmoid(hidden[:, width:])
    glu = (left_half * right_gate).astype(jnp.bfloat16)
    padded_glu = with_halo(glu, (("seq", 0),), margin)
    conv_out = jnp.zeros((frame_count, width), jnp.float32)
    for tap_index in range(taps):
        conv_out = (
            conv_out
            + kernel[tap_index]
            * padded_glu[tap_index : tap_index + frame_count].astype(jnp.float32)
            * masks[tap_index]
        )
    plain_sums, square_sums = lax.psum(
        (jnp.sum(conv_out, axis=0), jnp.sum(conv_out * conv_out, axis=0)), "seq"
    )
    bn_mean = plain_sums / stream
    bn_var = square_sums / stream - bn_mean * bn_mean
    bn_rstd = lax.rsqrt(bn_var + EPSILON)
    bn_hat = (conv_out - bn_mean) * bn_rstd
    zed = bn_hat * bn_scale + bn_shift
    zed_gate = jax.nn.sigmoid(zed)
    activation = (zed * zed_gate).astype(jnp.bfloat16)
    columns = activation
    projected = jnp.dot(
        columns,
        lax.all_gather(w_out, "seq", axis=0, tiled=True),
        preferred_element_type=jnp.float32,
    )
    outputs = (frames_float + projected).astype(jnp.bfloat16)
    grad_w_out = lax.psum_scatter(
        jnp.einsum("fa,fb->ab", activation, out_grad, preferred_element_type=jnp.float32)
        * grad_scale,
        "seq",
        scatter_dimension=0,
        tiled=True,
    )
    grad_act = jnp.einsum(
        "fe,ne->fn",
        out_grad,
        lax.all_gather(w_out, "seq", axis=0, tiled=True),
        preferred_element_type=jnp.float32,
    )
    grad_zed = grad_act * zed_gate * (1.0 + zed * (1.0 - zed_gate))
    bias_total, gain_total = lax.psum(
        (jnp.sum(grad_zed, axis=0), jnp.sum(grad_zed * bn_hat, axis=0)), "seq"
    )
    grad_conv = bn_scale * bn_rstd * (grad_zed - bias_total / stream - bn_hat * gain_total / stream)
    first_channel = lax.axis_index("seq") * share
    grad_bn_bias = lax.dynamic_slice_in_dim(bias_total, first_channel, share, 0) * grad_scale
    grad_bn_gain = lax.dynamic_slice_in_dim(gain_total, first_channel, share, 0) * grad_scale
    kernel_rows = [
        jnp.sum(
            grad_conv
            * padded_glu[tap_index : tap_index + frame_count].astype(jnp.float32)
            * masks[tap_index],
            axis=0,
        )
        for tap_index in range(taps)
    ]
    kernel_term = jnp.stack(kernel_rows) * grad_scale
    padded_conv = with_halo(grad_conv, (("seq", 0),), margin)
    grad_glu = jnp.zeros((frame_count, width), jnp.float32)
    for tap_index in range(taps):
        mirror = 2 * margin - tap_index
        grad_glu = (
            grad_glu
            + kernel[tap_index] * padded_conv[mirror : mirror + frame_count] * masks[mirror]
        )
    grad_hidden = jnp.concatenate(
        [grad_glu * right_gate, grad_glu * left_half * right_gate * (1.0 - right_gate)], axis=1
    ).astype(jnp.bfloat16)
    grad_ln = jnp.einsum(
        "fe,ne->fn",
        grad_hidden,
        lax.all_gather(w_in, "seq", axis=0, tiled=True),
        preferred_element_type=jnp.float32,
    )
    in_term = (
        jnp.einsum("fa,fb->ab", ln_x, grad_hidden, preferred_element_type=jnp.float32) * grad_scale
    )
    gain_term = jnp.sum(grad_ln * ln_hat, axis=0) * grad_scale
    grad_w_in, grad_kernel, grad_ln_gain = (
        lax.psum_scatter(in_term, "seq", scatter_dimension=0, tiled=True),
        lax.psum_scatter(kernel_term, "seq", scatter_dimension=1, tiled=True),
        lax.psum_scatter(gain_term, "seq", scatter_dimension=0, tiled=True),
    )
    grad_hat = grad_ln * gains
    grad_input = rstd_ln * (
        grad_hat
        - jnp.mean(grad_hat, axis=1, keepdims=True)
        - ln_hat * jnp.mean(grad_hat * ln_hat, axis=1, keepdims=True)
    )
    grad_frames = (out_grad.astype(jnp.float32) + grad_input).astype(jnp.bfloat16)
    return (
        outputs,
        grad_frames,
        grad_w_in,
        grad_w_out,
        grad_kernel,
        grad_ln_gain,
        grad_bn_gain,
        grad_bn_bias,
    )


def channel_local(frames, segment_ids, out_grad, ln_gain, w_in, dw_kernel, bn_gain, bn_bias, w_out):
    rows = frames.shape[0]
    width = frames.shape[1]
    taps = dw_kernel.shape[0]
    margin = taps // 2
    devices = lax.axis_size("seq")
    stream = rows * devices
    grad_scale = 1.0 / math.sqrt(stream)
    share = width // devices

    def spread(block):
        copies = jnp.broadcast_to(block[None], (devices,) + block.shape)
        return lax.all_to_all(copies, "seq", 0, 0, tiled=True)

    small = spread(jnp.concatenate([ln_gain, segment_ids.astype(jnp.float32)]))
    gains = small[:, :share].reshape(width)
    all_ids = small[:, share:].reshape(stream).astype(jnp.int32)

    out_rows = w_out.shape[0]
    pieces = lax.all_gather(jnp.concatenate([frames, out_grad], axis=0), "seq", axis=0)
    frames_all = pieces[:, :rows].reshape(stream, width)
    grad_all = pieces[:, rows:].reshape(stream, width)
    w_in_cols = lax.all_to_all(
        w_in.reshape(share, 2, devices, share).transpose(2, 0, 1, 3), "seq", 0, 0, tiled=True
    ).reshape(width, 2 * share)
    w_in_late, w_out_late, _, _, _ = lax.optimization_barrier(
        (w_in, w_out, pieces, w_in_cols, small)
    )
    weights = lax.all_gather(
        jnp.concatenate([w_out_late, w_in_late[:, :width], w_in_late[:, width:]], axis=0),
        "seq",
        axis=0,
    )
    w_out_all = weights[:, :out_rows].reshape(width, width)
    w_in_left = weights[:, out_rows : 2 * out_rows].reshape(width, width)
    w_in_right = weights[:, 2 * out_rows :].reshape(width, width)

    first_channel = lax.axis_index("seq") * share

    def norm(block):
        block_float = block.astype(jnp.float32)
        mean = jnp.mean(block_float, axis=1, keepdims=True)
        centred = block_float - mean
        rstd = lax.rsqrt(jnp.mean(centred * centred, axis=1, keepdims=True) + EPSILON)
        return centred * rstd, rstd

    ln_all, _ = norm(frames_all)
    ln_x_all = (ln_all * gains).astype(jnp.bfloat16)

    hidden = jnp.dot(ln_x_all, w_in_cols, preferred_element_type=jnp.float32)
    left_half = hidden[:, :share]
    right_gate = jax.nn.sigmoid(hidden[:, share:])
    glu = (left_half * right_gate).astype(jnp.bfloat16)

    own_ids = all_ids + 1
    padded_ids = jnp.pad(own_ids, margin)
    masks = [
        (padded_ids[tap_index : tap_index + stream] == own_ids).astype(jnp.float32)[:, None]
        for tap_index in range(taps)
    ]
    padded_glu = jnp.pad(glu, ((margin, margin), (0, 0)))
    conv_out = jnp.zeros((stream, share), jnp.float32)
    for tap_index in range(taps):
        conv_out = (
            conv_out
            + dw_kernel[tap_index]
            * padded_glu[tap_index : tap_index + stream].astype(jnp.float32)
            * masks[tap_index]
        )
    bn_mean = jnp.sum(conv_out, axis=0) / stream
    bn_var = jnp.sum((conv_out - bn_mean) ** 2, axis=0) / stream
    bn_rstd = lax.rsqrt(bn_var + EPSILON)
    bn_hat = (conv_out - bn_mean) * bn_rstd
    zed = bn_hat * bn_gain + bn_bias
    zed_gate = jax.nn.sigmoid(zed)
    activation = (zed * zed_gate).astype(jnp.bfloat16)


    grad_w_out = (
        jnp.einsum("fa,fb->ab", activation, grad_all, preferred_element_type=jnp.float32)
        * grad_scale
    )
    grad_act = jnp.einsum("fe,ne->fn", grad_all, w_out, preferred_element_type=jnp.float32)
    grad_zed = grad_act * zed_gate * (1.0 + zed * (1.0 - zed_gate))
    bias_total = jnp.sum(grad_zed, axis=0)
    gain_total = jnp.sum(grad_zed * bn_hat, axis=0)
    grad_conv = bn_gain * bn_rstd * (grad_zed - bias_total / stream - bn_hat * gain_total / stream)
    grad_kernel = (
        jnp.stack(
            [
                jnp.sum(
                    grad_conv
                    * padded_glu[tap_index : tap_index + stream].astype(jnp.float32)
                    * masks[tap_index],
                    axis=0,
                )
                for tap_index in range(taps)
            ]
        )
        * grad_scale
    )
    padded_conv = jnp.pad(grad_conv, ((margin, margin), (0, 0)))
    grad_glu = jnp.zeros((stream, share), jnp.float32)
    for tap_index in range(taps):
        mirror = 2 * margin - tap_index
        grad_glu = (
            grad_glu
            + dw_kernel[tap_index] * padded_conv[mirror : mirror + stream] * masks[mirror]
        )
    grad_hidden = jnp.concatenate(
        [grad_glu * right_gate, grad_glu * left_half * right_gate * (1.0 - right_gate)], axis=1
    ).astype(jnp.bfloat16)

    in_cols = (
        jnp.einsum("fa,fb->ab", ln_x_all, grad_hidden, preferred_element_type=jnp.float32)
        * grad_scale
    )
    back = lax.all_to_all(
        jnp.concatenate([activation, grad_hidden], axis=1).reshape(devices, rows, 3 * share),
        "seq", 0, 0, tiled=True,
    )
    act_rows = back[:, :, :share].transpose(1, 0, 2).reshape(rows, width)
    hidden_rows = (
        back[:, :, share:].reshape(devices, rows, 2, share).transpose(1, 2, 0, 3)
        .reshape(rows, 2, width)
    )
    projected = jnp.dot(act_rows, w_out_all, preferred_element_type=jnp.float32)
    outputs = (frames.astype(jnp.float32) + projected).astype(jnp.bfloat16)
    grad_ln = jnp.einsum(
        "fe,ne->fn", hidden_rows[:, 0], w_in_left, preferred_element_type=jnp.float32
    ) + jnp.einsum("fe,ne->fn", hidden_rows[:, 1], w_in_right, preferred_element_type=jnp.float32)
    ln_hat, rstd_ln = norm(frames)
    gain_part = jnp.sum(grad_ln * ln_hat, axis=0) * grad_scale
    packed = lax.all_to_all(
        jnp.concatenate(
            [in_cols.reshape(devices, share * 2 * share), gain_part.reshape(devices, share)],
            axis=1,
        ),
        "seq", 0, 0, tiled=True,
    )
    grad_w_in = (
        packed[:, : share * 2 * share]
        .reshape(devices, share, 2, share)
        .transpose(1, 2, 0, 3)
        .reshape(share, 2 * width)
    )
    grad_ln_gain = jnp.sum(packed[:, share * 2 * share :], axis=0)
    grad_hat = grad_ln * gains
    grad_input = rstd_ln * (
        grad_hat
        - jnp.mean(grad_hat, axis=1, keepdims=True)
        - ln_hat * jnp.mean(grad_hat * ln_hat, axis=1, keepdims=True)
    )
    grad_frames = (out_grad.astype(jnp.float32) + grad_input).astype(jnp.bfloat16)
    return (
        outputs,
        grad_frames,
        grad_w_in,
        grad_w_out,
        grad_kernel,
        grad_ln_gain,
        gain_total * grad_scale,
        bias_total * grad_scale,
    )


def solution(mesh):
    devices = mesh.shape["seq"]
    body = channel_local if devices <= 16 else local
    return jax.shard_map(
        body,
        mesh=mesh,
        in_specs=(
            P(("mix", "seq"), None),
            P(("mix", "seq")),
            P(("mix", "seq"), None),
            P(("mix", "seq")),
            P(("mix", "seq"), None),
            P("mix", "seq"),
            P(("mix", "seq")),
            P(("mix", "seq")),
            P(("mix", "seq"), None),
        ),
        out_specs=(
            P(("mix", "seq"), None),
            P(("mix", "seq"), None),
            P(("mix", "seq"), None),
            P(("mix", "seq"), None),
            P("mix", "seq"),
            P(("mix", "seq")),
            P(("mix", "seq")),
            P(("mix", "seq")),
        ),
        check_vma=False,
    )
```

```python
import math

import jax
import jax.numpy as jnp
from jax import lax
from jax.sharding import PartitionSpec as P

EPSILON = 1e-05


def with_halo(cells, sides, width):
    for axis, dim in sides:
        count = lax.axis_size(axis)
        ends = count - 1
        head = lax.slice_in_dim(cells, 0, width, axis=dim)
        tail = lax.slice_in_dim(cells, cells.shape[dim] - width, cells.shape[dim], axis=dim)
        cells = jnp.concatenate(
            [
                lax.ppermute(tail, axis, [(i, (i + 1) % count) for i in range(ends)]),
                cells,
                lax.ppermute(head, axis, [((i + 1) % count, i) for i in range(ends)]),
            ],
            axis=dim,
        )
    return cells


def local(frames, segment_ids, out_grad, ln_gain, w_in, dw_kernel, bn_gain, bn_bias, w_out):
    frame_count = frames.shape[0]
    width = frames.shape[1]
    taps = dw_kernel.shape[0]
    margin = taps // 2
    devices = lax.axis_size("seq")
    stream = frame_count * devices
    grad_scale = 1.0 / math.sqrt(stream)
    share = width // devices
    gains, kernel, bn_scale, bn_shift = (
        lax.all_gather(ln_gain, "seq", axis=0, tiled=True),
        lax.all_gather(dw_kernel, "seq", axis=1, tiled=True),
        lax.all_gather(bn_gain, "seq", axis=0, tiled=True),
        lax.all_gather(bn_bias, "seq", axis=0, tiled=True),
    )
    own_ids = segment_ids + 1
    padded_ids = with_halo(own_ids, (("seq", 0),), margin)
    masks = [
        (padded_ids[tap_index : tap_index + frame_count] == own_ids).astype(jnp.float32)[:, None]
        for tap_index in range(taps)
    ]
    frames_float = frames.astype(jnp.float32)
    mean_ln = jnp.mean(frames_float, axis=1, keepdims=True)
    centred = frames_float - mean_ln
    rstd_ln = lax.rsqrt(jnp.mean(centred * centred, axis=1, keepdims=True) + EPSILON)
    ln_hat = centred * rstd_ln
    ln_x = (ln_hat * gains).astype(jnp.bfloat16)
    columns = ln_x
    hidden = jnp.dot(
        columns, lax.all_gather(w_in, "seq", axis=0, tiled=True), preferred_element_type=jnp.float32
    )
    left_half = hidden[:, :width]
    right_gate = jax.nn.sigmoid(hidden[:, width:])
    glu = (left_half * right_gate).astype(jnp.bfloat16)
    padded_glu = with_halo(glu, (("seq", 0),), margin)
    conv_out = jnp.zeros((frame_count, width), jnp.float32)
    for tap_index in range(taps):
        conv_out = (
            conv_out
            + kernel[tap_index]
            * padded_glu[tap_index : tap_index + frame_count].astype(jnp.float32)
            * masks[tap_index]
        )
    plain_sums, square_sums = lax.psum(
        (jnp.sum(conv_out, axis=0), jnp.sum(conv_out * conv_out, axis=0)), "seq"
    )
    bn_mean = plain_sums / stream
    bn_var = square_sums / stream - bn_mean * bn_mean
    bn_rstd = lax.rsqrt(bn_var + EPSILON)
    bn_hat = (conv_out - bn_mean) * bn_rstd
    zed = bn_hat * bn_scale + bn_shift
    zed_gate = jax.nn.sigmoid(zed)
    activation = (zed * zed_gate).astype(jnp.bfloat16)
    columns = activation
    projected = jnp.dot(
        columns,
        lax.all_gather(w_out, "seq", axis=0, tiled=True),
        preferred_element_type=jnp.float32,
    )
    outputs = (frames_float + projected).astype(jnp.bfloat16)
    grad_w_out = lax.psum_scatter(
        jnp.einsum("fa,fb->ab", activation, out_grad, preferred_element_type=jnp.float32)
        * grad_scale,
        "seq",
        scatter_dimension=0,
        tiled=True,
    )
    grad_act = jnp.einsum(
        "fe,ne->fn",
        out_grad,
        lax.all_gather(w_out, "seq", axis=0, tiled=True),
        preferred_element_type=jnp.float32,
    )
    grad_zed = grad_act * zed_gate * (1.0 + zed * (1.0 - zed_gate))
    bias_total, gain_total = lax.psum(
        (jnp.sum(grad_zed, axis=0), jnp.sum(grad_zed * bn_hat, axis=0)), "seq"
    )
    grad_conv = bn_scale * bn_rstd * (grad_zed - bias_total / stream - bn_hat * gain_total / stream)
    first_channel = lax.axis_index("seq") * share
    grad_bn_bias = lax.dynamic_slice_in_dim(bias_total, first_channel, share, 0) * grad_scale
    grad_bn_gain = lax.dynamic_slice_in_dim(gain_total, first_channel, share, 0) * grad_scale
    kernel_rows = [
        jnp.sum(
            grad_conv
            * padded_glu[tap_index : tap_index + frame_count].astype(jnp.float32)
            * masks[tap_index],
            axis=0,
        )
        for tap_index in range(taps)
    ]
    kernel_term = jnp.stack(kernel_rows) * grad_scale
    padded_conv = with_halo(grad_conv, (("seq", 0),), margin)
    grad_glu = jnp.zeros((frame_count, width), jnp.float32)
    for tap_index in range(taps):
        mirror = 2 * margin - tap_index
        grad_glu = (
            grad_glu
            + kernel[tap_index] * padded_conv[mirror : mirror + frame_count] * masks[mirror]
        )
    grad_hidden = jnp.concatenate(
        [grad_glu * right_gate, grad_glu * left_half * right_gate * (1.0 - right_gate)], axis=1
    ).astype(jnp.bfloat16)
    grad_ln = jnp.einsum(
        "fe,ne->fn",
        grad_hidden,
        lax.all_gather(w_in, "seq", axis=0, tiled=True),
        preferred_element_type=jnp.float32,
    )
    in_term = (
        jnp.einsum("fa,fb->ab", ln_x, grad_hidden, preferred_element_type=jnp.float32) * grad_scale
    )
    gain_term = jnp.sum(grad_ln * ln_hat, axis=0) * grad_scale
    grad_w_in, grad_kernel, grad_ln_gain = (
        lax.psum_scatter(in_term, "seq", scatter_dimension=0, tiled=True),
        lax.psum_scatter(kernel_term, "seq", scatter_dimension=1, tiled=True),
        lax.psum_scatter(gain_term, "seq", scatter_dimension=0, tiled=True),
    )
    grad_hat = grad_ln * gains
    grad_input = rstd_ln * (
        grad_hat
        - jnp.mean(grad_hat, axis=1, keepdims=True)
        - ln_hat * jnp.mean(grad_hat * ln_hat, axis=1, keepdims=True)
    )
    grad_frames = (out_grad.astype(jnp.float32) + grad_input).astype(jnp.bfloat16)
    return (
        outputs,
        grad_frames,
        grad_w_in,
        grad_w_out,
        grad_kernel,
        grad_ln_gain,
        grad_bn_gain,
        grad_bn_bias,
    )


def channel_local(frames, segment_ids, out_grad, ln_gain, w_in, dw_kernel, bn_gain, bn_bias, w_out):
    rows = frames.shape[0]
    width = frames.shape[1]
    taps = dw_kernel.shape[0]
    margin = taps // 2
    devices = lax.axis_size("seq")
    stream = rows * devices
    grad_scale = 1.0 / math.sqrt(stream)
    share = width // devices

    def spread(block):
        copies = jnp.broadcast_to(block[None], (devices,) + block.shape)
        return lax.all_to_all(copies, "seq", 0, 0, tiled=True)

    small = spread(jnp.concatenate([ln_gain, segment_ids.astype(jnp.float32)]))
    gains = small[:, :share].reshape(width)
    all_ids = small[:, share:].reshape(stream).astype(jnp.int32)

    out_rows = w_out.shape[0]
    pieces = lax.all_gather(jnp.concatenate([frames, out_grad], axis=0), "seq", axis=0)
    frames_all = pieces[:, :rows].reshape(stream, width)
    grad_all = pieces[:, rows:].reshape(stream, width)
    w_in_cols = lax.all_to_all(
        w_in.reshape(share, 2, devices, share).transpose(2, 0, 1, 3), "seq", 0, 0, tiled=True
    ).reshape(width, 2 * share)
    w_in_late, w_out_late, _, _, _ = lax.optimization_barrier(
        (w_in, w_out, pieces, w_in_cols, small)
    )
    weights = lax.all_gather(
        jnp.concatenate([w_out_late, w_in_late[:, :width], w_in_late[:, width:]], axis=0),
        "seq",
        axis=0,
    )
    w_out_all = weights[:, :out_rows].reshape(width, width)
    w_in_left = weights[:, out_rows : 2 * out_rows].reshape(width, width)
    w_in_right = weights[:, 2 * out_rows :].reshape(width, width)

    first_channel = lax.axis_index("seq") * share

    def norm(block):
        block_float = block.astype(jnp.float32)
        mean = jnp.mean(block_float, axis=1, keepdims=True)
        centred = block_float - mean
        rstd = lax.rsqrt(jnp.mean(centred * centred, axis=1, keepdims=True) + EPSILON)
        return centred * rstd, rstd

    ln_all, _ = norm(frames_all)
    ln_x_all = (ln_all * gains).astype(jnp.bfloat16)

    hidden = jnp.dot(ln_x_all, w_in_cols, preferred_element_type=jnp.float32)
    left_half = hidden[:, :share]
    right_gate = jax.nn.sigmoid(hidden[:, share:])
    glu = (left_half * right_gate).astype(jnp.bfloat16)

    own_ids = all_ids + 1
    padded_ids = jnp.pad(own_ids, margin)
    masks = [
        (padded_ids[tap_index : tap_index + stream] == own_ids).astype(jnp.float32)[:, None]
        for tap_index in range(taps)
    ]
    padded_glu = jnp.pad(glu, ((margin, margin), (0, 0)))
    conv_out = jnp.zeros((stream, share), jnp.float32)
    for tap_index in range(taps):
        conv_out = (
            conv_out
            + dw_kernel[tap_index]
            * padded_glu[tap_index : tap_index + stream].astype(jnp.float32)
            * masks[tap_index]
        )
    bn_mean = jnp.sum(conv_out, axis=0) / stream
    bn_var = jnp.sum((conv_out - bn_mean) ** 2, axis=0) / stream
    bn_rstd = lax.rsqrt(bn_var + EPSILON)
    bn_hat = (conv_out - bn_mean) * bn_rstd
    zed = bn_hat * bn_gain + bn_bias
    zed_gate = jax.nn.sigmoid(zed)
    activation = (zed * zed_gate).astype(jnp.bfloat16)


    grad_w_out = (
        jnp.einsum("fa,fb->ab", activation, grad_all, preferred_element_type=jnp.float32)
        * grad_scale
    )
    grad_act = jnp.einsum("fe,ne->fn", grad_all, w_out, preferred_element_type=jnp.float32)
    grad_zed = grad_act * zed_gate * (1.0 + zed * (1.0 - zed_gate))
    bias_total = jnp.sum(grad_zed, axis=0)
    gain_total = jnp.sum(grad_zed * bn_hat, axis=0)
    grad_conv = bn_gain * bn_rstd * (grad_zed - bias_total / stream - bn_hat * gain_total / stream)
    grad_kernel = (
        jnp.stack(
            [
                jnp.sum(
                    grad_conv
                    * padded_glu[tap_index : tap_index + stream].astype(jnp.float32)
                    * masks[tap_index],
                    axis=0,
                )
                for tap_index in range(taps)
            ]
        )
        * grad_scale
    )
    padded_conv = jnp.pad(grad_conv, ((margin, margin), (0, 0)))
    grad_glu = jnp.zeros((stream, share), jnp.float32)
    for tap_index in range(taps):
        mirror = 2 * margin - tap_index
        grad_glu = (
            grad_glu
            + dw_kernel[tap_index] * padded_conv[mirror : mirror + stream] * masks[mirror]
        )
    grad_hidden = jnp.concatenate(
        [grad_glu * right_gate, grad_glu * left_half * right_gate * (1.0 - right_gate)], axis=1
    ).astype(jnp.bfloat16)

    in_cols = (
        jnp.einsum("fa,fb->ab", ln_x_all, grad_hidden, preferred_element_type=jnp.float32)
        * grad_scale
    )
    grad_w_in = (
        lax.all_to_all(in_cols.reshape(devices, share, 2, share), "seq", 0, 0, tiled=True)
        .transpose(1, 2, 0, 3)
        .reshape(share, 2 * width)
    )
    back = lax.all_to_all(
        jnp.concatenate([activation, grad_hidden], axis=1).reshape(devices, rows, 3 * share),
        "seq", 0, 0, tiled=True,
    )
    act_rows = back[:, :, :share].transpose(1, 0, 2).reshape(rows, width)
    hidden_rows = (
        back[:, :, share:].reshape(devices, rows, 2, share).transpose(1, 2, 0, 3)
        .reshape(rows, 2, width)
    )
    projected = jnp.dot(act_rows, w_out_all, preferred_element_type=jnp.float32)
    outputs = (frames.astype(jnp.float32) + projected).astype(jnp.bfloat16)
    grad_ln = jnp.einsum(
        "fe,ne->fn", hidden_rows[:, 0], w_in_left, preferred_element_type=jnp.float32
    ) + jnp.einsum("fe,ne->fn", hidden_rows[:, 1], w_in_right, preferred_element_type=jnp.float32)
    ln_hat, rstd_ln = norm(frames)
    gain_part = jnp.sum(grad_ln * ln_hat, axis=0) * grad_scale
    grad_ln_gain = jnp.sum(
        lax.all_to_all(gain_part.reshape(devices, share), "seq", 0, 0, tiled=True), axis=0
    )
    grad_hat = grad_ln * gains
    grad_input = rstd_ln * (
        grad_hat
        - jnp.mean(grad_hat, axis=1, keepdims=True)
        - ln_hat * jnp.mean(grad_hat * ln_hat, axis=1, keepdims=True)
    )
    grad_frames = (out_grad.astype(jnp.float32) + grad_input).astype(jnp.bfloat16)
    return (
        outputs,
        grad_frames,
        grad_w_in,
        grad_w_out,
        grad_kernel,
        grad_ln_gain,
        gain_total * grad_scale,
        bias_total * grad_scale,
    )


def solution(mesh):
    devices = mesh.shape["seq"]
    body = channel_local if devices <= 16 else local
    return jax.shard_map(
        body,
        mesh=mesh,
        in_specs=(
            P(("mix", "seq"), None),
            P(("mix", "seq")),
            P(("mix", "seq"), None),
            P(("mix", "seq")),
            P(("mix", "seq"), None),
            P("mix", "seq"),
            P(("mix", "seq")),
            P(("mix", "seq")),
            P(("mix", "seq"), None),
        ),
        out_specs=(
            P(("mix", "seq"), None),
            P(("mix", "seq"), None),
            P(("mix", "seq"), None),
            P(("mix", "seq"), None),
            P("mix", "seq"),
            P(("mix", "seq")),
            P(("mix", "seq")),
            P(("mix", "seq")),
        ),
        check_vma=False,
    )
```

```python
import math

import jax
import jax.numpy as jnp
from jax import lax
from jax.sharding import PartitionSpec as P

EPSILON = 1e-05


def with_halo(cells, sides, width):
    for axis, dim in sides:
        count = lax.axis_size(axis)
        ends = count - 1
        head = lax.slice_in_dim(cells, 0, width, axis=dim)
        tail = lax.slice_in_dim(cells, cells.shape[dim] - width, cells.shape[dim], axis=dim)
        cells = jnp.concatenate(
            [
                lax.ppermute(tail, axis, [(i, (i + 1) % count) for i in range(ends)]),
                cells,
                lax.ppermute(head, axis, [((i + 1) % count, i) for i in range(ends)]),
            ],
            axis=dim,
        )
    return cells


def local(frames, segment_ids, out_grad, ln_gain, w_in, dw_kernel, bn_gain, bn_bias, w_out):
    frame_count = frames.shape[0]
    width = frames.shape[1]
    taps = dw_kernel.shape[0]
    margin = taps // 2
    devices = lax.axis_size("seq")
    stream = frame_count * devices
    grad_scale = 1.0 / math.sqrt(stream)
    share = width // devices
    gains, kernel, bn_scale, bn_shift = (
        lax.all_gather(ln_gain, "seq", axis=0, tiled=True),
        lax.all_gather(dw_kernel, "seq", axis=1, tiled=True),
        lax.all_gather(bn_gain, "seq", axis=0, tiled=True),
        lax.all_gather(bn_bias, "seq", axis=0, tiled=True),
    )
    own_ids = segment_ids + 1
    padded_ids = with_halo(own_ids, (("seq", 0),), margin)
    masks = [
        (padded_ids[tap_index : tap_index + frame_count] == own_ids).astype(jnp.float32)[:, None]
        for tap_index in range(taps)
    ]
    frames_float = frames.astype(jnp.float32)
    mean_ln = jnp.mean(frames_float, axis=1, keepdims=True)
    centred = frames_float - mean_ln
    rstd_ln = lax.rsqrt(jnp.mean(centred * centred, axis=1, keepdims=True) + EPSILON)
    ln_hat = centred * rstd_ln
    ln_x = (ln_hat * gains).astype(jnp.bfloat16)
    columns = ln_x
    hidden = jnp.dot(
        columns, lax.all_gather(w_in, "seq", axis=0, tiled=True), preferred_element_type=jnp.float32
    )
    left_half = hidden[:, :width]
    right_gate = jax.nn.sigmoid(hidden[:, width:])
    glu = (left_half * right_gate).astype(jnp.bfloat16)
    padded_glu = with_halo(glu, (("seq", 0),), margin)
    conv_out = jnp.zeros((frame_count, width), jnp.float32)
    for tap_index in range(taps):
        conv_out = (
            conv_out
            + kernel[tap_index]
            * padded_glu[tap_index : tap_index + frame_count].astype(jnp.float32)
            * masks[tap_index]
        )
    plain_sums, square_sums = lax.psum(
        (jnp.sum(conv_out, axis=0), jnp.sum(conv_out * conv_out, axis=0)), "seq"
    )
    bn_mean = plain_sums / stream
    bn_var = square_sums / stream - bn_mean * bn_mean
    bn_rstd = lax.rsqrt(bn_var + EPSILON)
    bn_hat = (conv_out - bn_mean) * bn_rstd
    zed = bn_hat * bn_scale + bn_shift
    zed_gate = jax.nn.sigmoid(zed)
    activation = (zed * zed_gate).astype(jnp.bfloat16)
    columns = activation
    projected = jnp.dot(
        columns,
        lax.all_gather(w_out, "seq", axis=0, tiled=True),
        preferred_element_type=jnp.float32,
    )
    outputs = (frames_float + projected).astype(jnp.bfloat16)
    grad_w_out = lax.psum_scatter(
        jnp.einsum("fa,fb->ab", activation, out_grad, preferred_element_type=jnp.float32)
        * grad_scale,
        "seq",
        scatter_dimension=0,
        tiled=True,
    )
    grad_act = jnp.einsum(
        "fe,ne->fn",
        out_grad,
        lax.all_gather(w_out, "seq", axis=0, tiled=True),
        preferred_element_type=jnp.float32,
    )
    grad_zed = grad_act * zed_gate * (1.0 + zed * (1.0 - zed_gate))
    bias_total, gain_total = lax.psum(
        (jnp.sum(grad_zed, axis=0), jnp.sum(grad_zed * bn_hat, axis=0)), "seq"
    )
    grad_conv = bn_scale * bn_rstd * (grad_zed - bias_total / stream - bn_hat * gain_total / stream)
    first_channel = lax.axis_index("seq") * share
    grad_bn_bias = lax.dynamic_slice_in_dim(bias_total, first_channel, share, 0) * grad_scale
    grad_bn_gain = lax.dynamic_slice_in_dim(gain_total, first_channel, share, 0) * grad_scale
    kernel_rows = [
        jnp.sum(
            grad_conv
            * padded_glu[tap_index : tap_index + frame_count].astype(jnp.float32)
            * masks[tap_index],
            axis=0,
        )
        for tap_index in range(taps)
    ]
    kernel_term = jnp.stack(kernel_rows) * grad_scale
    padded_conv = with_halo(grad_conv, (("seq", 0),), margin)
    grad_glu = jnp.zeros((frame_count, width), jnp.float32)
    for tap_index in range(taps):
        mirror = 2 * margin - tap_index
        grad_glu = (
            grad_glu
            + kernel[tap_index] * padded_conv[mirror : mirror + frame_count] * masks[mirror]
        )
    grad_hidden = jnp.concatenate(
        [grad_glu * right_gate, grad_glu * left_half * right_gate * (1.0 - right_gate)], axis=1
    ).astype(jnp.bfloat16)
    grad_ln = jnp.einsum(
        "fe,ne->fn",
        grad_hidden,
        lax.all_gather(w_in, "seq", axis=0, tiled=True),
        preferred_element_type=jnp.float32,
    )
    in_term = (
        jnp.einsum("fa,fb->ab", ln_x, grad_hidden, preferred_element_type=jnp.float32) * grad_scale
    )
    gain_term = jnp.sum(grad_ln * ln_hat, axis=0) * grad_scale
    grad_w_in, grad_kernel, grad_ln_gain = (
        lax.psum_scatter(in_term, "seq", scatter_dimension=0, tiled=True),
        lax.psum_scatter(kernel_term, "seq", scatter_dimension=1, tiled=True),
        lax.psum_scatter(gain_term, "seq", scatter_dimension=0, tiled=True),
    )
    grad_hat = grad_ln * gains
    grad_input = rstd_ln * (
        grad_hat
        - jnp.mean(grad_hat, axis=1, keepdims=True)
        - ln_hat * jnp.mean(grad_hat * ln_hat, axis=1, keepdims=True)
    )
    grad_frames = (out_grad.astype(jnp.float32) + grad_input).astype(jnp.bfloat16)
    return (
        outputs,
        grad_frames,
        grad_w_in,
        grad_w_out,
        grad_kernel,
        grad_ln_gain,
        grad_bn_gain,
        grad_bn_bias,
    )


def channel_local(frames, segment_ids, out_grad, ln_gain, w_in, dw_kernel, bn_gain, bn_bias, w_out):
    rows = frames.shape[0]
    width = frames.shape[1]
    taps = dw_kernel.shape[0]
    margin = taps // 2
    devices = lax.axis_size("seq")
    stream = rows * devices
    grad_scale = 1.0 / math.sqrt(stream)
    share = width // devices

    def spread(block):
        copies = jnp.broadcast_to(block[None], (devices,) + block.shape)
        return lax.all_to_all(copies, "seq", 0, 0, tiled=True)

    small = spread(jnp.concatenate([ln_gain, segment_ids.astype(jnp.float32)]))
    gains = small[:, :share].reshape(width)
    all_ids = small[:, share:].reshape(stream).astype(jnp.int32)

    out_rows = w_out.shape[0]
    pieces = lax.all_gather(jnp.concatenate([frames, out_grad], axis=0), "seq", axis=0)
    frames_all = pieces[:, :rows].reshape(stream, width)
    grad_all = pieces[:, rows:].reshape(stream, width)
    w_in_cols = lax.all_to_all(
        w_in.reshape(share, 2, devices, share).transpose(2, 0, 1, 3), "seq", 0, 0, tiled=True
    ).reshape(width, 2 * share)
    w_in_late, w_out_late, _, _, _ = lax.optimization_barrier(
        (w_in, w_out, pieces, w_in_cols, small)
    )
    weights = lax.all_gather(
        jnp.concatenate([w_out_late, w_in_late[:, :width], w_in_late[:, width:]], axis=0),
        "seq",
        axis=0,
    )
    w_out_all = weights[:, :out_rows].reshape(width, width)
    w_in_left = weights[:, out_rows : 2 * out_rows].reshape(width, width)
    w_in_right = weights[:, 2 * out_rows :].reshape(width, width)

    first_channel = lax.axis_index("seq") * share

    def norm(block):
        block_float = block.astype(jnp.float32)
        mean = jnp.mean(block_float, axis=1, keepdims=True)
        centred = block_float - mean
        rstd = lax.rsqrt(jnp.mean(centred * centred, axis=1, keepdims=True) + EPSILON)
        return centred * rstd, rstd

    ln_all, _ = norm(frames_all)
    ln_x_all = (ln_all * gains).astype(jnp.bfloat16)

    hidden = jnp.dot(ln_x_all, w_in_cols, preferred_element_type=jnp.float32)
    left_half = hidden[:, :share]
    right_gate = jax.nn.sigmoid(hidden[:, share:])
    glu = (left_half * right_gate).astype(jnp.bfloat16)

    own_ids = all_ids + 1
    padded_ids = jnp.pad(own_ids, margin)
    masks = [
        (padded_ids[tap_index : tap_index + stream] == own_ids).astype(jnp.float32)[:, None]
        for tap_index in range(taps)
    ]
    padded_glu = jnp.pad(glu, ((margin, margin), (0, 0)))
    conv_out = jnp.zeros((stream, share), jnp.float32)
    for tap_index in range(taps):
        conv_out = (
            conv_out
            + dw_kernel[tap_index]
            * padded_glu[tap_index : tap_index + stream].astype(jnp.float32)
            * masks[tap_index]
        )
    bn_mean = jnp.sum(conv_out, axis=0) / stream
    bn_var = jnp.sum((conv_out - bn_mean) ** 2, axis=0) / stream
    bn_rstd = lax.rsqrt(bn_var + EPSILON)
    bn_hat = (conv_out - bn_mean) * bn_rstd
    zed = bn_hat * bn_gain + bn_bias
    zed_gate = jax.nn.sigmoid(zed)
    activation = (zed * zed_gate).astype(jnp.bfloat16)


    grad_w_out = (
        jnp.einsum("fa,fb->ab", activation, grad_all, preferred_element_type=jnp.float32)
        * grad_scale
    )
    grad_act = jnp.einsum("fe,ne->fn", grad_all, w_out, preferred_element_type=jnp.float32)
    grad_zed = grad_act * zed_gate * (1.0 + zed * (1.0 - zed_gate))
    bias_total = jnp.sum(grad_zed, axis=0)
    gain_total = jnp.sum(grad_zed * bn_hat, axis=0)
    grad_conv = bn_gain * bn_rstd * (grad_zed - bias_total / stream - bn_hat * gain_total / stream)
    grad_kernel = (
        jnp.stack(
            [
                jnp.sum(
                    grad_conv
                    * padded_glu[tap_index : tap_index + stream].astype(jnp.float32)
                    * masks[tap_index],
                    axis=0,
                )
                for tap_index in range(taps)
            ]
        )
        * grad_scale
    )
    padded_conv = jnp.pad(grad_conv, ((margin, margin), (0, 0)))
    grad_glu = jnp.zeros((stream, share), jnp.float32)
    for tap_index in range(taps):
        mirror = 2 * margin - tap_index
        grad_glu = (
            grad_glu
            + dw_kernel[tap_index] * padded_conv[mirror : mirror + stream] * masks[mirror]
        )
    grad_hidden = jnp.concatenate(
        [grad_glu * right_gate, grad_glu * left_half * right_gate * (1.0 - right_gate)], axis=1
    ).astype(jnp.bfloat16)

    in_cols = (
        jnp.einsum("fa,fb->ab", ln_x_all, grad_hidden, preferred_element_type=jnp.float32)
        * grad_scale
    )
    moments = jnp.einsum(
        "fa,fb->ab",
        ln_all,
        grad_hidden.astype(jnp.float32),
        preferred_element_type=jnp.float32,
        precision=lax.Precision.HIGHEST,
    )
    gain_part = jnp.sum(w_in_cols.astype(jnp.float32) * moments, axis=1) * grad_scale
    packed = lax.all_to_all(
        jnp.concatenate(
            [in_cols.reshape(devices, share * 2 * share), gain_part.reshape(devices, share)],
            axis=1,
        ),
        "seq", 0, 0, tiled=True,
    )
    grad_w_in = (
        packed[:, : share * 2 * share]
        .reshape(devices, share, 2, share)
        .transpose(1, 2, 0, 3)
        .reshape(share, 2 * width)
    )
    grad_ln_gain = jnp.sum(packed[:, share * 2 * share :], axis=0)
    back = lax.all_to_all(
        jnp.concatenate([activation, grad_hidden], axis=1).reshape(devices, rows, 3 * share),
        "seq", 0, 0, tiled=True,
    )
    act_rows = back[:, :, :share].transpose(1, 0, 2).reshape(rows, width)
    hidden_rows = (
        back[:, :, share:].reshape(devices, rows, 2, share).transpose(1, 2, 0, 3)
        .reshape(rows, 2, width)
    )
    projected = jnp.dot(act_rows, w_out_all, preferred_element_type=jnp.float32)
    outputs = (frames.astype(jnp.float32) + projected).astype(jnp.bfloat16)
    grad_ln = jnp.einsum(
        "fe,ne->fn", hidden_rows[:, 0], w_in_left, preferred_element_type=jnp.float32
    ) + jnp.einsum("fe,ne->fn", hidden_rows[:, 1], w_in_right, preferred_element_type=jnp.float32)
    ln_hat, rstd_ln = norm(frames)
    grad_hat = grad_ln * gains
    grad_input = rstd_ln * (
        grad_hat
        - jnp.mean(grad_hat, axis=1, keepdims=True)
        - ln_hat * jnp.mean(grad_hat * ln_hat, axis=1, keepdims=True)
    )
    grad_frames = (out_grad.astype(jnp.float32) + grad_input).astype(jnp.bfloat16)
    return (
        outputs,
        grad_frames,
        grad_w_in,
        grad_w_out,
        grad_kernel,
        grad_ln_gain,
        gain_total * grad_scale,
        bias_total * grad_scale,
    )


def solution(mesh):
    devices = mesh.shape["seq"]
    body = channel_local if devices <= 16 else local
    return jax.shard_map(
        body,
        mesh=mesh,
        in_specs=(
            P(("mix", "seq"), None),
            P(("mix", "seq")),
            P(("mix", "seq"), None),
            P(("mix", "seq")),
            P(("mix", "seq"), None),
            P("mix", "seq"),
            P(("mix", "seq")),
            P(("mix", "seq")),
            P(("mix", "seq"), None),
        ),
        out_specs=(
            P(("mix", "seq"), None),
            P(("mix", "seq"), None),
            P(("mix", "seq"), None),
            P(("mix", "seq"), None),
            P("mix", "seq"),
            P(("mix", "seq")),
            P(("mix", "seq")),
            P(("mix", "seq")),
        ),
        check_vma=False,
    )
```

```python
import math

import jax
import jax.numpy as jnp
from jax import lax
from jax.sharding import PartitionSpec as P

EPSILON = 1e-05


def with_halo(cells, sides, width):
    for axis, dim in sides:
        count = lax.axis_size(axis)
        ends = count - 1
        head = lax.slice_in_dim(cells, 0, width, axis=dim)
        tail = lax.slice_in_dim(cells, cells.shape[dim] - width, cells.shape[dim], axis=dim)
        cells = jnp.concatenate(
            [
                lax.ppermute(tail, axis, [(i, (i + 1) % count) for i in range(ends)]),
                cells,
                lax.ppermute(head, axis, [((i + 1) % count, i) for i in range(ends)]),
            ],
            axis=dim,
        )
    return cells


def local(frames, segment_ids, out_grad, ln_gain, w_in, dw_kernel, bn_gain, bn_bias, w_out):
    frame_count = frames.shape[0]
    width = frames.shape[1]
    taps = dw_kernel.shape[0]
    margin = taps // 2
    devices = lax.axis_size("seq")
    stream = frame_count * devices
    grad_scale = 1.0 / math.sqrt(stream)
    share = width // devices
    gains, kernel, bn_scale, bn_shift = (
        lax.all_gather(ln_gain, "seq", axis=0, tiled=True),
        lax.all_gather(dw_kernel, "seq", axis=1, tiled=True),
        lax.all_gather(bn_gain, "seq", axis=0, tiled=True),
        lax.all_gather(bn_bias, "seq", axis=0, tiled=True),
    )
    own_ids = segment_ids + 1
    padded_ids = with_halo(own_ids, (("seq", 0),), margin)
    masks = [
        (padded_ids[tap_index : tap_index + frame_count] == own_ids).astype(jnp.float32)[:, None]
        for tap_index in range(taps)
    ]
    frames_float = frames.astype(jnp.float32)
    mean_ln = jnp.mean(frames_float, axis=1, keepdims=True)
    centred = frames_float - mean_ln
    rstd_ln = lax.rsqrt(jnp.mean(centred * centred, axis=1, keepdims=True) + EPSILON)
    ln_hat = centred * rstd_ln
    ln_x = (ln_hat * gains).astype(jnp.bfloat16)
    columns = ln_x
    hidden = jnp.dot(
        columns, lax.all_gather(w_in, "seq", axis=0, tiled=True), preferred_element_type=jnp.float32
    )
    left_half = hidden[:, :width]
    right_gate = jax.nn.sigmoid(hidden[:, width:])
    glu = (left_half * right_gate).astype(jnp.bfloat16)
    padded_glu = with_halo(glu, (("seq", 0),), margin)
    conv_out = jnp.zeros((frame_count, width), jnp.float32)
    for tap_index in range(taps):
        conv_out = (
            conv_out
            + kernel[tap_index]
            * padded_glu[tap_index : tap_index + frame_count].astype(jnp.float32)
            * masks[tap_index]
        )
    plain_sums, square_sums = lax.psum(
        (jnp.sum(conv_out, axis=0), jnp.sum(conv_out * conv_out, axis=0)), "seq"
    )
    bn_mean = plain_sums / stream
    bn_var = square_sums / stream - bn_mean * bn_mean
    bn_rstd = lax.rsqrt(bn_var + EPSILON)
    bn_hat = (conv_out - bn_mean) * bn_rstd
    zed = bn_hat * bn_scale + bn_shift
    zed_gate = jax.nn.sigmoid(zed)
    activation = (zed * zed_gate).astype(jnp.bfloat16)
    columns = activation
    projected = jnp.dot(
        columns,
        lax.all_gather(w_out, "seq", axis=0, tiled=True),
        preferred_element_type=jnp.float32,
    )
    outputs = (frames_float + projected).astype(jnp.bfloat16)
    grad_w_out = lax.psum_scatter(
        jnp.einsum("fa,fb->ab", activation, out_grad, preferred_element_type=jnp.float32)
        * grad_scale,
        "seq",
        scatter_dimension=0,
        tiled=True,
    )
    grad_act = jnp.einsum(
        "fe,ne->fn",
        out_grad,
        lax.all_gather(w_out, "seq", axis=0, tiled=True),
        preferred_element_type=jnp.float32,
    )
    grad_zed = grad_act * zed_gate * (1.0 + zed * (1.0 - zed_gate))
    bias_total, gain_total = lax.psum(
        (jnp.sum(grad_zed, axis=0), jnp.sum(grad_zed * bn_hat, axis=0)), "seq"
    )
    grad_conv = bn_scale * bn_rstd * (grad_zed - bias_total / stream - bn_hat * gain_total / stream)
    first_channel = lax.axis_index("seq") * share
    grad_bn_bias = lax.dynamic_slice_in_dim(bias_total, first_channel, share, 0) * grad_scale
    grad_bn_gain = lax.dynamic_slice_in_dim(gain_total, first_channel, share, 0) * grad_scale
    kernel_rows = [
        jnp.sum(
            grad_conv
            * padded_glu[tap_index : tap_index + frame_count].astype(jnp.float32)
            * masks[tap_index],
            axis=0,
        )
        for tap_index in range(taps)
    ]
    kernel_term = jnp.stack(kernel_rows) * grad_scale
    padded_conv = with_halo(grad_conv, (("seq", 0),), margin)
    grad_glu = jnp.zeros((frame_count, width), jnp.float32)
    for tap_index in range(taps):
        mirror = 2 * margin - tap_index
        grad_glu = (
            grad_glu
            + kernel[tap_index] * padded_conv[mirror : mirror + frame_count] * masks[mirror]
        )
    grad_hidden = jnp.concatenate(
        [grad_glu * right_gate, grad_glu * left_half * right_gate * (1.0 - right_gate)], axis=1
    ).astype(jnp.bfloat16)
    grad_ln = jnp.einsum(
        "fe,ne->fn",
        grad_hidden,
        lax.all_gather(w_in, "seq", axis=0, tiled=True),
        preferred_element_type=jnp.float32,
    )
    in_term = (
        jnp.einsum("fa,fb->ab", ln_x, grad_hidden, preferred_element_type=jnp.float32) * grad_scale
    )
    gain_term = jnp.sum(grad_ln * ln_hat, axis=0) * grad_scale
    grad_w_in, grad_kernel, grad_ln_gain = (
        lax.psum_scatter(in_term, "seq", scatter_dimension=0, tiled=True),
        lax.psum_scatter(kernel_term, "seq", scatter_dimension=1, tiled=True),
        lax.psum_scatter(gain_term, "seq", scatter_dimension=0, tiled=True),
    )
    grad_hat = grad_ln * gains
    grad_input = rstd_ln * (
        grad_hat
        - jnp.mean(grad_hat, axis=1, keepdims=True)
        - ln_hat * jnp.mean(grad_hat * ln_hat, axis=1, keepdims=True)
    )
    grad_frames = (out_grad.astype(jnp.float32) + grad_input).astype(jnp.bfloat16)
    return (
        outputs,
        grad_frames,
        grad_w_in,
        grad_w_out,
        grad_kernel,
        grad_ln_gain,
        grad_bn_gain,
        grad_bn_bias,
    )


def channel_local(frames, segment_ids, out_grad, ln_gain, w_in, dw_kernel, bn_gain, bn_bias, w_out):
    rows = frames.shape[0]
    width = frames.shape[1]
    taps = dw_kernel.shape[0]
    margin = taps // 2
    devices = lax.axis_size("seq")
    stream = rows * devices
    grad_scale = 1.0 / math.sqrt(stream)
    share = width // devices

    def spread(block):
        copies = jnp.broadcast_to(block[None], (devices,) + block.shape)
        return lax.all_to_all(copies, "seq", 0, 0, tiled=True)

    small = spread(jnp.concatenate([ln_gain, segment_ids.astype(jnp.float32)]))
    gains = small[:, :share].reshape(width)
    all_ids = small[:, share:].reshape(stream).astype(jnp.int32)

    out_rows = w_out.shape[0]
    pieces = lax.all_gather(jnp.concatenate([frames, out_grad], axis=0), "seq", axis=0)
    frames_all = pieces[:, :rows].reshape(stream, width)
    grad_all = pieces[:, rows:].reshape(stream, width)
    w_in_cols = lax.all_to_all(
        w_in.reshape(share, 2, devices, share).transpose(2, 0, 1, 3), "seq", 0, 0, tiled=True
    ).reshape(width, 2 * share)
    w_in_late, w_out_late, _, _, _ = lax.optimization_barrier(
        (w_in, w_out, pieces, w_in_cols, small)
    )
    weights = lax.all_gather(
        jnp.concatenate([w_out_late, w_in_late[:, :width], w_in_late[:, width:]], axis=0),
        "seq",
        axis=0,
    )
    w_out_all = weights[:, :out_rows].reshape(width, width)
    w_in_left = weights[:, out_rows : 2 * out_rows].reshape(width, width)
    w_in_right = weights[:, 2 * out_rows :].reshape(width, width)

    first_channel = lax.axis_index("seq") * share

    def norm(block):
        block_float = block.astype(jnp.float32)
        mean = jnp.mean(block_float, axis=1, keepdims=True)
        centred = block_float - mean
        rstd = lax.rsqrt(jnp.mean(centred * centred, axis=1, keepdims=True) + EPSILON)
        return centred * rstd, rstd

    ln_all, _ = norm(frames_all)
    ln_x_all = (ln_all * gains).astype(jnp.bfloat16)

    hidden = jnp.dot(ln_x_all, w_in_cols, preferred_element_type=jnp.float32)
    left_half = hidden[:, :share]
    right_gate = jax.nn.sigmoid(hidden[:, share:])
    glu = (left_half * right_gate).astype(jnp.bfloat16)

    own_ids = all_ids + 1
    padded_ids = jnp.pad(own_ids, margin)
    masks = [
        (padded_ids[tap_index : tap_index + stream] == own_ids).astype(jnp.float32)[:, None]
        for tap_index in range(taps)
    ]
    padded_glu = jnp.pad(glu, ((margin, margin), (0, 0)))
    conv_out = jnp.zeros((stream, share), jnp.float32)
    for tap_index in range(taps):
        conv_out = (
            conv_out
            + dw_kernel[tap_index]
            * padded_glu[tap_index : tap_index + stream].astype(jnp.float32)
            * masks[tap_index]
        )
    bn_mean = jnp.sum(conv_out, axis=0) / stream
    bn_var = jnp.sum((conv_out - bn_mean) ** 2, axis=0) / stream
    bn_rstd = lax.rsqrt(bn_var + EPSILON)
    bn_hat = (conv_out - bn_mean) * bn_rstd
    zed = bn_hat * bn_gain + bn_bias
    zed_gate = jax.nn.sigmoid(zed)
    activation = (zed * zed_gate).astype(jnp.bfloat16)


    grad_w_out = (
        jnp.einsum("fa,fb->ab", activation, grad_all, preferred_element_type=jnp.float32)
        * grad_scale
    )
    grad_act = jnp.einsum("fe,ne->fn", grad_all, w_out, preferred_element_type=jnp.float32)
    grad_zed = grad_act * zed_gate * (1.0 + zed * (1.0 - zed_gate))
    bias_total = jnp.sum(grad_zed, axis=0)
    gain_total = jnp.sum(grad_zed * bn_hat, axis=0)
    grad_conv = bn_gain * bn_rstd * (grad_zed - bias_total / stream - bn_hat * gain_total / stream)
    grad_kernel = (
        jnp.stack(
            [
                jnp.sum(
                    grad_conv
                    * padded_glu[tap_index : tap_index + stream].astype(jnp.float32)
                    * masks[tap_index],
                    axis=0,
                )
                for tap_index in range(taps)
            ]
        )
        * grad_scale
    )
    padded_conv = jnp.pad(grad_conv, ((margin, margin), (0, 0)))
    grad_glu = jnp.zeros((stream, share), jnp.float32)
    for tap_index in range(taps):
        mirror = 2 * margin - tap_index
        grad_glu = (
            grad_glu
            + dw_kernel[tap_index] * padded_conv[mirror : mirror + stream] * masks[mirror]
        )
    grad_hidden = jnp.concatenate(
        [grad_glu * right_gate, grad_glu * left_half * right_gate * (1.0 - right_gate)], axis=1
    ).astype(jnp.bfloat16)

    in_cols = (
        jnp.einsum("fa,fb->ab", ln_x_all, grad_hidden, preferred_element_type=jnp.float32)
        * grad_scale
    )
    moments = jnp.einsum(
        "fa,fb->ab",
        ln_all,
        grad_hidden.astype(jnp.float32),
        preferred_element_type=jnp.float32,
        precision=lax.Precision.HIGHEST,
    )
    gain_part = jnp.sum(w_in_cols.astype(jnp.float32) * moments, axis=1) * grad_scale
    back = lax.all_to_all(
        jnp.concatenate([activation, grad_hidden], axis=1).reshape(devices, rows, 3 * share),
        "seq", 0, 0, tiled=True,
    )
    act_rows = back[:, :, :share].transpose(1, 0, 2).reshape(rows, width)
    payload, _ = lax.optimization_barrier(
        (
            jnp.concatenate(
                [in_cols.reshape(devices, share * 2 * share), gain_part.reshape(devices, share)],
                axis=1,
            ),
            back,
        )
    )
    packed = lax.all_to_all(payload, "seq", 0, 0, tiled=True)
    grad_w_in = (
        packed[:, : share * 2 * share]
        .reshape(devices, share, 2, share)
        .transpose(1, 2, 0, 3)
        .reshape(share, 2 * width)
    )
    grad_ln_gain = jnp.sum(packed[:, share * 2 * share :], axis=0)
    hidden_rows = (
        back[:, :, share:].reshape(devices, rows, 2, share).transpose(1, 2, 0, 3)
        .reshape(rows, 2, width)
    )
    projected = jnp.dot(act_rows, w_out_all, preferred_element_type=jnp.float32)
    outputs = (frames.astype(jnp.float32) + projected).astype(jnp.bfloat16)
    grad_ln = jnp.einsum(
        "fe,ne->fn", hidden_rows[:, 0], w_in_left, preferred_element_type=jnp.float32
    ) + jnp.einsum("fe,ne->fn", hidden_rows[:, 1], w_in_right, preferred_element_type=jnp.float32)
    ln_hat, rstd_ln = norm(frames)
    grad_hat = grad_ln * gains
    grad_input = rstd_ln * (
        grad_hat
        - jnp.mean(grad_hat, axis=1, keepdims=True)
        - ln_hat * jnp.mean(grad_hat * ln_hat, axis=1, keepdims=True)
    )
    grad_frames = (out_grad.astype(jnp.float32) + grad_input).astype(jnp.bfloat16)
    return (
        outputs,
        grad_frames,
        grad_w_in,
        grad_w_out,
        grad_kernel,
        grad_ln_gain,
        gain_total * grad_scale,
        bias_total * grad_scale,
    )


def solution(mesh):
    devices = mesh.shape["seq"]
    body = channel_local if devices <= 16 else local
    return jax.shard_map(
        body,
        mesh=mesh,
        in_specs=(
            P(("mix", "seq"), None),
            P(("mix", "seq")),
            P(("mix", "seq"), None),
            P(("mix", "seq")),
            P(("mix", "seq"), None),
            P("mix", "seq"),
            P(("mix", "seq")),
            P(("mix", "seq")),
            P(("mix", "seq"), None),
        ),
        out_specs=(
            P(("mix", "seq"), None),
            P(("mix", "seq"), None),
            P(("mix", "seq"), None),
            P(("mix", "seq"), None),
            P("mix", "seq"),
            P(("mix", "seq")),
            P(("mix", "seq")),
            P(("mix", "seq")),
        ),
        check_vma=False,
    )
```

```python
import math

import jax
import jax.numpy as jnp
from jax import lax
from jax.sharding import PartitionSpec as P

EPSILON = 1e-05


def with_halo(cells, sides, width):
    for axis, dim in sides:
        count = lax.axis_size(axis)
        ends = count - 1
        head = lax.slice_in_dim(cells, 0, width, axis=dim)
        tail = lax.slice_in_dim(cells, cells.shape[dim] - width, cells.shape[dim], axis=dim)
        cells = jnp.concatenate(
            [
                lax.ppermute(tail, axis, [(i, (i + 1) % count) for i in range(ends)]),
                cells,
                lax.ppermute(head, axis, [((i + 1) % count, i) for i in range(ends)]),
            ],
            axis=dim,
        )
    return cells


def local(frames, segment_ids, out_grad, ln_gain, w_in, dw_kernel, bn_gain, bn_bias, w_out):
    frame_count = frames.shape[0]
    width = frames.shape[1]
    taps = dw_kernel.shape[0]
    margin = taps // 2
    devices = lax.axis_size("seq")
    stream = frame_count * devices
    grad_scale = 1.0 / math.sqrt(stream)
    share = width // devices
    gains, kernel, bn_scale, bn_shift = (
        lax.all_gather(ln_gain, "seq", axis=0, tiled=True),
        lax.all_gather(dw_kernel, "seq", axis=1, tiled=True),
        lax.all_gather(bn_gain, "seq", axis=0, tiled=True),
        lax.all_gather(bn_bias, "seq", axis=0, tiled=True),
    )
    own_ids = segment_ids + 1
    padded_ids = with_halo(own_ids, (("seq", 0),), margin)
    masks = [
        (padded_ids[tap_index : tap_index + frame_count] == own_ids).astype(jnp.float32)[:, None]
        for tap_index in range(taps)
    ]
    frames_float = frames.astype(jnp.float32)
    mean_ln = jnp.mean(frames_float, axis=1, keepdims=True)
    centred = frames_float - mean_ln
    rstd_ln = lax.rsqrt(jnp.mean(centred * centred, axis=1, keepdims=True) + EPSILON)
    ln_hat = centred * rstd_ln
    ln_x = (ln_hat * gains).astype(jnp.bfloat16)
    columns = ln_x
    hidden = jnp.dot(
        columns, lax.all_gather(w_in, "seq", axis=0, tiled=True), preferred_element_type=jnp.float32
    )
    left_half = hidden[:, :width]
    right_gate = jax.nn.sigmoid(hidden[:, width:])
    glu = (left_half * right_gate).astype(jnp.bfloat16)
    padded_glu = with_halo(glu, (("seq", 0),), margin)
    conv_out = jnp.zeros((frame_count, width), jnp.float32)
    for tap_index in range(taps):
        conv_out = (
            conv_out
            + kernel[tap_index]
            * padded_glu[tap_index : tap_index + frame_count].astype(jnp.float32)
            * masks[tap_index]
        )
    plain_sums, square_sums = lax.psum(
        (jnp.sum(conv_out, axis=0), jnp.sum(conv_out * conv_out, axis=0)), "seq"
    )
    bn_mean = plain_sums / stream
    bn_var = square_sums / stream - bn_mean * bn_mean
    bn_rstd = lax.rsqrt(bn_var + EPSILON)
    bn_hat = (conv_out - bn_mean) * bn_rstd
    zed = bn_hat * bn_scale + bn_shift
    zed_gate = jax.nn.sigmoid(zed)
    activation = (zed * zed_gate).astype(jnp.bfloat16)
    columns = activation
    projected = jnp.dot(
        columns,
        lax.all_gather(w_out, "seq", axis=0, tiled=True),
        preferred_element_type=jnp.float32,
    )
    outputs = (frames_float + projected).astype(jnp.bfloat16)
    grad_w_out = lax.psum_scatter(
        jnp.einsum("fa,fb->ab", activation, out_grad, preferred_element_type=jnp.float32)
        * grad_scale,
        "seq",
        scatter_dimension=0,
        tiled=True,
    )
    grad_act = jnp.einsum(
        "fe,ne->fn",
        out_grad,
        lax.all_gather(w_out, "seq", axis=0, tiled=True),
        preferred_element_type=jnp.float32,
    )
    grad_zed = grad_act * zed_gate * (1.0 + zed * (1.0 - zed_gate))
    bias_total, gain_total = lax.psum(
        (jnp.sum(grad_zed, axis=0), jnp.sum(grad_zed * bn_hat, axis=0)), "seq"
    )
    grad_conv = bn_scale * bn_rstd * (grad_zed - bias_total / stream - bn_hat * gain_total / stream)
    first_channel = lax.axis_index("seq") * share
    grad_bn_bias = lax.dynamic_slice_in_dim(bias_total, first_channel, share, 0) * grad_scale
    grad_bn_gain = lax.dynamic_slice_in_dim(gain_total, first_channel, share, 0) * grad_scale
    kernel_rows = [
        jnp.sum(
            grad_conv
            * padded_glu[tap_index : tap_index + frame_count].astype(jnp.float32)
            * masks[tap_index],
            axis=0,
        )
        for tap_index in range(taps)
    ]
    kernel_term = jnp.stack(kernel_rows) * grad_scale
    padded_conv = with_halo(grad_conv, (("seq", 0),), margin)
    grad_glu = jnp.zeros((frame_count, width), jnp.float32)
    for tap_index in range(taps):
        mirror = 2 * margin - tap_index
        grad_glu = (
            grad_glu
            + kernel[tap_index] * padded_conv[mirror : mirror + frame_count] * masks[mirror]
        )
    grad_hidden = jnp.concatenate(
        [grad_glu * right_gate, grad_glu * left_half * right_gate * (1.0 - right_gate)], axis=1
    ).astype(jnp.bfloat16)
    grad_ln = jnp.einsum(
        "fe,ne->fn",
        grad_hidden,
        lax.all_gather(w_in, "seq", axis=0, tiled=True),
        preferred_element_type=jnp.float32,
    )
    in_term = (
        jnp.einsum("fa,fb->ab", ln_x, grad_hidden, preferred_element_type=jnp.float32) * grad_scale
    )
    gain_term = jnp.sum(grad_ln * ln_hat, axis=0) * grad_scale
    grad_w_in, grad_kernel, grad_ln_gain = (
        lax.psum_scatter(in_term, "seq", scatter_dimension=0, tiled=True),
        lax.psum_scatter(kernel_term, "seq", scatter_dimension=1, tiled=True),
        lax.psum_scatter(gain_term, "seq", scatter_dimension=0, tiled=True),
    )
    grad_hat = grad_ln * gains
    grad_input = rstd_ln * (
        grad_hat
        - jnp.mean(grad_hat, axis=1, keepdims=True)
        - ln_hat * jnp.mean(grad_hat * ln_hat, axis=1, keepdims=True)
    )
    grad_frames = (out_grad.astype(jnp.float32) + grad_input).astype(jnp.bfloat16)
    return (
        outputs,
        grad_frames,
        grad_w_in,
        grad_w_out,
        grad_kernel,
        grad_ln_gain,
        grad_bn_gain,
        grad_bn_bias,
    )


def channel_local(frames, segment_ids, out_grad, ln_gain, w_in, dw_kernel, bn_gain, bn_bias, w_out):
    rows = frames.shape[0]
    width = frames.shape[1]
    taps = dw_kernel.shape[0]
    margin = taps // 2
    devices = lax.axis_size("seq")
    stream = rows * devices
    grad_scale = 1.0 / math.sqrt(stream)
    share = width // devices

    def spread(block):
        copies = jnp.broadcast_to(block[None], (devices,) + block.shape)
        return lax.all_to_all(copies, "seq", 0, 0, tiled=True)

    small = spread(jnp.concatenate([ln_gain, segment_ids.astype(jnp.float32)]))
    gains = small[:, :share].reshape(width)
    all_ids = small[:, share:].reshape(stream).astype(jnp.int32)

    out_rows = w_out.shape[0]
    pieces = lax.all_gather(jnp.concatenate([frames, out_grad], axis=0), "seq", axis=0)
    frames_all = pieces[:, :rows].reshape(stream, width)
    grad_all = pieces[:, rows:].reshape(stream, width)
    w_in_cols = lax.all_to_all(
        w_in.reshape(share, 2, devices, share).transpose(2, 0, 1, 3), "seq", 0, 0, tiled=True
    ).reshape(width, 2 * share)
    w_in_late, w_out_late, _, _, _ = lax.optimization_barrier(
        (w_in, w_out, pieces, w_in_cols, small)
    )
    weights = lax.all_gather(
        jnp.concatenate([w_out_late, w_in_late[:, :width], w_in_late[:, width:]], axis=0),
        "seq",
        axis=0,
    )
    w_out_all = weights[:, :out_rows].reshape(width, width)
    w_in_left = weights[:, out_rows : 2 * out_rows].reshape(width, width)
    w_in_right = weights[:, 2 * out_rows :].reshape(width, width)

    first_channel = lax.axis_index("seq") * share

    def norm(block):
        block_float = block.astype(jnp.float32)
        mean = jnp.mean(block_float, axis=1, keepdims=True)
        centred = block_float - mean
        rstd = lax.rsqrt(jnp.mean(centred * centred, axis=1, keepdims=True) + EPSILON)
        return centred * rstd, rstd

    ln_all, _ = norm(frames_all)
    ln_x_all = (ln_all * gains).astype(jnp.bfloat16)

    hidden = jnp.dot(ln_x_all, w_in_cols, preferred_element_type=jnp.float32)
    left_half = hidden[:, :share]
    right_gate = jax.nn.sigmoid(hidden[:, share:])
    glu = (left_half * right_gate).astype(jnp.bfloat16)

    own_ids = all_ids + 1
    padded_ids = jnp.pad(own_ids, margin)
    masks = [
        (padded_ids[tap_index : tap_index + stream] == own_ids).astype(jnp.float32)[:, None]
        for tap_index in range(taps)
    ]
    padded_glu = jnp.pad(glu, ((margin, margin), (0, 0)))
    conv_out = jnp.zeros((stream, share), jnp.float32)
    for tap_index in range(taps):
        conv_out = (
            conv_out
            + dw_kernel[tap_index]
            * padded_glu[tap_index : tap_index + stream].astype(jnp.float32)
            * masks[tap_index]
        )
    bn_mean = jnp.sum(conv_out, axis=0) / stream
    bn_var = jnp.sum((conv_out - bn_mean) ** 2, axis=0) / stream
    bn_rstd = lax.rsqrt(bn_var + EPSILON)
    bn_hat = (conv_out - bn_mean) * bn_rstd
    zed = bn_hat * bn_gain + bn_bias
    zed_gate = jax.nn.sigmoid(zed)
    activation = (zed * zed_gate).astype(jnp.bfloat16)


    grad_w_out = (
        jnp.einsum("fa,fb->ab", activation, grad_all, preferred_element_type=jnp.float32)
        * grad_scale
    )
    grad_act = jnp.einsum("fe,ne->fn", grad_all, w_out, preferred_element_type=jnp.float32)
    grad_zed = grad_act * zed_gate * (1.0 + zed * (1.0 - zed_gate))
    bias_total = jnp.sum(grad_zed, axis=0)
    gain_total = jnp.sum(grad_zed * bn_hat, axis=0)
    grad_conv = bn_gain * bn_rstd * (grad_zed - bias_total / stream - bn_hat * gain_total / stream)
    grad_kernel = (
        jnp.stack(
            [
                jnp.sum(
                    grad_conv
                    * padded_glu[tap_index : tap_index + stream].astype(jnp.float32)
                    * masks[tap_index],
                    axis=0,
                )
                for tap_index in range(taps)
            ]
        )
        * grad_scale
    )
    padded_conv = jnp.pad(grad_conv, ((margin, margin), (0, 0)))
    grad_glu = jnp.zeros((stream, share), jnp.float32)
    for tap_index in range(taps):
        mirror = 2 * margin - tap_index
        grad_glu = (
            grad_glu
            + dw_kernel[tap_index] * padded_conv[mirror : mirror + stream] * masks[mirror]
        )
    grad_hidden = jnp.concatenate(
        [grad_glu * right_gate, grad_glu * left_half * right_gate * (1.0 - right_gate)], axis=1
    ).astype(jnp.bfloat16)

    in_cols = (
        jnp.einsum("fa,fb->ab", ln_x_all, grad_hidden, preferred_element_type=jnp.float32)
        * grad_scale
    )
    ln_head = lax.reduce_precision(ln_all, exponent_bits=8, mantissa_bits=7)
    moments = jnp.einsum(
        "fa,fb->ab", ln_head.astype(jnp.bfloat16), grad_hidden, preferred_element_type=jnp.float32
    ) + jnp.einsum(
        "fa,fb->ab",
        (ln_all - ln_head).astype(jnp.bfloat16),
        grad_hidden,
        preferred_element_type=jnp.float32,
    )
    gain_part = jnp.sum(w_in_cols.astype(jnp.float32) * moments, axis=1) * grad_scale
    packed = lax.all_to_all(
        jnp.concatenate(
            [in_cols.reshape(devices, share * 2 * share), gain_part.reshape(devices, share)],
            axis=1,
        ),
        "seq", 0, 0, tiled=True,
    )
    grad_w_in = (
        packed[:, : share * 2 * share]
        .reshape(devices, share, 2, share)
        .transpose(1, 2, 0, 3)
        .reshape(share, 2 * width)
    )
    grad_ln_gain = jnp.sum(packed[:, share * 2 * share :], axis=0)
    back = lax.all_to_all(
        jnp.concatenate([activation, grad_hidden], axis=1).reshape(devices, rows, 3 * share),
        "seq", 0, 0, tiled=True,
    )
    act_rows = back[:, :, :share].transpose(1, 0, 2).reshape(rows, width)
    hidden_rows = (
        back[:, :, share:].reshape(devices, rows, 2, share).transpose(1, 2, 0, 3)
        .reshape(rows, 2, width)
    )
    projected = jnp.dot(act_rows, w_out_all, preferred_element_type=jnp.float32)
    outputs = (frames.astype(jnp.float32) + projected).astype(jnp.bfloat16)
    grad_ln = jnp.einsum(
        "fe,ne->fn", hidden_rows[:, 0], w_in_left, preferred_element_type=jnp.float32
    ) + jnp.einsum("fe,ne->fn", hidden_rows[:, 1], w_in_right, preferred_element_type=jnp.float32)
    ln_hat, rstd_ln = norm(frames)
    grad_hat = grad_ln * gains
    grad_input = rstd_ln * (
        grad_hat
        - jnp.mean(grad_hat, axis=1, keepdims=True)
        - ln_hat * jnp.mean(grad_hat * ln_hat, axis=1, keepdims=True)
    )
    grad_frames = (out_grad.astype(jnp.float32) + grad_input).astype(jnp.bfloat16)
    return (
        outputs,
        grad_frames,
        grad_w_in,
        grad_w_out,
        grad_kernel,
        grad_ln_gain,
        gain_total * grad_scale,
        bias_total * grad_scale,
    )


def solution(mesh):
    devices = mesh.shape["seq"]
    body = channel_local if devices <= 16 else local
    return jax.shard_map(
        body,
        mesh=mesh,
        in_specs=(
            P(("mix", "seq"), None),
            P(("mix", "seq")),
            P(("mix", "seq"), None),
            P(("mix", "seq")),
            P(("mix", "seq"), None),
            P("mix", "seq"),
            P(("mix", "seq")),
            P(("mix", "seq")),
            P(("mix", "seq"), None),
        ),
        out_specs=(
            P(("mix", "seq"), None),
            P(("mix", "seq"), None),
            P(("mix", "seq"), None),
            P(("mix", "seq"), None),
            P("mix", "seq"),
            P(("mix", "seq")),
            P(("mix", "seq")),
            P(("mix", "seq")),
        ),
        check_vma=False,
    )
```

```python
import math

import jax
import jax.numpy as jnp
from jax import lax
from jax.sharding import PartitionSpec as P

EPSILON = 1e-05


def with_halo(cells, sides, width):
    for axis, dim in sides:
        count = lax.axis_size(axis)
        ends = count - 1
        head = lax.slice_in_dim(cells, 0, width, axis=dim)
        tail = lax.slice_in_dim(cells, cells.shape[dim] - width, cells.shape[dim], axis=dim)
        cells = jnp.concatenate(
            [
                lax.ppermute(tail, axis, [(i, (i + 1) % count) for i in range(ends)]),
                cells,
                lax.ppermute(head, axis, [((i + 1) % count, i) for i in range(ends)]),
            ],
            axis=dim,
        )
    return cells


def local(frames, segment_ids, out_grad, ln_gain, w_in, dw_kernel, bn_gain, bn_bias, w_out):
    frame_count = frames.shape[0]
    width = frames.shape[1]
    taps = dw_kernel.shape[0]
    margin = taps // 2
    devices = lax.axis_size("seq")
    stream = frame_count * devices
    grad_scale = 1.0 / math.sqrt(stream)
    share = width // devices
    gains, kernel, bn_scale, bn_shift = (
        lax.all_gather(ln_gain, "seq", axis=0, tiled=True),
        lax.all_gather(dw_kernel, "seq", axis=1, tiled=True),
        lax.all_gather(bn_gain, "seq", axis=0, tiled=True),
        lax.all_gather(bn_bias, "seq", axis=0, tiled=True),
    )
    own_ids = segment_ids + 1
    padded_ids = with_halo(own_ids, (("seq", 0),), margin)
    masks = [
        (padded_ids[tap_index : tap_index + frame_count] == own_ids).astype(jnp.float32)[:, None]
        for tap_index in range(taps)
    ]
    frames_float = frames.astype(jnp.float32)
    mean_ln = jnp.mean(frames_float, axis=1, keepdims=True)
    centred = frames_float - mean_ln
    rstd_ln = lax.rsqrt(jnp.mean(centred * centred, axis=1, keepdims=True) + EPSILON)
    ln_hat = centred * rstd_ln
    ln_x = (ln_hat * gains).astype(jnp.bfloat16)
    columns = ln_x
    hidden = jnp.dot(
        columns, lax.all_gather(w_in, "seq", axis=0, tiled=True), preferred_element_type=jnp.float32
    )
    left_half = hidden[:, :width]
    right_gate = jax.nn.sigmoid(hidden[:, width:])
    glu = (left_half * right_gate).astype(jnp.bfloat16)
    padded_glu = with_halo(glu, (("seq", 0),), margin)
    conv_out = jnp.zeros((frame_count, width), jnp.float32)
    for tap_index in range(taps):
        conv_out = (
            conv_out
            + kernel[tap_index]
            * padded_glu[tap_index : tap_index + frame_count].astype(jnp.float32)
            * masks[tap_index]
        )
    plain_sums, square_sums = lax.psum(
        (jnp.sum(conv_out, axis=0), jnp.sum(conv_out * conv_out, axis=0)), "seq"
    )
    bn_mean = plain_sums / stream
    bn_var = square_sums / stream - bn_mean * bn_mean
    bn_rstd = lax.rsqrt(bn_var + EPSILON)
    bn_hat = (conv_out - bn_mean) * bn_rstd
    zed = bn_hat * bn_scale + bn_shift
    zed_gate = jax.nn.sigmoid(zed)
    activation = (zed * zed_gate).astype(jnp.bfloat16)
    columns = activation
    projected = jnp.dot(
        columns,
        lax.all_gather(w_out, "seq", axis=0, tiled=True),
        preferred_element_type=jnp.float32,
    )
    outputs = (frames_float + projected).astype(jnp.bfloat16)
    grad_w_out = lax.psum_scatter(
        jnp.einsum("fa,fb->ab", activation, out_grad, preferred_element_type=jnp.float32)
        * grad_scale,
        "seq",
        scatter_dimension=0,
        tiled=True,
    )
    grad_act = jnp.einsum(
        "fe,ne->fn",
        out_grad,
        lax.all_gather(w_out, "seq", axis=0, tiled=True),
        preferred_element_type=jnp.float32,
    )
    grad_zed = grad_act * zed_gate * (1.0 + zed * (1.0 - zed_gate))
    bias_total, gain_total = lax.psum(
        (jnp.sum(grad_zed, axis=0), jnp.sum(grad_zed * bn_hat, axis=0)), "seq"
    )
    grad_conv = bn_scale * bn_rstd * (grad_zed - bias_total / stream - bn_hat * gain_total / stream)
    first_channel = lax.axis_index("seq") * share
    grad_bn_bias = lax.dynamic_slice_in_dim(bias_total, first_channel, share, 0) * grad_scale
    grad_bn_gain = lax.dynamic_slice_in_dim(gain_total, first_channel, share, 0) * grad_scale
    kernel_rows = [
        jnp.sum(
            grad_conv
            * padded_glu[tap_index : tap_index + frame_count].astype(jnp.float32)
            * masks[tap_index],
            axis=0,
        )
        for tap_index in range(taps)
    ]
    kernel_term = jnp.stack(kernel_rows) * grad_scale
    padded_conv = with_halo(grad_conv, (("seq", 0),), margin)
    grad_glu = jnp.zeros((frame_count, width), jnp.float32)
    for tap_index in range(taps):
        mirror = 2 * margin - tap_index
        grad_glu = (
            grad_glu
            + kernel[tap_index] * padded_conv[mirror : mirror + frame_count] * masks[mirror]
        )
    grad_hidden = jnp.concatenate(
        [grad_glu * right_gate, grad_glu * left_half * right_gate * (1.0 - right_gate)], axis=1
    ).astype(jnp.bfloat16)
    grad_ln = jnp.einsum(
        "fe,ne->fn",
        grad_hidden,
        lax.all_gather(w_in, "seq", axis=0, tiled=True),
        preferred_element_type=jnp.float32,
    )
    in_term = (
        jnp.einsum("fa,fb->ab", ln_x, grad_hidden, preferred_element_type=jnp.float32) * grad_scale
    )
    gain_term = jnp.sum(grad_ln * ln_hat, axis=0) * grad_scale
    grad_w_in, grad_kernel, grad_ln_gain = (
        lax.psum_scatter(in_term, "seq", scatter_dimension=0, tiled=True),
        lax.psum_scatter(kernel_term, "seq", scatter_dimension=1, tiled=True),
        lax.psum_scatter(gain_term, "seq", scatter_dimension=0, tiled=True),
    )
    grad_hat = grad_ln * gains
    grad_input = rstd_ln * (
        grad_hat
        - jnp.mean(grad_hat, axis=1, keepdims=True)
        - ln_hat * jnp.mean(grad_hat * ln_hat, axis=1, keepdims=True)
    )
    grad_frames = (out_grad.astype(jnp.float32) + grad_input).astype(jnp.bfloat16)
    return (
        outputs,
        grad_frames,
        grad_w_in,
        grad_w_out,
        grad_kernel,
        grad_ln_gain,
        grad_bn_gain,
        grad_bn_bias,
    )


def channel_local(frames, segment_ids, out_grad, ln_gain, w_in, dw_kernel, bn_gain, bn_bias, w_out):
    rows = frames.shape[0]
    width = frames.shape[1]
    taps = dw_kernel.shape[0]
    margin = taps // 2
    devices = lax.axis_size("seq")
    stream = rows * devices
    grad_scale = 1.0 / math.sqrt(stream)
    share = width // devices

    def spread(block):
        copies = jnp.broadcast_to(block[None], (devices,) + block.shape)
        return lax.all_to_all(copies, "seq", 0, 0, tiled=True)

    small = spread(jnp.concatenate([ln_gain, segment_ids.astype(jnp.float32)]))
    gains = small[:, :share].reshape(width)
    all_ids = small[:, share:].reshape(stream).astype(jnp.int32)

    out_rows = w_out.shape[0]
    pieces = lax.all_gather(jnp.concatenate([frames, out_grad], axis=0), "seq", axis=0)
    frames_all = pieces[:, :rows].reshape(stream, width)
    grad_all = pieces[:, rows:].reshape(stream, width)
    w_in_cols = lax.all_to_all(
        w_in.reshape(share, 2, devices, share).transpose(2, 0, 1, 3), "seq", 0, 0, tiled=True
    ).reshape(width, 2 * share)
    w_in_late, w_out_late, _, _, _ = lax.optimization_barrier(
        (w_in, w_out, pieces, w_in_cols, small)
    )
    weights = lax.all_gather(
        jnp.concatenate([w_out_late, w_in_late[:, :width], w_in_late[:, width:]], axis=0),
        "seq",
        axis=0,
    )
    w_out_all = weights[:, :out_rows].reshape(width, width)
    w_in_left = weights[:, out_rows : 2 * out_rows].reshape(width, width)
    w_in_right = weights[:, 2 * out_rows :].reshape(width, width)

    first_channel = lax.axis_index("seq") * share

    def norm(block):
        block_float = block.astype(jnp.float32)
        mean = jnp.mean(block_float, axis=1, keepdims=True)
        centred = block_float - mean
        rstd = lax.rsqrt(jnp.mean(centred * centred, axis=1, keepdims=True) + EPSILON)
        return centred * rstd, rstd

    ln_all, rstd_all = norm(frames_all)
    ln_x_all = (ln_all * gains).astype(jnp.bfloat16)

    hidden = jnp.dot(ln_x_all, w_in_cols, preferred_element_type=jnp.float32)
    left_half = hidden[:, :share]
    right_gate = jax.nn.sigmoid(hidden[:, share:])
    glu = (left_half * right_gate).astype(jnp.bfloat16)

    own_ids = all_ids + 1
    padded_ids = jnp.pad(own_ids, margin)
    masks = [
        (padded_ids[tap_index : tap_index + stream] == own_ids).astype(jnp.float32)[:, None]
        for tap_index in range(taps)
    ]
    padded_glu = jnp.pad(glu, ((margin, margin), (0, 0)))
    conv_out = jnp.zeros((stream, share), jnp.float32)
    for tap_index in range(taps):
        conv_out = (
            conv_out
            + dw_kernel[tap_index]
            * padded_glu[tap_index : tap_index + stream].astype(jnp.float32)
            * masks[tap_index]
        )
    bn_mean = jnp.sum(conv_out, axis=0) / stream
    bn_var = jnp.sum((conv_out - bn_mean) ** 2, axis=0) / stream
    bn_rstd = lax.rsqrt(bn_var + EPSILON)
    bn_hat = (conv_out - bn_mean) * bn_rstd
    zed = bn_hat * bn_gain + bn_bias
    zed_gate = jax.nn.sigmoid(zed)
    activation = (zed * zed_gate).astype(jnp.bfloat16)


    grad_w_out = (
        jnp.einsum("fa,fb->ab", activation, grad_all, preferred_element_type=jnp.float32)
        * grad_scale
    )
    grad_act = jnp.einsum("fe,ne->fn", grad_all, w_out, preferred_element_type=jnp.float32)
    grad_zed = grad_act * zed_gate * (1.0 + zed * (1.0 - zed_gate))
    bias_total = jnp.sum(grad_zed, axis=0)
    gain_total = jnp.sum(grad_zed * bn_hat, axis=0)
    grad_conv = bn_gain * bn_rstd * (grad_zed - bias_total / stream - bn_hat * gain_total / stream)
    grad_kernel = (
        jnp.stack(
            [
                jnp.sum(
                    grad_conv
                    * padded_glu[tap_index : tap_index + stream].astype(jnp.float32)
                    * masks[tap_index],
                    axis=0,
                )
                for tap_index in range(taps)
            ]
        )
        * grad_scale
    )
    padded_conv = jnp.pad(grad_conv, ((margin, margin), (0, 0)))
    grad_glu = jnp.zeros((stream, share), jnp.float32)
    for tap_index in range(taps):
        mirror = 2 * margin - tap_index
        grad_glu = (
            grad_glu
            + dw_kernel[tap_index] * padded_conv[mirror : mirror + stream] * masks[mirror]
        )
    grad_hidden = jnp.concatenate(
        [grad_glu * right_gate, grad_glu * left_half * right_gate * (1.0 - right_gate)], axis=1
    ).astype(jnp.bfloat16)

    in_cols = (
        jnp.einsum("fa,fb->ab", ln_x_all, grad_hidden, preferred_element_type=jnp.float32)
        * grad_scale
    )
    ln_head = lax.reduce_precision(ln_all, exponent_bits=8, mantissa_bits=7)
    moments = jnp.einsum(
        "fa,fb->ab", ln_head.astype(jnp.bfloat16), grad_hidden, preferred_element_type=jnp.float32
    ) + jnp.einsum(
        "fa,fb->ab",
        (ln_all - ln_head).astype(jnp.bfloat16),
        grad_hidden,
        preferred_element_type=jnp.float32,
    )
    gain_part = jnp.sum(w_in_cols.astype(jnp.float32) * moments, axis=1) * grad_scale
    packed = lax.all_to_all(
        jnp.concatenate(
            [in_cols.reshape(devices, share * 2 * share), gain_part.reshape(devices, share)],
            axis=1,
        ),
        "seq", 0, 0, tiled=True,
    )
    grad_w_in = (
        packed[:, : share * 2 * share]
        .reshape(devices, share, 2, share)
        .transpose(1, 2, 0, 3)
        .reshape(share, 2 * width)
    )
    grad_ln_gain = jnp.sum(packed[:, share * 2 * share :], axis=0)
    back = lax.all_to_all(
        jnp.concatenate([activation, grad_hidden], axis=1).reshape(devices, rows, 3 * share),
        "seq", 0, 0, tiled=True,
    )
    act_rows = back[:, :, :share].transpose(1, 0, 2).reshape(rows, width)
    hidden_rows = (
        back[:, :, share:].reshape(devices, rows, 2, share).transpose(1, 2, 0, 3)
        .reshape(rows, 2, width)
    )
    projected = jnp.dot(act_rows, w_out_all, preferred_element_type=jnp.float32)
    outputs = (frames.astype(jnp.float32) + projected).astype(jnp.bfloat16)
    grad_ln = jnp.einsum(
        "fe,ne->fn", hidden_rows[:, 0], w_in_left, preferred_element_type=jnp.float32
    ) + jnp.einsum("fe,ne->fn", hidden_rows[:, 1], w_in_right, preferred_element_type=jnp.float32)
    first_row = lax.axis_index("seq") * rows
    ln_hat = lax.dynamic_slice_in_dim(ln_all, first_row, rows, 0)
    rstd_ln = lax.dynamic_slice_in_dim(rstd_all, first_row, rows, 0)
    grad_hat = grad_ln * gains
    grad_input = rstd_ln * (
        grad_hat
        - jnp.mean(grad_hat, axis=1, keepdims=True)
        - ln_hat * jnp.mean(grad_hat * ln_hat, axis=1, keepdims=True)
    )
    grad_frames = (out_grad.astype(jnp.float32) + grad_input).astype(jnp.bfloat16)
    return (
        outputs,
        grad_frames,
        grad_w_in,
        grad_w_out,
        grad_kernel,
        grad_ln_gain,
        gain_total * grad_scale,
        bias_total * grad_scale,
    )


def solution(mesh):
    devices = mesh.shape["seq"]
    body = channel_local if devices <= 16 else local
    return jax.shard_map(
        body,
        mesh=mesh,
        in_specs=(
            P(("mix", "seq"), None),
            P(("mix", "seq")),
            P(("mix", "seq"), None),
            P(("mix", "seq")),
            P(("mix", "seq"), None),
            P("mix", "seq"),
            P(("mix", "seq")),
            P(("mix", "seq")),
            P(("mix", "seq"), None),
        ),
        out_specs=(
            P(("mix", "seq"), None),
            P(("mix", "seq"), None),
            P(("mix", "seq"), None),
            P(("mix", "seq"), None),
            P("mix", "seq"),
            P(("mix", "seq")),
            P(("mix", "seq")),
            P(("mix", "seq")),
        ),
        check_vma=False,
    )
```

```python
import math

import jax
import jax.numpy as jnp
from jax import lax
from jax.sharding import PartitionSpec as P

EPSILON = 1e-05


def with_halo(cells, sides, width):
    for axis, dim in sides:
        count = lax.axis_size(axis)
        ends = count - 1
        head = lax.slice_in_dim(cells, 0, width, axis=dim)
        tail = lax.slice_in_dim(cells, cells.shape[dim] - width, cells.shape[dim], axis=dim)
        cells = jnp.concatenate(
            [
                lax.ppermute(tail, axis, [(i, (i + 1) % count) for i in range(ends)]),
                cells,
                lax.ppermute(head, axis, [((i + 1) % count, i) for i in range(ends)]),
            ],
            axis=dim,
        )
    return cells


def local(frames, segment_ids, out_grad, ln_gain, w_in, dw_kernel, bn_gain, bn_bias, w_out):
    frame_count = frames.shape[0]
    width = frames.shape[1]
    taps = dw_kernel.shape[0]
    margin = taps // 2
    devices = lax.axis_size("seq")
    stream = frame_count * devices
    grad_scale = 1.0 / math.sqrt(stream)
    share = width // devices
    gains, kernel, bn_scale, bn_shift = (
        lax.all_gather(ln_gain, "seq", axis=0, tiled=True),
        lax.all_gather(dw_kernel, "seq", axis=1, tiled=True),
        lax.all_gather(bn_gain, "seq", axis=0, tiled=True),
        lax.all_gather(bn_bias, "seq", axis=0, tiled=True),
    )
    own_ids = segment_ids + 1
    padded_ids = with_halo(own_ids, (("seq", 0),), margin)
    masks = [
        (padded_ids[tap_index : tap_index + frame_count] == own_ids).astype(jnp.float32)[:, None]
        for tap_index in range(taps)
    ]
    frames_float = frames.astype(jnp.float32)
    mean_ln = jnp.mean(frames_float, axis=1, keepdims=True)
    centred = frames_float - mean_ln
    rstd_ln = lax.rsqrt(jnp.mean(centred * centred, axis=1, keepdims=True) + EPSILON)
    ln_hat = centred * rstd_ln
    ln_x = (ln_hat * gains).astype(jnp.bfloat16)
    columns = ln_x
    hidden = jnp.dot(
        columns, lax.all_gather(w_in, "seq", axis=0, tiled=True), preferred_element_type=jnp.float32
    )
    left_half = hidden[:, :width]
    right_gate = jax.nn.sigmoid(hidden[:, width:])
    glu = (left_half * right_gate).astype(jnp.bfloat16)
    padded_glu = with_halo(glu, (("seq", 0),), margin)
    conv_out = jnp.zeros((frame_count, width), jnp.float32)
    for tap_index in range(taps):
        conv_out = (
            conv_out
            + kernel[tap_index]
            * padded_glu[tap_index : tap_index + frame_count].astype(jnp.float32)
            * masks[tap_index]
        )
    plain_sums, square_sums = lax.psum(
        (jnp.sum(conv_out, axis=0), jnp.sum(conv_out * conv_out, axis=0)), "seq"
    )
    bn_mean = plain_sums / stream
    bn_var = square_sums / stream - bn_mean * bn_mean
    bn_rstd = lax.rsqrt(bn_var + EPSILON)
    bn_hat = (conv_out - bn_mean) * bn_rstd
    zed = bn_hat * bn_scale + bn_shift
    zed_gate = jax.nn.sigmoid(zed)
    activation = (zed * zed_gate).astype(jnp.bfloat16)
    columns = activation
    projected = jnp.dot(
        columns,
        lax.all_gather(w_out, "seq", axis=0, tiled=True),
        preferred_element_type=jnp.float32,
    )
    outputs = (frames_float + projected).astype(jnp.bfloat16)
    grad_w_out = lax.psum_scatter(
        jnp.einsum("fa,fb->ab", activation, out_grad, preferred_element_type=jnp.float32)
        * grad_scale,
        "seq",
        scatter_dimension=0,
        tiled=True,
    )
    grad_act = jnp.einsum(
        "fe,ne->fn",
        out_grad,
        lax.all_gather(w_out, "seq", axis=0, tiled=True),
        preferred_element_type=jnp.float32,
    )
    grad_zed = grad_act * zed_gate * (1.0 + zed * (1.0 - zed_gate))
    bias_total, gain_total = lax.psum(
        (jnp.sum(grad_zed, axis=0), jnp.sum(grad_zed * bn_hat, axis=0)), "seq"
    )
    grad_conv = bn_scale * bn_rstd * (grad_zed - bias_total / stream - bn_hat * gain_total / stream)
    first_channel = lax.axis_index("seq") * share
    grad_bn_bias = lax.dynamic_slice_in_dim(bias_total, first_channel, share, 0) * grad_scale
    grad_bn_gain = lax.dynamic_slice_in_dim(gain_total, first_channel, share, 0) * grad_scale
    kernel_rows = [
        jnp.sum(
            grad_conv
            * padded_glu[tap_index : tap_index + frame_count].astype(jnp.float32)
            * masks[tap_index],
            axis=0,
        )
        for tap_index in range(taps)
    ]
    kernel_term = jnp.stack(kernel_rows) * grad_scale
    padded_conv = with_halo(grad_conv, (("seq", 0),), margin)
    grad_glu = jnp.zeros((frame_count, width), jnp.float32)
    for tap_index in range(taps):
        mirror = 2 * margin - tap_index
        grad_glu = (
            grad_glu
            + kernel[tap_index] * padded_conv[mirror : mirror + frame_count] * masks[mirror]
        )
    grad_hidden = jnp.concatenate(
        [grad_glu * right_gate, grad_glu * left_half * right_gate * (1.0 - right_gate)], axis=1
    ).astype(jnp.bfloat16)
    grad_ln = jnp.einsum(
        "fe,ne->fn",
        grad_hidden,
        lax.all_gather(w_in, "seq", axis=0, tiled=True),
        preferred_element_type=jnp.float32,
    )
    in_term = (
        jnp.einsum("fa,fb->ab", ln_x, grad_hidden, preferred_element_type=jnp.float32) * grad_scale
    )
    gain_term = jnp.sum(grad_ln * ln_hat, axis=0) * grad_scale
    grad_w_in, grad_kernel, grad_ln_gain = (
        lax.psum_scatter(in_term, "seq", scatter_dimension=0, tiled=True),
        lax.psum_scatter(kernel_term, "seq", scatter_dimension=1, tiled=True),
        lax.psum_scatter(gain_term, "seq", scatter_dimension=0, tiled=True),
    )
    grad_hat = grad_ln * gains
    grad_input = rstd_ln * (
        grad_hat
        - jnp.mean(grad_hat, axis=1, keepdims=True)
        - ln_hat * jnp.mean(grad_hat * ln_hat, axis=1, keepdims=True)
    )
    grad_frames = (out_grad.astype(jnp.float32) + grad_input).astype(jnp.bfloat16)
    return (
        outputs,
        grad_frames,
        grad_w_in,
        grad_w_out,
        grad_kernel,
        grad_ln_gain,
        grad_bn_gain,
        grad_bn_bias,
    )


def channel_local(frames, segment_ids, out_grad, ln_gain, w_in, dw_kernel, bn_gain, bn_bias, w_out):
    rows = frames.shape[0]
    width = frames.shape[1]
    taps = dw_kernel.shape[0]
    margin = taps // 2
    devices = lax.axis_size("seq")
    stream = rows * devices
    grad_scale = 1.0 / math.sqrt(stream)
    share = width // devices

    def spread(block):
        copies = jnp.broadcast_to(block[None], (devices,) + block.shape)
        return lax.all_to_all(copies, "seq", 0, 0, tiled=True)

    small = spread(jnp.concatenate([ln_gain, segment_ids.astype(jnp.float32)]))
    gains = small[:, :share].reshape(width)
    all_ids = small[:, share:].reshape(stream).astype(jnp.int32)

    out_rows = w_out.shape[0]
    pieces = lax.all_gather(jnp.concatenate([frames, out_grad, w_out], axis=0), "seq", axis=0)
    frames_all = pieces[:, :rows].reshape(stream, width)
    grad_all = pieces[:, rows : 2 * rows].reshape(stream, width)
    w_out_all = pieces[:, 2 * rows :].reshape(width, width)
    w_in_cols = lax.all_to_all(
        w_in.reshape(share, 2, devices, share).transpose(2, 0, 1, 3), "seq", 0, 0, tiled=True
    ).reshape(width, 2 * share)
    w_in_late, _, _, _ = lax.optimization_barrier((w_in, pieces, w_in_cols, small))
    weights = lax.all_gather(
        jnp.concatenate([w_in_late[:, :width], w_in_late[:, width:]], axis=0), "seq", axis=0
    )
    w_in_left = weights[:, :out_rows].reshape(width, width)
    w_in_right = weights[:, out_rows:].reshape(width, width)

    first_channel = lax.axis_index("seq") * share

    def norm(block):
        block_float = block.astype(jnp.float32)
        mean = jnp.mean(block_float, axis=1, keepdims=True)
        centred = block_float - mean
        rstd = lax.rsqrt(jnp.mean(centred * centred, axis=1, keepdims=True) + EPSILON)
        return centred * rstd, rstd

    ln_all, _ = norm(frames_all)
    ln_x_all = (ln_all * gains).astype(jnp.bfloat16)

    hidden = jnp.dot(ln_x_all, w_in_cols, preferred_element_type=jnp.float32)
    left_half = hidden[:, :share]
    right_gate = jax.nn.sigmoid(hidden[:, share:])
    glu = (left_half * right_gate).astype(jnp.bfloat16)

    own_ids = all_ids + 1
    padded_ids = jnp.pad(own_ids, margin)
    masks = [
        (padded_ids[tap_index : tap_index + stream] == own_ids).astype(jnp.float32)[:, None]
        for tap_index in range(taps)
    ]
    padded_glu = jnp.pad(glu, ((margin, margin), (0, 0)))
    conv_out = jnp.zeros((stream, share), jnp.float32)
    for tap_index in range(taps):
        conv_out = (
            conv_out
            + dw_kernel[tap_index]
            * padded_glu[tap_index : tap_index + stream].astype(jnp.float32)
            * masks[tap_index]
        )
    bn_mean = jnp.sum(conv_out, axis=0) / stream
    bn_var = jnp.sum((conv_out - bn_mean) ** 2, axis=0) / stream
    bn_rstd = lax.rsqrt(bn_var + EPSILON)
    bn_hat = (conv_out - bn_mean) * bn_rstd
    zed = bn_hat * bn_gain + bn_bias
    zed_gate = jax.nn.sigmoid(zed)
    activation = (zed * zed_gate).astype(jnp.bfloat16)


    grad_w_out = (
        jnp.einsum("fa,fb->ab", activation, grad_all, preferred_element_type=jnp.float32)
        * grad_scale
    )
    grad_act = jnp.einsum("fe,ne->fn", grad_all, w_out, preferred_element_type=jnp.float32)
    grad_zed = grad_act * zed_gate * (1.0 + zed * (1.0 - zed_gate))
    bias_total = jnp.sum(grad_zed, axis=0)
    gain_total = jnp.sum(grad_zed * bn_hat, axis=0)
    grad_conv = bn_gain * bn_rstd * (grad_zed - bias_total / stream - bn_hat * gain_total / stream)
    grad_kernel = (
        jnp.stack(
            [
                jnp.sum(
                    grad_conv
                    * padded_glu[tap_index : tap_index + stream].astype(jnp.float32)
                    * masks[tap_index],
                    axis=0,
                )
                for tap_index in range(taps)
            ]
        )
        * grad_scale
    )
    padded_conv = jnp.pad(grad_conv, ((margin, margin), (0, 0)))
    grad_glu = jnp.zeros((stream, share), jnp.float32)
    for tap_index in range(taps):
        mirror = 2 * margin - tap_index
        grad_glu = (
            grad_glu
            + dw_kernel[tap_index] * padded_conv[mirror : mirror + stream] * masks[mirror]
        )
    grad_hidden = jnp.concatenate(
        [grad_glu * right_gate, grad_glu * left_half * right_gate * (1.0 - right_gate)], axis=1
    ).astype(jnp.bfloat16)

    in_cols = (
        jnp.einsum("fa,fb->ab", ln_x_all, grad_hidden, preferred_element_type=jnp.float32)
        * grad_scale
    )
    ln_head = lax.reduce_precision(ln_all, exponent_bits=8, mantissa_bits=7)
    moments = jnp.einsum(
        "fa,fb->ab", ln_head.astype(jnp.bfloat16), grad_hidden, preferred_element_type=jnp.float32
    ) + jnp.einsum(
        "fa,fb->ab",
        (ln_all - ln_head).astype(jnp.bfloat16),
        grad_hidden,
        preferred_element_type=jnp.float32,
    )
    gain_part = jnp.sum(w_in_cols.astype(jnp.float32) * moments, axis=1) * grad_scale
    packed = lax.all_to_all(
        jnp.concatenate(
            [in_cols.reshape(devices, share * 2 * share), gain_part.reshape(devices, share)],
            axis=1,
        ),
        "seq", 0, 0, tiled=True,
    )
    grad_w_in = (
        packed[:, : share * 2 * share]
        .reshape(devices, share, 2, share)
        .transpose(1, 2, 0, 3)
        .reshape(share, 2 * width)
    )
    grad_ln_gain = jnp.sum(packed[:, share * 2 * share :], axis=0)
    back = lax.all_to_all(
        jnp.concatenate([activation, grad_hidden], axis=1).reshape(devices, rows, 3 * share),
        "seq", 0, 0, tiled=True,
    )
    act_rows = back[:, :, :share].transpose(1, 0, 2).reshape(rows, width)
    hidden_rows = (
        back[:, :, share:].reshape(devices, rows, 2, share).transpose(1, 2, 0, 3)
        .reshape(rows, 2, width)
    )
    projected = jnp.dot(act_rows, w_out_all, preferred_element_type=jnp.float32)
    outputs = (frames.astype(jnp.float32) + projected).astype(jnp.bfloat16)
    grad_ln = jnp.einsum(
        "fe,ne->fn", hidden_rows[:, 0], w_in_left, preferred_element_type=jnp.float32
    ) + jnp.einsum("fe,ne->fn", hidden_rows[:, 1], w_in_right, preferred_element_type=jnp.float32)
    ln_hat, rstd_ln = norm(frames)
    grad_hat = grad_ln * gains
    grad_input = rstd_ln * (
        grad_hat
        - jnp.mean(grad_hat, axis=1, keepdims=True)
        - ln_hat * jnp.mean(grad_hat * ln_hat, axis=1, keepdims=True)
    )
    grad_frames = (out_grad.astype(jnp.float32) + grad_input).astype(jnp.bfloat16)
    return (
        outputs,
        grad_frames,
        grad_w_in,
        grad_w_out,
        grad_kernel,
        grad_ln_gain,
        gain_total * grad_scale,
        bias_total * grad_scale,
    )


def solution(mesh):
    devices = mesh.shape["seq"]
    body = channel_local if devices <= 16 else local
    return jax.shard_map(
        body,
        mesh=mesh,
        in_specs=(
            P(("mix", "seq"), None),
            P(("mix", "seq")),
            P(("mix", "seq"), None),
            P(("mix", "seq")),
            P(("mix", "seq"), None),
            P("mix", "seq"),
            P(("mix", "seq")),
            P(("mix", "seq")),
            P(("mix", "seq"), None),
        ),
        out_specs=(
            P(("mix", "seq"), None),
            P(("mix", "seq"), None),
            P(("mix", "seq"), None),
            P(("mix", "seq"), None),
            P("mix", "seq"),
            P(("mix", "seq")),
            P(("mix", "seq")),
            P(("mix", "seq")),
        ),
        check_vma=False,
    )
```

```python
import math

import jax
import jax.numpy as jnp
from jax import lax
from jax.sharding import PartitionSpec as P

EPSILON = 1e-05


def with_halo(cells, sides, width):
    for axis, dim in sides:
        count = lax.axis_size(axis)
        ends = count - 1
        head = lax.slice_in_dim(cells, 0, width, axis=dim)
        tail = lax.slice_in_dim(cells, cells.shape[dim] - width, cells.shape[dim], axis=dim)
        cells = jnp.concatenate(
            [
                lax.ppermute(tail, axis, [(i, (i + 1) % count) for i in range(ends)]),
                cells,
                lax.ppermute(head, axis, [((i + 1) % count, i) for i in range(ends)]),
            ],
            axis=dim,
        )
    return cells


def local(frames, segment_ids, out_grad, ln_gain, w_in, dw_kernel, bn_gain, bn_bias, w_out):
    frame_count = frames.shape[0]
    width = frames.shape[1]
    taps = dw_kernel.shape[0]
    margin = taps // 2
    devices = lax.axis_size("seq")
    stream = frame_count * devices
    grad_scale = 1.0 / math.sqrt(stream)
    share = width // devices
    gains, kernel, bn_scale, bn_shift = (
        lax.all_gather(ln_gain, "seq", axis=0, tiled=True),
        lax.all_gather(dw_kernel, "seq", axis=1, tiled=True),
        lax.all_gather(bn_gain, "seq", axis=0, tiled=True),
        lax.all_gather(bn_bias, "seq", axis=0, tiled=True),
    )
    own_ids = segment_ids + 1
    padded_ids = with_halo(own_ids, (("seq", 0),), margin)
    masks = [
        (padded_ids[tap_index : tap_index + frame_count] == own_ids).astype(jnp.float32)[:, None]
        for tap_index in range(taps)
    ]
    frames_float = frames.astype(jnp.float32)
    mean_ln = jnp.mean(frames_float, axis=1, keepdims=True)
    centred = frames_float - mean_ln
    rstd_ln = lax.rsqrt(jnp.mean(centred * centred, axis=1, keepdims=True) + EPSILON)
    ln_hat = centred * rstd_ln
    ln_x = (ln_hat * gains).astype(jnp.bfloat16)
    columns = ln_x
    hidden = jnp.dot(
        columns, lax.all_gather(w_in, "seq", axis=0, tiled=True), preferred_element_type=jnp.float32
    )
    left_half = hidden[:, :width]
    right_gate = jax.nn.sigmoid(hidden[:, width:])
    glu = (left_half * right_gate).astype(jnp.bfloat16)
    padded_glu = with_halo(glu, (("seq", 0),), margin)
    conv_out = jnp.zeros((frame_count, width), jnp.float32)
    for tap_index in range(taps):
        conv_out = (
            conv_out
            + kernel[tap_index]
            * padded_glu[tap_index : tap_index + frame_count].astype(jnp.float32)
            * masks[tap_index]
        )
    plain_sums, square_sums = lax.psum(
        (jnp.sum(conv_out, axis=0), jnp.sum(conv_out * conv_out, axis=0)), "seq"
    )
    bn_mean = plain_sums / stream
    bn_var = square_sums / stream - bn_mean * bn_mean
    bn_rstd = lax.rsqrt(bn_var + EPSILON)
    bn_hat = (conv_out - bn_mean) * bn_rstd
    zed = bn_hat * bn_scale + bn_shift
    zed_gate = jax.nn.sigmoid(zed)
    activation = (zed * zed_gate).astype(jnp.bfloat16)
    columns = activation
    projected = jnp.dot(
        columns,
        lax.all_gather(w_out, "seq", axis=0, tiled=True),
        preferred_element_type=jnp.float32,
    )
    outputs = (frames_float + projected).astype(jnp.bfloat16)
    grad_w_out = lax.psum_scatter(
        jnp.einsum("fa,fb->ab", activation, out_grad, preferred_element_type=jnp.float32)
        * grad_scale,
        "seq",
        scatter_dimension=0,
        tiled=True,
    )
    grad_act = jnp.einsum(
        "fe,ne->fn",
        out_grad,
        lax.all_gather(w_out, "seq", axis=0, tiled=True),
        preferred_element_type=jnp.float32,
    )
    grad_zed = grad_act * zed_gate * (1.0 + zed * (1.0 - zed_gate))
    bias_total, gain_total = lax.psum(
        (jnp.sum(grad_zed, axis=0), jnp.sum(grad_zed * bn_hat, axis=0)), "seq"
    )
    grad_conv = bn_scale * bn_rstd * (grad_zed - bias_total / stream - bn_hat * gain_total / stream)
    first_channel = lax.axis_index("seq") * share
    grad_bn_bias = lax.dynamic_slice_in_dim(bias_total, first_channel, share, 0) * grad_scale
    grad_bn_gain = lax.dynamic_slice_in_dim(gain_total, first_channel, share, 0) * grad_scale
    kernel_rows = [
        jnp.sum(
            grad_conv
            * padded_glu[tap_index : tap_index + frame_count].astype(jnp.float32)
            * masks[tap_index],
            axis=0,
        )
        for tap_index in range(taps)
    ]
    kernel_term = jnp.stack(kernel_rows) * grad_scale
    padded_conv = with_halo(grad_conv, (("seq", 0),), margin)
    grad_glu = jnp.zeros((frame_count, width), jnp.float32)
    for tap_index in range(taps):
        mirror = 2 * margin - tap_index
        grad_glu = (
            grad_glu
            + kernel[tap_index] * padded_conv[mirror : mirror + frame_count] * masks[mirror]
        )
    grad_hidden = jnp.concatenate(
        [grad_glu * right_gate, grad_glu * left_half * right_gate * (1.0 - right_gate)], axis=1
    ).astype(jnp.bfloat16)
    grad_ln = jnp.einsum(
        "fe,ne->fn",
        grad_hidden,
        lax.all_gather(w_in, "seq", axis=0, tiled=True),
        preferred_element_type=jnp.float32,
    )
    in_term = (
        jnp.einsum("fa,fb->ab", ln_x, grad_hidden, preferred_element_type=jnp.float32) * grad_scale
    )
    gain_term = jnp.sum(grad_ln * ln_hat, axis=0) * grad_scale
    grad_w_in, grad_kernel, grad_ln_gain = (
        lax.psum_scatter(in_term, "seq", scatter_dimension=0, tiled=True),
        lax.psum_scatter(kernel_term, "seq", scatter_dimension=1, tiled=True),
        lax.psum_scatter(gain_term, "seq", scatter_dimension=0, tiled=True),
    )
    grad_hat = grad_ln * gains
    grad_input = rstd_ln * (
        grad_hat
        - jnp.mean(grad_hat, axis=1, keepdims=True)
        - ln_hat * jnp.mean(grad_hat * ln_hat, axis=1, keepdims=True)
    )
    grad_frames = (out_grad.astype(jnp.float32) + grad_input).astype(jnp.bfloat16)
    return (
        outputs,
        grad_frames,
        grad_w_in,
        grad_w_out,
        grad_kernel,
        grad_ln_gain,
        grad_bn_gain,
        grad_bn_bias,
    )


def channel_local(frames, segment_ids, out_grad, ln_gain, w_in, dw_kernel, bn_gain, bn_bias, w_out):
    rows = frames.shape[0]
    width = frames.shape[1]
    taps = dw_kernel.shape[0]
    margin = taps // 2
    devices = lax.axis_size("seq")
    stream = rows * devices
    grad_scale = 1.0 / math.sqrt(stream)
    share = width // devices

    def spread(block):
        copies = jnp.broadcast_to(block[None], (devices,) + block.shape)
        return lax.all_to_all(copies, "seq", 0, 0, tiled=True)

    small = spread(jnp.concatenate([ln_gain, segment_ids.astype(jnp.float32)]))
    gains = small[:, :share].reshape(width)
    all_ids = small[:, share:].reshape(stream).astype(jnp.int32)

    out_rows = w_out.shape[0]
    pieces = lax.all_gather(jnp.concatenate([frames, out_grad], axis=0), "seq", axis=0)
    frames_all = pieces[:, :rows].reshape(stream, width)
    grad_all = pieces[:, rows:].reshape(stream, width)
    w_in_cols = lax.all_to_all(
        w_in.reshape(share, 2, devices, share).transpose(2, 0, 1, 3), "seq", 0, 0, tiled=True
    ).reshape(width, 2 * share)
    w_in_late, w_out_late, _, _, _ = lax.optimization_barrier(
        (w_in, w_out, pieces, w_in_cols, small)
    )
    weights = lax.all_gather(
        jnp.concatenate([w_out_late, w_in_late[:, :width], w_in_late[:, width:]], axis=0),
        "seq",
        axis=0,
    )
    w_out_all = weights[:, :out_rows].reshape(width, width)
    w_in_left = weights[:, out_rows : 2 * out_rows].reshape(width, width)
    w_in_right = weights[:, 2 * out_rows :].reshape(width, width)

    first_channel = lax.axis_index("seq") * share

    def norm(block):
        block_float = block.astype(jnp.float32)
        mean = jnp.mean(block_float, axis=1, keepdims=True)
        centred = block_float - mean
        rstd = lax.rsqrt(jnp.mean(centred * centred, axis=1, keepdims=True) + EPSILON)
        return centred * rstd, rstd

    ln_all, _ = norm(frames_all)
    ln_x_all = (ln_all * gains).astype(jnp.bfloat16)
    ln_head32 = lax.reduce_precision(ln_all, exponent_bits=8, mantissa_bits=7)
    ln_x_all, ln_head, ln_tail = lax.optimization_barrier(
        (ln_x_all, ln_head32.astype(jnp.bfloat16), (ln_all - ln_head32).astype(jnp.bfloat16))
    )

    hidden = jnp.dot(ln_x_all, w_in_cols, preferred_element_type=jnp.float32)
    left_half = hidden[:, :share]
    right_gate = jax.nn.sigmoid(hidden[:, share:])
    glu = (left_half * right_gate).astype(jnp.bfloat16)

    own_ids = all_ids + 1
    padded_ids = jnp.pad(own_ids, margin)
    masks = [
        (padded_ids[tap_index : tap_index + stream] == own_ids).astype(jnp.float32)[:, None]
        for tap_index in range(taps)
    ]
    padded_glu = jnp.pad(glu, ((margin, margin), (0, 0)))
    conv_out = jnp.zeros((stream, share), jnp.float32)
    for tap_index in range(taps):
        conv_out = (
            conv_out
            + dw_kernel[tap_index]
            * padded_glu[tap_index : tap_index + stream].astype(jnp.float32)
            * masks[tap_index]
        )
    bn_mean = jnp.sum(conv_out, axis=0) / stream
    bn_var = jnp.sum((conv_out - bn_mean) ** 2, axis=0) / stream
    bn_rstd = lax.rsqrt(bn_var + EPSILON)
    bn_hat = (conv_out - bn_mean) * bn_rstd
    zed = bn_hat * bn_gain + bn_bias
    zed_gate = jax.nn.sigmoid(zed)
    activation = (zed * zed_gate).astype(jnp.bfloat16)


    grad_w_out = (
        jnp.einsum("fa,fb->ab", activation, grad_all, preferred_element_type=jnp.float32)
        * grad_scale
    )
    grad_act = jnp.einsum("fe,ne->fn", grad_all, w_out, preferred_element_type=jnp.float32)
    grad_zed = grad_act * zed_gate * (1.0 + zed * (1.0 - zed_gate))
    bias_total = jnp.sum(grad_zed, axis=0)
    gain_total = jnp.sum(grad_zed * bn_hat, axis=0)
    grad_conv = bn_gain * bn_rstd * (grad_zed - bias_total / stream - bn_hat * gain_total / stream)
    grad_kernel = (
        jnp.stack(
            [
                jnp.sum(
                    grad_conv
                    * padded_glu[tap_index : tap_index + stream].astype(jnp.float32)
                    * masks[tap_index],
                    axis=0,
                )
                for tap_index in range(taps)
            ]
        )
        * grad_scale
    )
    padded_conv = jnp.pad(grad_conv, ((margin, margin), (0, 0)))
    grad_glu = jnp.zeros((stream, share), jnp.float32)
    for tap_index in range(taps):
        mirror = 2 * margin - tap_index
        grad_glu = (
            grad_glu
            + dw_kernel[tap_index] * padded_conv[mirror : mirror + stream] * masks[mirror]
        )
    grad_hidden = jnp.concatenate(
        [grad_glu * right_gate, grad_glu * left_half * right_gate * (1.0 - right_gate)], axis=1
    ).astype(jnp.bfloat16)

    in_cols = (
        jnp.einsum("fa,fb->ab", ln_x_all, grad_hidden, preferred_element_type=jnp.float32)
        * grad_scale
    )
    moments = jnp.einsum(
        "fa,fb->ab", ln_head, grad_hidden, preferred_element_type=jnp.float32
    ) + jnp.einsum("fa,fb->ab", ln_tail, grad_hidden, preferred_element_type=jnp.float32)
    gain_part = jnp.sum(w_in_cols.astype(jnp.float32) * moments, axis=1) * grad_scale
    packed = lax.all_to_all(
        jnp.concatenate(
            [in_cols.reshape(devices, share * 2 * share), gain_part.reshape(devices, share)],
            axis=1,
        ),
        "seq", 0, 0, tiled=True,
    )
    grad_w_in = (
        packed[:, : share * 2 * share]
        .reshape(devices, share, 2, share)
        .transpose(1, 2, 0, 3)
        .reshape(share, 2 * width)
    )
    grad_ln_gain = jnp.sum(packed[:, share * 2 * share :], axis=0)
    back = lax.all_to_all(
        jnp.concatenate([activation, grad_hidden], axis=1).reshape(devices, rows, 3 * share),
        "seq", 0, 0, tiled=True,
    )
    act_rows = back[:, :, :share].transpose(1, 0, 2).reshape(rows, width)
    hidden_rows = (
        back[:, :, share:].reshape(devices, rows, 2, share).transpose(1, 2, 0, 3)
        .reshape(rows, 2, width)
    )
    projected = jnp.dot(act_rows, w_out_all, preferred_element_type=jnp.float32)
    outputs = (frames.astype(jnp.float32) + projected).astype(jnp.bfloat16)
    grad_ln = jnp.einsum(
        "fe,ne->fn", hidden_rows[:, 0], w_in_left, preferred_element_type=jnp.float32
    ) + jnp.einsum("fe,ne->fn", hidden_rows[:, 1], w_in_right, preferred_element_type=jnp.float32)
    ln_hat, rstd_ln = norm(frames)
    grad_hat = grad_ln * gains
    grad_input = rstd_ln * (
        grad_hat
        - jnp.mean(grad_hat, axis=1, keepdims=True)
        - ln_hat * jnp.mean(grad_hat * ln_hat, axis=1, keepdims=True)
    )
    grad_frames = (out_grad.astype(jnp.float32) + grad_input).astype(jnp.bfloat16)
    return (
        outputs,
        grad_frames,
        grad_w_in,
        grad_w_out,
        grad_kernel,
        grad_ln_gain,
        gain_total * grad_scale,
        bias_total * grad_scale,
    )


def solution(mesh):
    devices = mesh.shape["seq"]
    body = channel_local if devices <= 16 else local
    return jax.shard_map(
        body,
        mesh=mesh,
        in_specs=(
            P(("mix", "seq"), None),
            P(("mix", "seq")),
            P(("mix", "seq"), None),
            P(("mix", "seq")),
            P(("mix", "seq"), None),
            P("mix", "seq"),
            P(("mix", "seq")),
            P(("mix", "seq")),
            P(("mix", "seq"), None),
        ),
        out_specs=(
            P(("mix", "seq"), None),
            P(("mix", "seq"), None),
            P(("mix", "seq"), None),
            P(("mix", "seq"), None),
            P("mix", "seq"),
            P(("mix", "seq")),
            P(("mix", "seq")),
            P(("mix", "seq")),
        ),
        check_vma=False,
    )
```

```python
import math

import jax
import jax.numpy as jnp
from jax import lax
from jax.sharding import PartitionSpec as P

EPSILON = 1e-05


def with_halo(cells, sides, width):
    for axis, dim in sides:
        count = lax.axis_size(axis)
        ends = count - 1
        head = lax.slice_in_dim(cells, 0, width, axis=dim)
        tail = lax.slice_in_dim(cells, cells.shape[dim] - width, cells.shape[dim], axis=dim)
        cells = jnp.concatenate(
            [
                lax.ppermute(tail, axis, [(i, (i + 1) % count) for i in range(ends)]),
                cells,
                lax.ppermute(head, axis, [((i + 1) % count, i) for i in range(ends)]),
            ],
            axis=dim,
        )
    return cells


def local(frames, segment_ids, out_grad, ln_gain, w_in, dw_kernel, bn_gain, bn_bias, w_out):
    frame_count = frames.shape[0]
    width = frames.shape[1]
    taps = dw_kernel.shape[0]
    margin = taps // 2
    devices = lax.axis_size("seq")
    stream = frame_count * devices
    grad_scale = 1.0 / math.sqrt(stream)
    share = width // devices
    gains, kernel, bn_scale, bn_shift = (
        lax.all_gather(ln_gain, "seq", axis=0, tiled=True),
        lax.all_gather(dw_kernel, "seq", axis=1, tiled=True),
        lax.all_gather(bn_gain, "seq", axis=0, tiled=True),
        lax.all_gather(bn_bias, "seq", axis=0, tiled=True),
    )
    own_ids = segment_ids + 1
    padded_ids = with_halo(own_ids, (("seq", 0),), margin)
    masks = [
        (padded_ids[tap_index : tap_index + frame_count] == own_ids).astype(jnp.float32)[:, None]
        for tap_index in range(taps)
    ]
    frames_float = frames.astype(jnp.float32)
    mean_ln = jnp.mean(frames_float, axis=1, keepdims=True)
    centred = frames_float - mean_ln
    rstd_ln = lax.rsqrt(jnp.mean(centred * centred, axis=1, keepdims=True) + EPSILON)
    ln_hat = centred * rstd_ln
    ln_x = (ln_hat * gains).astype(jnp.bfloat16)
    columns = ln_x
    hidden = jnp.dot(
        columns, lax.all_gather(w_in, "seq", axis=0, tiled=True), preferred_element_type=jnp.float32
    )
    left_half = hidden[:, :width]
    right_gate = jax.nn.sigmoid(hidden[:, width:])
    glu = (left_half * right_gate).astype(jnp.bfloat16)
    padded_glu = with_halo(glu, (("seq", 0),), margin)
    conv_out = jnp.zeros((frame_count, width), jnp.float32)
    for tap_index in range(taps):
        conv_out = (
            conv_out
            + kernel[tap_index]
            * padded_glu[tap_index : tap_index + frame_count].astype(jnp.float32)
            * masks[tap_index]
        )
    plain_sums, square_sums = lax.psum(
        (jnp.sum(conv_out, axis=0), jnp.sum(conv_out * conv_out, axis=0)), "seq"
    )
    bn_mean = plain_sums / stream
    bn_var = square_sums / stream - bn_mean * bn_mean
    bn_rstd = lax.rsqrt(bn_var + EPSILON)
    bn_hat = (conv_out - bn_mean) * bn_rstd
    zed = bn_hat * bn_scale + bn_shift
    zed_gate = jax.nn.sigmoid(zed)
    activation = (zed * zed_gate).astype(jnp.bfloat16)
    columns = activation
    projected = jnp.dot(
        columns,
        lax.all_gather(w_out, "seq", axis=0, tiled=True),
        preferred_element_type=jnp.float32,
    )
    outputs = (frames_float + projected).astype(jnp.bfloat16)
    grad_w_out = lax.psum_scatter(
        jnp.einsum("fa,fb->ab", activation, out_grad, preferred_element_type=jnp.float32)
        * grad_scale,
        "seq",
        scatter_dimension=0,
        tiled=True,
    )
    grad_act = jnp.einsum(
        "fe,ne->fn",
        out_grad,
        lax.all_gather(w_out, "seq", axis=0, tiled=True),
        preferred_element_type=jnp.float32,
    )
    grad_zed = grad_act * zed_gate * (1.0 + zed * (1.0 - zed_gate))
    bias_total, gain_total = lax.psum(
        (jnp.sum(grad_zed, axis=0), jnp.sum(grad_zed * bn_hat, axis=0)), "seq"
    )
    grad_conv = bn_scale * bn_rstd * (grad_zed - bias_total / stream - bn_hat * gain_total / stream)
    first_channel = lax.axis_index("seq") * share
    grad_bn_bias = lax.dynamic_slice_in_dim(bias_total, first_channel, share, 0) * grad_scale
    grad_bn_gain = lax.dynamic_slice_in_dim(gain_total, first_channel, share, 0) * grad_scale
    kernel_rows = [
        jnp.sum(
            grad_conv
            * padded_glu[tap_index : tap_index + frame_count].astype(jnp.float32)
            * masks[tap_index],
            axis=0,
        )
        for tap_index in range(taps)
    ]
    kernel_term = jnp.stack(kernel_rows) * grad_scale
    padded_conv = with_halo(grad_conv, (("seq", 0),), margin)
    grad_glu = jnp.zeros((frame_count, width), jnp.float32)
    for tap_index in range(taps):
        mirror = 2 * margin - tap_index
        grad_glu = (
            grad_glu
            + kernel[tap_index] * padded_conv[mirror : mirror + frame_count] * masks[mirror]
        )
    grad_hidden = jnp.concatenate(
        [grad_glu * right_gate, grad_glu * left_half * right_gate * (1.0 - right_gate)], axis=1
    ).astype(jnp.bfloat16)
    grad_ln = jnp.einsum(
        "fe,ne->fn",
        grad_hidden,
        lax.all_gather(w_in, "seq", axis=0, tiled=True),
        preferred_element_type=jnp.float32,
    )
    in_term = (
        jnp.einsum("fa,fb->ab", ln_x, grad_hidden, preferred_element_type=jnp.float32) * grad_scale
    )
    gain_term = jnp.sum(grad_ln * ln_hat, axis=0) * grad_scale
    grad_w_in, grad_kernel, grad_ln_gain = (
        lax.psum_scatter(in_term, "seq", scatter_dimension=0, tiled=True),
        lax.psum_scatter(kernel_term, "seq", scatter_dimension=1, tiled=True),
        lax.psum_scatter(gain_term, "seq", scatter_dimension=0, tiled=True),
    )
    grad_hat = grad_ln * gains
    grad_input = rstd_ln * (
        grad_hat
        - jnp.mean(grad_hat, axis=1, keepdims=True)
        - ln_hat * jnp.mean(grad_hat * ln_hat, axis=1, keepdims=True)
    )
    grad_frames = (out_grad.astype(jnp.float32) + grad_input).astype(jnp.bfloat16)
    return (
        outputs,
        grad_frames,
        grad_w_in,
        grad_w_out,
        grad_kernel,
        grad_ln_gain,
        grad_bn_gain,
        grad_bn_bias,
    )


def channel_local(frames, segment_ids, out_grad, ln_gain, w_in, dw_kernel, bn_gain, bn_bias, w_out):
    rows = frames.shape[0]
    width = frames.shape[1]
    taps = dw_kernel.shape[0]
    margin = taps // 2
    devices = lax.axis_size("seq")
    stream = rows * devices
    grad_scale = 1.0 / math.sqrt(stream)
    share = width // devices

    def spread(block):
        copies = jnp.broadcast_to(block[None], (devices,) + block.shape)
        return lax.all_to_all(copies, "seq", 0, 0, tiled=True)

    small = spread(jnp.concatenate([ln_gain, segment_ids.astype(jnp.float32)]))
    gains = small[:, :share].reshape(width)
    all_ids = small[:, share:].reshape(stream).astype(jnp.int32)

    out_rows = w_out.shape[0]
    pieces = lax.all_gather(jnp.concatenate([frames, out_grad], axis=0), "seq", axis=0)
    frames_all = pieces[:, :rows].reshape(stream, width)
    grad_all = pieces[:, rows:].reshape(stream, width)
    w_in_cols = lax.all_to_all(
        w_in.reshape(share, 2, devices, share).transpose(2, 0, 1, 3), "seq", 0, 0, tiled=True
    ).reshape(width, 2 * share)
    w_in_late, w_out_late, _, _, _ = lax.optimization_barrier(
        (w_in, w_out, pieces, w_in_cols, small)
    )
    weights = lax.all_gather(
        jnp.concatenate([w_out_late, w_in_late[:, :width], w_in_late[:, width:]], axis=0),
        "seq",
        axis=0,
    )
    w_out_all = weights[:, :out_rows].reshape(width, width)
    w_in_left = weights[:, out_rows : 2 * out_rows].reshape(width, width)
    w_in_right = weights[:, 2 * out_rows :].reshape(width, width)

    first_channel = lax.axis_index("seq") * share

    def norm(block):
        block_float = block.astype(jnp.float32)
        mean = jnp.mean(block_float, axis=1, keepdims=True)
        centred = block_float - mean
        rstd = lax.rsqrt(jnp.mean(centred * centred, axis=1, keepdims=True) + EPSILON)
        return centred * rstd, rstd

    ln_all, _ = norm(frames_all)
    ln_x_all = (ln_all * gains).astype(jnp.bfloat16)
    ln_head32 = lax.reduce_precision(ln_all, exponent_bits=8, mantissa_bits=7)
    ln_x_all, ln_head, ln_tail = lax.optimization_barrier(
        (ln_x_all, ln_head32.astype(jnp.bfloat16), (ln_all - ln_head32).astype(jnp.bfloat16))
    )

    hidden = jnp.dot(ln_x_all, w_in_cols, preferred_element_type=jnp.float32)
    left_half = hidden[:, :share]
    right_gate = jax.nn.sigmoid(hidden[:, share:])
    glu = (left_half * right_gate).astype(jnp.bfloat16)

    own_ids = all_ids + 1
    padded_ids = jnp.pad(own_ids, margin)
    masks = [
        (padded_ids[tap_index : tap_index + stream] == own_ids).astype(jnp.float32)[:, None]
        for tap_index in range(taps)
    ]
    padded_glu = jnp.pad(glu, ((margin, margin), (0, 0)))
    conv_out = jnp.zeros((stream, share), jnp.float32)
    for tap_index in range(taps):
        conv_out = (
            conv_out
            + dw_kernel[tap_index]
            * padded_glu[tap_index : tap_index + stream].astype(jnp.float32)
            * masks[tap_index]
        )
    bn_mean = jnp.sum(conv_out, axis=0) / stream
    bn_var = jnp.sum((conv_out - bn_mean) ** 2, axis=0) / stream
    bn_rstd = lax.rsqrt(bn_var + EPSILON)
    bn_hat = (conv_out - bn_mean) * bn_rstd
    zed = bn_hat * bn_gain + bn_bias
    zed_gate = jax.nn.sigmoid(zed)
    activation = (zed * zed_gate).astype(jnp.bfloat16)


    grad_w_out = (
        jnp.einsum("fa,fb->ab", activation, grad_all, preferred_element_type=jnp.float32)
        * grad_scale
    )
    grad_act = jnp.einsum("fe,ne->fn", grad_all, w_out, preferred_element_type=jnp.float32)
    grad_zed = grad_act * zed_gate * (1.0 + zed * (1.0 - zed_gate))
    bias_total = jnp.sum(grad_zed, axis=0)
    gain_total = jnp.sum(grad_zed * bn_hat, axis=0)
    grad_conv = bn_gain * bn_rstd * (grad_zed - bias_total / stream - bn_hat * gain_total / stream)
    grad_kernel = (
        jnp.stack(
            [
                jnp.sum(
                    grad_conv
                    * padded_glu[tap_index : tap_index + stream].astype(jnp.float32)
                    * masks[tap_index],
                    axis=0,
                )
                for tap_index in range(taps)
            ]
        )
        * grad_scale
    )
    padded_conv = jnp.pad(grad_conv, ((margin, margin), (0, 0)))
    grad_glu = jnp.zeros((stream, share), jnp.float32)
    for tap_index in range(taps):
        mirror = 2 * margin - tap_index
        grad_glu = (
            grad_glu
            + dw_kernel[tap_index] * padded_conv[mirror : mirror + stream] * masks[mirror]
        )
    grad_hidden = jnp.concatenate(
        [grad_glu * right_gate, grad_glu * left_half * right_gate * (1.0 - right_gate)], axis=1
    ).astype(jnp.bfloat16)

    in_cols = (
        jnp.einsum("fa,fb->ab", ln_x_all, grad_hidden, preferred_element_type=jnp.float32)
        * grad_scale
    )
    moments = jnp.einsum(
        "fa,fb->ab", ln_head, grad_hidden, preferred_element_type=jnp.float32
    ) + jnp.einsum("fa,fb->ab", ln_tail, grad_hidden, preferred_element_type=jnp.float32)
    gain_part = jnp.sum(w_in_cols.astype(jnp.float32) * moments, axis=1) * grad_scale
    packed = lax.all_to_all(
        jnp.concatenate(
            [in_cols.reshape(devices, share * 2 * share), gain_part.reshape(devices, share)],
            axis=1,
        ),
        "seq", 0, 0, tiled=True,
    )
    grad_w_in = (
        packed[:, : share * 2 * share]
        .reshape(devices, share, 2, share)
        .transpose(1, 2, 0, 3)
        .reshape(share, 2 * width)
    )
    grad_ln_gain = jnp.sum(packed[:, share * 2 * share :], axis=0)
    back = lax.all_to_all(
        jnp.concatenate([activation, grad_hidden], axis=1).T.reshape(3 * share, devices, rows),
        "seq", 1, 1, tiled=True,
    ).transpose(1, 2, 0)
    act_rows = back[:, :, :share].transpose(1, 0, 2).reshape(rows, width)
    hidden_rows = (
        back[:, :, share:].reshape(devices, rows, 2, share).transpose(1, 2, 0, 3)
        .reshape(rows, 2, width)
    )
    projected = jnp.dot(act_rows, w_out_all, preferred_element_type=jnp.float32)
    outputs = (frames.astype(jnp.float32) + projected).astype(jnp.bfloat16)
    grad_ln = jnp.einsum(
        "fe,ne->fn", hidden_rows[:, 0], w_in_left, preferred_element_type=jnp.float32
    ) + jnp.einsum("fe,ne->fn", hidden_rows[:, 1], w_in_right, preferred_element_type=jnp.float32)
    ln_hat, rstd_ln = norm(frames)
    grad_hat = grad_ln * gains
    grad_input = rstd_ln * (
        grad_hat
        - jnp.mean(grad_hat, axis=1, keepdims=True)
        - ln_hat * jnp.mean(grad_hat * ln_hat, axis=1, keepdims=True)
    )
    grad_frames = (out_grad.astype(jnp.float32) + grad_input).astype(jnp.bfloat16)
    return (
        outputs,
        grad_frames,
        grad_w_in,
        grad_w_out,
        grad_kernel,
        grad_ln_gain,
        gain_total * grad_scale,
        bias_total * grad_scale,
    )


def solution(mesh):
    devices = mesh.shape["seq"]
    body = channel_local if devices <= 16 else local
    return jax.shard_map(
        body,
        mesh=mesh,
        in_specs=(
            P(("mix", "seq"), None),
            P(("mix", "seq")),
            P(("mix", "seq"), None),
            P(("mix", "seq")),
            P(("mix", "seq"), None),
            P("mix", "seq"),
            P(("mix", "seq")),
            P(("mix", "seq")),
            P(("mix", "seq"), None),
        ),
        out_specs=(
            P(("mix", "seq"), None),
            P(("mix", "seq"), None),
            P(("mix", "seq"), None),
            P(("mix", "seq"), None),
            P("mix", "seq"),
            P(("mix", "seq")),
            P(("mix", "seq")),
            P(("mix", "seq")),
        ),
        check_vma=False,
    )
```

```python
import math

import jax
import jax.numpy as jnp
from jax import lax
from jax.sharding import PartitionSpec as P

EPSILON = 1e-05


def with_halo(cells, sides, width):
    for axis, dim in sides:
        count = lax.axis_size(axis)
        ends = count - 1
        head = lax.slice_in_dim(cells, 0, width, axis=dim)
        tail = lax.slice_in_dim(cells, cells.shape[dim] - width, cells.shape[dim], axis=dim)
        cells = jnp.concatenate(
            [
                lax.ppermute(tail, axis, [(i, (i + 1) % count) for i in range(ends)]),
                cells,
                lax.ppermute(head, axis, [((i + 1) % count, i) for i in range(ends)]),
            ],
            axis=dim,
        )
    return cells


def local(frames, segment_ids, out_grad, ln_gain, w_in, dw_kernel, bn_gain, bn_bias, w_out):
    frame_count = frames.shape[0]
    width = frames.shape[1]
    taps = dw_kernel.shape[0]
    margin = taps // 2
    devices = lax.axis_size("seq")
    stream = frame_count * devices
    grad_scale = 1.0 / math.sqrt(stream)
    share = width // devices
    gains, kernel, bn_scale, bn_shift = (
        lax.all_gather(ln_gain, "seq", axis=0, tiled=True),
        lax.all_gather(dw_kernel, "seq", axis=1, tiled=True),
        lax.all_gather(bn_gain, "seq", axis=0, tiled=True),
        lax.all_gather(bn_bias, "seq", axis=0, tiled=True),
    )
    own_ids = segment_ids + 1
    padded_ids = with_halo(own_ids, (("seq", 0),), margin)
    masks = [
        (padded_ids[tap_index : tap_index + frame_count] == own_ids).astype(jnp.float32)[:, None]
        for tap_index in range(taps)
    ]
    frames_float = frames.astype(jnp.float32)
    mean_ln = jnp.mean(frames_float, axis=1, keepdims=True)
    centred = frames_float - mean_ln
    rstd_ln = lax.rsqrt(jnp.mean(centred * centred, axis=1, keepdims=True) + EPSILON)
    ln_hat = centred * rstd_ln
    ln_x = (ln_hat * gains).astype(jnp.bfloat16)
    columns = ln_x
    hidden = jnp.dot(
        columns, lax.all_gather(w_in, "seq", axis=0, tiled=True), preferred_element_type=jnp.float32
    )
    left_half = hidden[:, :width]
    right_gate = jax.nn.sigmoid(hidden[:, width:])
    glu = (left_half * right_gate).astype(jnp.bfloat16)
    padded_glu = with_halo(glu, (("seq", 0),), margin)
    conv_out = jnp.zeros((frame_count, width), jnp.float32)
    for tap_index in range(taps):
        conv_out = (
            conv_out
            + kernel[tap_index]
            * padded_glu[tap_index : tap_index + frame_count].astype(jnp.float32)
            * masks[tap_index]
        )
    plain_sums, square_sums = lax.psum(
        (jnp.sum(conv_out, axis=0), jnp.sum(conv_out * conv_out, axis=0)), "seq"
    )
    bn_mean = plain_sums / stream
    bn_var = square_sums / stream - bn_mean * bn_mean
    bn_rstd = lax.rsqrt(bn_var + EPSILON)
    bn_hat = (conv_out - bn_mean) * bn_rstd
    zed = bn_hat * bn_scale + bn_shift
    zed_gate = jax.nn.sigmoid(zed)
    activation = (zed * zed_gate).astype(jnp.bfloat16)
    columns = activation
    projected = jnp.dot(
        columns,
        lax.all_gather(w_out, "seq", axis=0, tiled=True),
        preferred_element_type=jnp.float32,
    )
    outputs = (frames_float + projected).astype(jnp.bfloat16)
    grad_w_out = lax.psum_scatter(
        jnp.einsum("fa,fb->ab", activation, out_grad, preferred_element_type=jnp.float32)
        * grad_scale,
        "seq",
        scatter_dimension=0,
        tiled=True,
    )
    grad_act = jnp.einsum(
        "fe,ne->fn",
        out_grad,
        lax.all_gather(w_out, "seq", axis=0, tiled=True),
        preferred_element_type=jnp.float32,
    )
    grad_zed = grad_act * zed_gate * (1.0 + zed * (1.0 - zed_gate))
    bias_total, gain_total = lax.psum(
        (jnp.sum(grad_zed, axis=0), jnp.sum(grad_zed * bn_hat, axis=0)), "seq"
    )
    grad_conv = bn_scale * bn_rstd * (grad_zed - bias_total / stream - bn_hat * gain_total / stream)
    first_channel = lax.axis_index("seq") * share
    grad_bn_bias = lax.dynamic_slice_in_dim(bias_total, first_channel, share, 0) * grad_scale
    grad_bn_gain = lax.dynamic_slice_in_dim(gain_total, first_channel, share, 0) * grad_scale
    kernel_rows = [
        jnp.sum(
            grad_conv
            * padded_glu[tap_index : tap_index + frame_count].astype(jnp.float32)
            * masks[tap_index],
            axis=0,
        )
        for tap_index in range(taps)
    ]
    kernel_term = jnp.stack(kernel_rows) * grad_scale
    padded_conv = with_halo(grad_conv, (("seq", 0),), margin)
    grad_glu = jnp.zeros((frame_count, width), jnp.float32)
    for tap_index in range(taps):
        mirror = 2 * margin - tap_index
        grad_glu = (
            grad_glu
            + kernel[tap_index] * padded_conv[mirror : mirror + frame_count] * masks[mirror]
        )
    grad_hidden = jnp.concatenate(
        [grad_glu * right_gate, grad_glu * left_half * right_gate * (1.0 - right_gate)], axis=1
    ).astype(jnp.bfloat16)
    grad_ln = jnp.einsum(
        "fe,ne->fn",
        grad_hidden,
        lax.all_gather(w_in, "seq", axis=0, tiled=True),
        preferred_element_type=jnp.float32,
    )
    in_term = (
        jnp.einsum("fa,fb->ab", ln_x, grad_hidden, preferred_element_type=jnp.float32) * grad_scale
    )
    gain_term = jnp.sum(grad_ln * ln_hat, axis=0) * grad_scale
    grad_w_in, grad_kernel, grad_ln_gain = (
        lax.psum_scatter(in_term, "seq", scatter_dimension=0, tiled=True),
        lax.psum_scatter(kernel_term, "seq", scatter_dimension=1, tiled=True),
        lax.psum_scatter(gain_term, "seq", scatter_dimension=0, tiled=True),
    )
    grad_hat = grad_ln * gains
    grad_input = rstd_ln * (
        grad_hat
        - jnp.mean(grad_hat, axis=1, keepdims=True)
        - ln_hat * jnp.mean(grad_hat * ln_hat, axis=1, keepdims=True)
    )
    grad_frames = (out_grad.astype(jnp.float32) + grad_input).astype(jnp.bfloat16)
    return (
        outputs,
        grad_frames,
        grad_w_in,
        grad_w_out,
        grad_kernel,
        grad_ln_gain,
        grad_bn_gain,
        grad_bn_bias,
    )


def channel_local(frames, segment_ids, out_grad, ln_gain, w_in, dw_kernel, bn_gain, bn_bias, w_out):
    rows = frames.shape[0]
    width = frames.shape[1]
    taps = dw_kernel.shape[0]
    margin = taps // 2
    devices = lax.axis_size("seq")
    stream = rows * devices
    grad_scale = 1.0 / math.sqrt(stream)
    share = width // devices

    def spread(block):
        copies = jnp.broadcast_to(block[None], (devices,) + block.shape)
        return lax.all_to_all(copies, "seq", 0, 0, tiled=True)

    small = spread(jnp.concatenate([ln_gain, segment_ids.astype(jnp.float32)]))
    gains = small[:, :share].reshape(width)
    all_ids = small[:, share:].reshape(stream).astype(jnp.int32)

    out_rows = w_out.shape[0]
    pieces = lax.all_gather(jnp.stack([frames, out_grad]), "seq", axis=1, tiled=True)
    frames_all = pieces[0]
    grad_all = pieces[1]
    w_in_cols = lax.all_to_all(
        w_in.reshape(share, 2, devices, share).transpose(2, 0, 1, 3), "seq", 0, 0, tiled=True
    ).reshape(width, 2 * share)
    w_in_late, w_out_late, _, _, _ = lax.optimization_barrier(
        (w_in, w_out, pieces, w_in_cols, small)
    )
    weights = lax.all_gather(
        jnp.concatenate([w_out_late, w_in_late[:, :width], w_in_late[:, width:]], axis=0),
        "seq",
        axis=0,
    )
    w_out_all = weights[:, :out_rows].reshape(width, width)
    w_in_left = weights[:, out_rows : 2 * out_rows].reshape(width, width)
    w_in_right = weights[:, 2 * out_rows :].reshape(width, width)

    first_channel = lax.axis_index("seq") * share

    def norm(block):
        block_float = block.astype(jnp.float32)
        mean = jnp.mean(block_float, axis=1, keepdims=True)
        centred = block_float - mean
        rstd = lax.rsqrt(jnp.mean(centred * centred, axis=1, keepdims=True) + EPSILON)
        return centred * rstd, rstd

    ln_all, _ = norm(frames_all)
    ln_x_all = (ln_all * gains).astype(jnp.bfloat16)
    ln_head32 = lax.reduce_precision(ln_all, exponent_bits=8, mantissa_bits=7)
    ln_x_all, ln_head, ln_tail = lax.optimization_barrier(
        (ln_x_all, ln_head32.astype(jnp.bfloat16), (ln_all - ln_head32).astype(jnp.bfloat16))
    )

    hidden = jnp.dot(ln_x_all, w_in_cols, preferred_element_type=jnp.float32)
    left_half = hidden[:, :share]
    right_gate = jax.nn.sigmoid(hidden[:, share:])
    glu = (left_half * right_gate).astype(jnp.bfloat16)

    own_ids = all_ids + 1
    padded_ids = jnp.pad(own_ids, margin)
    masks = [
        (padded_ids[tap_index : tap_index + stream] == own_ids).astype(jnp.float32)[:, None]
        for tap_index in range(taps)
    ]
    padded_glu = jnp.pad(glu, ((margin, margin), (0, 0)))
    conv_out = jnp.zeros((stream, share), jnp.float32)
    for tap_index in range(taps):
        conv_out = (
            conv_out
            + dw_kernel[tap_index]
            * padded_glu[tap_index : tap_index + stream].astype(jnp.float32)
            * masks[tap_index]
        )
    bn_mean = jnp.sum(conv_out, axis=0) / stream
    bn_var = jnp.sum((conv_out - bn_mean) ** 2, axis=0) / stream
    bn_rstd = lax.rsqrt(bn_var + EPSILON)
    bn_hat = (conv_out - bn_mean) * bn_rstd
    zed = bn_hat * bn_gain + bn_bias
    zed_gate = jax.nn.sigmoid(zed)
    activation = (zed * zed_gate).astype(jnp.bfloat16)


    grad_w_out = (
        jnp.einsum("fa,fb->ab", activation, grad_all, preferred_element_type=jnp.float32)
        * grad_scale
    )
    grad_act = jnp.einsum("fe,ne->fn", grad_all, w_out, preferred_element_type=jnp.float32)
    grad_zed = grad_act * zed_gate * (1.0 + zed * (1.0 - zed_gate))
    bias_total = jnp.sum(grad_zed, axis=0)
    gain_total = jnp.sum(grad_zed * bn_hat, axis=0)
    grad_conv = bn_gain * bn_rstd * (grad_zed - bias_total / stream - bn_hat * gain_total / stream)
    grad_kernel = (
        jnp.stack(
            [
                jnp.sum(
                    grad_conv
                    * padded_glu[tap_index : tap_index + stream].astype(jnp.float32)
                    * masks[tap_index],
                    axis=0,
                )
                for tap_index in range(taps)
            ]
        )
        * grad_scale
    )
    padded_conv = jnp.pad(grad_conv, ((margin, margin), (0, 0)))
    grad_glu = jnp.zeros((stream, share), jnp.float32)
    for tap_index in range(taps):
        mirror = 2 * margin - tap_index
        grad_glu = (
            grad_glu
            + dw_kernel[tap_index] * padded_conv[mirror : mirror + stream] * masks[mirror]
        )
    grad_hidden = jnp.concatenate(
        [grad_glu * right_gate, grad_glu * left_half * right_gate * (1.0 - right_gate)], axis=1
    ).astype(jnp.bfloat16)

    in_cols = (
        jnp.einsum("fa,fb->ab", ln_x_all, grad_hidden, preferred_element_type=jnp.float32)
        * grad_scale
    )
    moments = jnp.einsum(
        "fa,fb->ab", ln_head, grad_hidden, preferred_element_type=jnp.float32
    ) + jnp.einsum("fa,fb->ab", ln_tail, grad_hidden, preferred_element_type=jnp.float32)
    gain_part = jnp.sum(w_in_cols.astype(jnp.float32) * moments, axis=1) * grad_scale
    packed = lax.all_to_all(
        jnp.concatenate(
            [in_cols.reshape(devices, share * 2 * share), gain_part.reshape(devices, share)],
            axis=1,
        ),
        "seq", 0, 0, tiled=True,
    )
    grad_w_in = (
        packed[:, : share * 2 * share]
        .reshape(devices, share, 2, share)
        .transpose(1, 2, 0, 3)
        .reshape(share, 2 * width)
    )
    grad_ln_gain = jnp.sum(packed[:, share * 2 * share :], axis=0)
    back = lax.all_to_all(
        jnp.concatenate([activation, grad_hidden], axis=1).T.reshape(3 * share, devices, rows),
        "seq", 1, 1, tiled=True,
    ).transpose(1, 2, 0)
    act_rows = back[:, :, :share].transpose(1, 0, 2).reshape(rows, width)
    hidden_rows = (
        back[:, :, share:].reshape(devices, rows, 2, share).transpose(1, 2, 0, 3)
        .reshape(rows, 2, width)
    )
    projected = jnp.dot(act_rows, w_out_all, preferred_element_type=jnp.float32)
    outputs = (frames.astype(jnp.float32) + projected).astype(jnp.bfloat16)
    grad_ln = jnp.einsum(
        "fe,ne->fn", hidden_rows[:, 0], w_in_left, preferred_element_type=jnp.float32
    ) + jnp.einsum("fe,ne->fn", hidden_rows[:, 1], w_in_right, preferred_element_type=jnp.float32)
    ln_hat, rstd_ln = norm(frames)
    grad_hat = grad_ln * gains
    grad_input = rstd_ln * (
        grad_hat
        - jnp.mean(grad_hat, axis=1, keepdims=True)
        - ln_hat * jnp.mean(grad_hat * ln_hat, axis=1, keepdims=True)
    )
    grad_frames = (out_grad.astype(jnp.float32) + grad_input).astype(jnp.bfloat16)
    return (
        outputs,
        grad_frames,
        grad_w_in,
        grad_w_out,
        grad_kernel,
        grad_ln_gain,
        gain_total * grad_scale,
        bias_total * grad_scale,
    )


def solution(mesh):
    devices = mesh.shape["seq"]
    body = channel_local if devices <= 16 else local
    return jax.shard_map(
        body,
        mesh=mesh,
        in_specs=(
            P(("mix", "seq"), None),
            P(("mix", "seq")),
            P(("mix", "seq"), None),
            P(("mix", "seq")),
            P(("mix", "seq"), None),
            P("mix", "seq"),
            P(("mix", "seq")),
            P(("mix", "seq")),
            P(("mix", "seq"), None),
        ),
        out_specs=(
            P(("mix", "seq"), None),
            P(("mix", "seq"), None),
            P(("mix", "seq"), None),
            P(("mix", "seq"), None),
            P("mix", "seq"),
            P(("mix", "seq")),
            P(("mix", "seq")),
            P(("mix", "seq")),
        ),
        check_vma=False,
    )
```

```python
import math

import jax
import jax.numpy as jnp
from jax import lax
from jax.sharding import PartitionSpec as P

EPSILON = 1e-05


def with_halo(cells, sides, width):
    for axis, dim in sides:
        count = lax.axis_size(axis)
        ends = count - 1
        head = lax.slice_in_dim(cells, 0, width, axis=dim)
        tail = lax.slice_in_dim(cells, cells.shape[dim] - width, cells.shape[dim], axis=dim)
        cells = jnp.concatenate(
            [
                lax.ppermute(tail, axis, [(i, (i + 1) % count) for i in range(ends)]),
                cells,
                lax.ppermute(head, axis, [((i + 1) % count, i) for i in range(ends)]),
            ],
            axis=dim,
        )
    return cells


def local(frames, segment_ids, out_grad, ln_gain, w_in, dw_kernel, bn_gain, bn_bias, w_out):
    frame_count = frames.shape[0]
    width = frames.shape[1]
    taps = dw_kernel.shape[0]
    margin = taps // 2
    devices = lax.axis_size("seq")
    stream = frame_count * devices
    grad_scale = 1.0 / math.sqrt(stream)
    share = width // devices
    gains, kernel, bn_scale, bn_shift = (
        lax.all_gather(ln_gain, "seq", axis=0, tiled=True),
        lax.all_gather(dw_kernel, "seq", axis=1, tiled=True),
        lax.all_gather(bn_gain, "seq", axis=0, tiled=True),
        lax.all_gather(bn_bias, "seq", axis=0, tiled=True),
    )
    own_ids = segment_ids + 1
    padded_ids = with_halo(own_ids, (("seq", 0),), margin)
    masks = [
        (padded_ids[tap_index : tap_index + frame_count] == own_ids).astype(jnp.float32)[:, None]
        for tap_index in range(taps)
    ]
    frames_float = frames.astype(jnp.float32)
    mean_ln = jnp.mean(frames_float, axis=1, keepdims=True)
    centred = frames_float - mean_ln
    rstd_ln = lax.rsqrt(jnp.mean(centred * centred, axis=1, keepdims=True) + EPSILON)
    ln_hat = centred * rstd_ln
    ln_x = (ln_hat * gains).astype(jnp.bfloat16)
    columns = ln_x
    hidden = jnp.dot(
        columns, lax.all_gather(w_in, "seq", axis=0, tiled=True), preferred_element_type=jnp.float32
    )
    left_half = hidden[:, :width]
    right_gate = jax.nn.sigmoid(hidden[:, width:])
    glu = (left_half * right_gate).astype(jnp.bfloat16)
    padded_glu = with_halo(glu, (("seq", 0),), margin)
    conv_out = jnp.zeros((frame_count, width), jnp.float32)
    for tap_index in range(taps):
        conv_out = (
            conv_out
            + kernel[tap_index]
            * padded_glu[tap_index : tap_index + frame_count].astype(jnp.float32)
            * masks[tap_index]
        )
    plain_sums, square_sums = lax.psum(
        (jnp.sum(conv_out, axis=0), jnp.sum(conv_out * conv_out, axis=0)), "seq"
    )
    bn_mean = plain_sums / stream
    bn_var = square_sums / stream - bn_mean * bn_mean
    bn_rstd = lax.rsqrt(bn_var + EPSILON)
    bn_hat = (conv_out - bn_mean) * bn_rstd
    zed = bn_hat * bn_scale + bn_shift
    zed_gate = jax.nn.sigmoid(zed)
    activation = (zed * zed_gate).astype(jnp.bfloat16)
    columns = activation
    projected = jnp.dot(
        columns,
        lax.all_gather(w_out, "seq", axis=0, tiled=True),
        preferred_element_type=jnp.float32,
    )
    outputs = (frames_float + projected).astype(jnp.bfloat16)
    grad_w_out = lax.psum_scatter(
        jnp.einsum("fa,fb->ab", activation, out_grad, preferred_element_type=jnp.float32)
        * grad_scale,
        "seq",
        scatter_dimension=0,
        tiled=True,
    )
    grad_act = jnp.einsum(
        "fe,ne->fn",
        out_grad,
        lax.all_gather(w_out, "seq", axis=0, tiled=True),
        preferred_element_type=jnp.float32,
    )
    grad_zed = grad_act * zed_gate * (1.0 + zed * (1.0 - zed_gate))
    bias_total, gain_total = lax.psum(
        (jnp.sum(grad_zed, axis=0), jnp.sum(grad_zed * bn_hat, axis=0)), "seq"
    )
    grad_conv = bn_scale * bn_rstd * (grad_zed - bias_total / stream - bn_hat * gain_total / stream)
    first_channel = lax.axis_index("seq") * share
    grad_bn_bias = lax.dynamic_slice_in_dim(bias_total, first_channel, share, 0) * grad_scale
    grad_bn_gain = lax.dynamic_slice_in_dim(gain_total, first_channel, share, 0) * grad_scale
    kernel_rows = [
        jnp.sum(
            grad_conv
            * padded_glu[tap_index : tap_index + frame_count].astype(jnp.float32)
            * masks[tap_index],
            axis=0,
        )
        for tap_index in range(taps)
    ]
    kernel_term = jnp.stack(kernel_rows) * grad_scale
    padded_conv = with_halo(grad_conv, (("seq", 0),), margin)
    grad_glu = jnp.zeros((frame_count, width), jnp.float32)
    for tap_index in range(taps):
        mirror = 2 * margin - tap_index
        grad_glu = (
            grad_glu
            + kernel[tap_index] * padded_conv[mirror : mirror + frame_count] * masks[mirror]
        )
    grad_hidden = jnp.concatenate(
        [grad_glu * right_gate, grad_glu * left_half * right_gate * (1.0 - right_gate)], axis=1
    ).astype(jnp.bfloat16)
    grad_ln = jnp.einsum(
        "fe,ne->fn",
        grad_hidden,
        lax.all_gather(w_in, "seq", axis=0, tiled=True),
        preferred_element_type=jnp.float32,
    )
    in_term = (
        jnp.einsum("fa,fb->ab", ln_x, grad_hidden, preferred_element_type=jnp.float32) * grad_scale
    )
    gain_term = jnp.sum(grad_ln * ln_hat, axis=0) * grad_scale
    grad_w_in, grad_kernel, grad_ln_gain = (
        lax.psum_scatter(in_term, "seq", scatter_dimension=0, tiled=True),
        lax.psum_scatter(kernel_term, "seq", scatter_dimension=1, tiled=True),
        lax.psum_scatter(gain_term, "seq", scatter_dimension=0, tiled=True),
    )
    grad_hat = grad_ln * gains
    grad_input = rstd_ln * (
        grad_hat
        - jnp.mean(grad_hat, axis=1, keepdims=True)
        - ln_hat * jnp.mean(grad_hat * ln_hat, axis=1, keepdims=True)
    )
    grad_frames = (out_grad.astype(jnp.float32) + grad_input).astype(jnp.bfloat16)
    return (
        outputs,
        grad_frames,
        grad_w_in,
        grad_w_out,
        grad_kernel,
        grad_ln_gain,
        grad_bn_gain,
        grad_bn_bias,
    )


def channel_local(frames, segment_ids, out_grad, ln_gain, w_in, dw_kernel, bn_gain, bn_bias, w_out):
    rows = frames.shape[0]
    width = frames.shape[1]
    taps = dw_kernel.shape[0]
    margin = taps // 2
    devices = lax.axis_size("seq")
    stream = rows * devices
    grad_scale = 1.0 / math.sqrt(stream)
    share = width // devices

    def spread(block):
        copies = jnp.broadcast_to(block[None], (devices,) + block.shape)
        return lax.all_to_all(copies, "seq", 0, 0, tiled=True)

    small = spread(jnp.concatenate([ln_gain, segment_ids.astype(jnp.float32)]))
    gains = small[:, :share].reshape(width)
    all_ids = small[:, share:].reshape(stream).astype(jnp.int32)

    out_rows = w_out.shape[0]
    pieces = lax.all_gather(jnp.stack([frames, out_grad]), "seq", axis=1, tiled=True)
    frames_all = pieces[0]
    grad_all = pieces[1]
    w_in_cols = lax.all_to_all(
        w_in.reshape(share, 2, devices, share).transpose(2, 0, 1, 3), "seq", 0, 0, tiled=True
    ).reshape(width, 2 * share)
    w_in_late, w_out_late, _, _, _ = lax.optimization_barrier(
        (w_in, w_out, pieces, w_in_cols, small)
    )
    weights = lax.all_gather(
        jnp.stack([w_out_late, w_in_late[:, :width], w_in_late[:, width:]]),
        "seq",
        axis=1,
        tiled=True,
    )
    w_out_all = weights[0]
    w_in_left = weights[1]
    w_in_right = weights[2]

    first_channel = lax.axis_index("seq") * share

    def norm(block):
        block_float = block.astype(jnp.float32)
        mean = jnp.mean(block_float, axis=1, keepdims=True)
        centred = block_float - mean
        rstd = lax.rsqrt(jnp.mean(centred * centred, axis=1, keepdims=True) + EPSILON)
        return centred * rstd, rstd

    ln_all, _ = norm(frames_all)
    ln_x_all = (ln_all * gains).astype(jnp.bfloat16)
    ln_head32 = lax.reduce_precision(ln_all, exponent_bits=8, mantissa_bits=7)
    ln_x_all, ln_head, ln_tail = lax.optimization_barrier(
        (ln_x_all, ln_head32.astype(jnp.bfloat16), (ln_all - ln_head32).astype(jnp.bfloat16))
    )

    hidden = jnp.dot(ln_x_all, w_in_cols, preferred_element_type=jnp.float32)
    left_half = hidden[:, :share]
    right_gate = jax.nn.sigmoid(hidden[:, share:])
    glu = (left_half * right_gate).astype(jnp.bfloat16)

    own_ids = all_ids + 1
    padded_ids = jnp.pad(own_ids, margin)
    masks = [
        (padded_ids[tap_index : tap_index + stream] == own_ids).astype(jnp.float32)[:, None]
        for tap_index in range(taps)
    ]
    padded_glu = jnp.pad(glu, ((margin, margin), (0, 0)))
    conv_out = jnp.zeros((stream, share), jnp.float32)
    for tap_index in range(taps):
        conv_out = (
            conv_out
            + dw_kernel[tap_index]
            * padded_glu[tap_index : tap_index + stream].astype(jnp.float32)
            * masks[tap_index]
        )
    bn_mean = jnp.sum(conv_out, axis=0) / stream
    bn_var = jnp.sum((conv_out - bn_mean) ** 2, axis=0) / stream
    bn_rstd = lax.rsqrt(bn_var + EPSILON)
    bn_hat = (conv_out - bn_mean) * bn_rstd
    zed = bn_hat * bn_gain + bn_bias
    zed_gate = jax.nn.sigmoid(zed)
    activation = (zed * zed_gate).astype(jnp.bfloat16)


    grad_w_out = (
        jnp.einsum("fa,fb->ab", activation, grad_all, preferred_element_type=jnp.float32)
        * grad_scale
    )
    grad_act = jnp.einsum("fe,ne->fn", grad_all, w_out, preferred_element_type=jnp.float32)
    grad_zed = grad_act * zed_gate * (1.0 + zed * (1.0 - zed_gate))
    bias_total = jnp.sum(grad_zed, axis=0)
    gain_total = jnp.sum(grad_zed * bn_hat, axis=0)
    grad_conv = bn_gain * bn_rstd * (grad_zed - bias_total / stream - bn_hat * gain_total / stream)
    grad_kernel = (
        jnp.stack(
            [
                jnp.sum(
                    grad_conv
                    * padded_glu[tap_index : tap_index + stream].astype(jnp.float32)
                    * masks[tap_index],
                    axis=0,
                )
                for tap_index in range(taps)
            ]
        )
        * grad_scale
    )
    padded_conv = jnp.pad(grad_conv, ((margin, margin), (0, 0)))
    grad_glu = jnp.zeros((stream, share), jnp.float32)
    for tap_index in range(taps):
        mirror = 2 * margin - tap_index
        grad_glu = (
            grad_glu
            + dw_kernel[tap_index] * padded_conv[mirror : mirror + stream] * masks[mirror]
        )
    grad_hidden = jnp.concatenate(
        [grad_glu * right_gate, grad_glu * left_half * right_gate * (1.0 - right_gate)], axis=1
    ).astype(jnp.bfloat16)

    in_cols = (
        jnp.einsum("fa,fb->ab", ln_x_all, grad_hidden, preferred_element_type=jnp.float32)
        * grad_scale
    )
    moments = jnp.einsum(
        "fa,fb->ab", ln_head, grad_hidden, preferred_element_type=jnp.float32
    ) + jnp.einsum("fa,fb->ab", ln_tail, grad_hidden, preferred_element_type=jnp.float32)
    gain_part = jnp.sum(w_in_cols.astype(jnp.float32) * moments, axis=1) * grad_scale
    packed = lax.all_to_all(
        jnp.concatenate(
            [in_cols.reshape(devices, share * 2 * share), gain_part.reshape(devices, share)],
            axis=1,
        ),
        "seq", 0, 0, tiled=True,
    )
    grad_w_in = (
        packed[:, : share * 2 * share]
        .reshape(devices, share, 2, share)
        .transpose(1, 2, 0, 3)
        .reshape(share, 2 * width)
    )
    grad_ln_gain = jnp.sum(packed[:, share * 2 * share :], axis=0)
    back = lax.all_to_all(
        jnp.concatenate([activation, grad_hidden], axis=1).T.reshape(3 * share, devices, rows),
        "seq", 1, 1, tiled=True,
    ).transpose(1, 2, 0)
    act_rows = back[:, :, :share].transpose(1, 0, 2).reshape(rows, width)
    hidden_rows = (
        back[:, :, share:].reshape(devices, rows, 2, share).transpose(1, 2, 0, 3)
        .reshape(rows, 2, width)
    )
    projected = jnp.dot(act_rows, w_out_all, preferred_element_type=jnp.float32)
    outputs = (frames.astype(jnp.float32) + projected).astype(jnp.bfloat16)
    grad_ln = jnp.einsum(
        "fe,ne->fn", hidden_rows[:, 0], w_in_left, preferred_element_type=jnp.float32
    ) + jnp.einsum("fe,ne->fn", hidden_rows[:, 1], w_in_right, preferred_element_type=jnp.float32)
    ln_hat, rstd_ln = norm(frames)
    grad_hat = grad_ln * gains
    grad_input = rstd_ln * (
        grad_hat
        - jnp.mean(grad_hat, axis=1, keepdims=True)
        - ln_hat * jnp.mean(grad_hat * ln_hat, axis=1, keepdims=True)
    )
    grad_frames = (out_grad.astype(jnp.float32) + grad_input).astype(jnp.bfloat16)
    return (
        outputs,
        grad_frames,
        grad_w_in,
        grad_w_out,
        grad_kernel,
        grad_ln_gain,
        gain_total * grad_scale,
        bias_total * grad_scale,
    )


def solution(mesh):
    devices = mesh.shape["seq"]
    body = channel_local if devices <= 16 else local
    return jax.shard_map(
        body,
        mesh=mesh,
        in_specs=(
            P(("mix", "seq"), None),
            P(("mix", "seq")),
            P(("mix", "seq"), None),
            P(("mix", "seq")),
            P(("mix", "seq"), None),
            P("mix", "seq"),
            P(("mix", "seq")),
            P(("mix", "seq")),
            P(("mix", "seq"), None),
        ),
        out_specs=(
            P(("mix", "seq"), None),
            P(("mix", "seq"), None),
            P(("mix", "seq"), None),
            P(("mix", "seq"), None),
            P("mix", "seq"),
            P(("mix", "seq")),
            P(("mix", "seq")),
            P(("mix", "seq")),
        ),
        check_vma=False,
    )
```
